32 devices in a mesh: track: 4 (over z), cross: 8 (over y, x, core).
Axes of the slice: x: 2, y: 2, z: 4, core: 2. Of those that a mesh axis runs over, the one named last changes fastest.
Arguments:
- cube: bfloat16 [1024, 256, 224], P('track', 'cross'), may hold values from -60 to 113, as said below
Outputs:
- scores: float32 [1024, 256], P('track', 'cross')
The draws below stay inside these ranges and needn't reach their ends.
Inputs may be any that keep to these rules, and one draw needn't show every extreme that they name: `cube`: A positive radiance level per band plus noise, scaled per band and by position.
All inputs are finite; a program needn't handle non-finite values.
Results may differ from the reference program's by a relative error of at most 0.0003.
Values may be sent and summed in bfloat16 or wider, within the bound.
No kernel may reach another device: no remote copies, remote signals or barrier semaphores. Data moves between devices by JAX's collectives and lax.ppermute only.
A program may use at most 64 MiB of HBM per device.

```python
import math
import jax
import jax.numpy as jnp
from jax import lax

B = 224
HALF = 15
LINES = 1024
PIX = 256


def draw_cube(key, part):
    key_band, key_level, key_noise = jax.random.split(key, 3)
    band_scale = jnp.exp(jax.random.uniform(key_band, (B,), jnp.float32, 0.0, math.log(10.0)))
    level = jax.random.uniform(key_level, (B,), jnp.float32, 2.0, 4.0)
    line_pos = jnp.arange(LINES, dtype=jnp.float32) / max(LINES - 1, 1)
    pixel_pos = jnp.arange(PIX, dtype=jnp.float32) / max(PIX - 1, 1)
    illumination = (1.0 + 2.0 * line_pos)[:, None, None] * (1.0 + 2.0 * pixel_pos)[None, :, None]
    noise = jnp.clip(jax.random.normal(key_noise, (LINES, PIX, B), jnp.float32), -6.0, 6.0)
    values = 0.1 * illumination * band_scale * (level + noise)
    return values.astype(jnp.bfloat16)


def setup_inputs(seed: int = 0) -> dict:
    streams_of = jax.random.split(jax.random.key(seed), 2)
    cube = draw_cube(jax.random.fold_in(streams_of[1], 71), 0)
    return dict(cube=cube)


LOAD = 0.02

def window_count(length):
    index = jnp.arange(length)
    upper = jnp.minimum(index + HALF, length - 1)
    lower = jnp.maximum(index - HALF, 0)
    return (upper - lower + 1).astype(jnp.float32)

def window_sum(values, axis, length):
    widths = [(0, 0), (0, 0)]
    widths[axis] = (HALF + 1, HALF)
    padded = jnp.pad(values, widths)
    running = jnp.cumsum(padded, axis=axis)
    upper = lax.slice_in_dim(running, 2 * HALF + 1, 2 * HALF + 1 + length, axis=axis)
    lower = lax.slice_in_dim(running, 0, length, axis=axis)
    return upper - lower

def reference(cube):
    count = window_count(LINES)[:, None] * window_count(PIX)[None, :]

    def one_band(band_index):
        plane = lax.dynamic_index_in_dim(cube, band_index, 2, keepdims=False).astype(jnp.float32)
        summed = window_sum(window_sum(plane, 1, PIX), 0, LINES)
        return plane - summed / count
    residual = lax.map(one_band, jnp.arange(B, dtype=jnp.int32))
    residual = residual.reshape(B, LINES * PIX)
    residual_bf = residual.astype(jnp.bfloat16)
    covariance = jnp.dot(residual_bf.astype(jnp.float32), residual_bf.T.astype(jnp.float32), preferred_element_type=jnp.float32) / (LINES * PIX)
    loaded = covariance + LOAD * (jnp.trace(covariance) / B) * jnp.eye(B, dtype=jnp.float32)
    factor = jnp.linalg.cholesky(loaded)
    inverse = jax.scipy.linalg.solve_triangular(factor, jnp.eye(B, dtype=jnp.float32), lower=True)
    whitened = jnp.dot(inverse.astype(jnp.float32), residual.astype(jnp.float32), precision=lax.Precision.HIGHEST, preferred_element_type=jnp.float32)
    scores = jnp.sum(whitened * whitened, axis=0) / B
    return scores.reshape(LINES, PIX)
```

```python
import jax
import jax.numpy as jnp
from jax import lax
from jax.sharding import PartitionSpec as P

HALF = 15


LOAD = 0.02


def with_halo(block, sides, width):
    for axis, dim in sides:
        count = lax.axis_size(axis)
        forward = [(i, i + 1) for i in range(count - 1)]
        backward = [(target, source) for source, target in forward]
        low = lax.ppermute(
            lax.slice_in_dim(block, block.shape[dim] - width, None, axis=dim), axis, forward
        )
        high = lax.ppermute(lax.slice_in_dim(block, 0, width, axis=dim), axis, backward)
        block = jnp.concatenate([low, block, high], axis=dim)
    return block


def band_matrix(rows_in, rows_out, dtype):
    source = jnp.arange(rows_in)[:, None]
    target = jnp.arange(rows_out)[None, :]
    inside = (source >= target) & (source <= target + 2 * HALF)
    return inside.astype(dtype)


def butterfly_sum(x, axis):
    count = lax.axis_size(axis)
    step = 1
    while step < count:
        pairs = [(i, i ^ step) for i in range(count)]
        x = x + lax.ppermute(x, axis, pairs)
        step *= 2
    return x


def pack_symmetric(c):
    h = c.shape[0] // 2
    row = jnp.arange(h)[:, None]
    col = jnp.arange(h)[None, :]
    c11, c12, c22 = c[:h, :h], c[:h, h:], c[h:, h:]
    mixed = jnp.where(col >= row, c11, c22)
    return jnp.concatenate([c12, mixed, jnp.diagonal(c22)[None, :]], axis=0)


def unpack_symmetric(p):
    h = p.shape[1]
    row = jnp.arange(h)[:, None]
    col = jnp.arange(h)[None, :]
    c12, mixed, d22 = p[:h], p[h:2 * h], p[2 * h]
    c11 = jnp.where(col >= row, mixed, mixed.T)
    c22 = jnp.where(col < row, mixed, mixed.T)
    c22 = jnp.where(col == row, d22[None, :], c22)
    top = jnp.concatenate([c11, c12], axis=1)
    bottom = jnp.concatenate([c12.T, c22], axis=1)
    return jnp.concatenate([top, bottom], axis=0)


def window_count(first, local, total):
    index = first + jnp.arange(local)
    upper = jnp.minimum(index + HALF, total - 1)
    lower = jnp.maximum(index - HALF, 0)
    return (upper - lower + 1).astype(jnp.float32)


def sum_pixels(values, width, dtype):
    weights = band_matrix(width + 2 * HALF, width, dtype)
    return jnp.einsum(
        "lqb,qp->lpb", values, weights, precision=None, preferred_element_type=jnp.float32
    )


def sum_lines(values, height, dtype, precision):
    weights = band_matrix(height + 2 * HALF, height, dtype)
    return jnp.einsum(
        "kpb,kl->lpb", values, weights, precision=precision, preferred_element_type=jnp.float32
    )


def shards(cube):
    lines_dev, pix_dev, bands = cube.shape
    n_track = lax.axis_size("track")
    n_cross = lax.axis_size("cross")
    total_lines = lines_dev * n_track
    total_pix = pix_dev * n_cross
    highest = lax.Precision.HIGHEST
    extended = with_halo(cube, (("track", 0), ("cross", 1)), HALF)
    across = sum_pixels(extended, pix_dev, jnp.bfloat16)
    window = sum_lines(across, lines_dev, jnp.float32, highest)
    line_count = window_count(lax.axis_index("track") * lines_dev, lines_dev, total_lines)
    pixel_count = window_count(lax.axis_index("cross") * pix_dev, pix_dev, total_pix)
    count = line_count[:, None, None] * pixel_count[None, :, None]
    residual = cube.astype(jnp.float32) - window / count
    flat = residual.reshape(lines_dev * pix_dev, bands)
    flat_bf = flat.astype(jnp.bfloat16)
    partial_cov = jnp.dot(flat_bf.T, flat_bf, preferred_element_type=jnp.float32)
    packed = butterfly_sum(butterfly_sum(pack_symmetric(partial_cov), "cross"), "track")
    covariance = unpack_symmetric(packed) / (total_lines * total_pix)
    identity = jnp.eye(bands, dtype=jnp.float32)
    loaded = covariance + LOAD * (jnp.trace(covariance) / bands) * identity
    factor = jnp.linalg.cholesky(loaded)
    inverse = jax.scipy.linalg.solve_triangular(factor, identity, lower=True)
    whitened = jnp.dot(flat, inverse.T, precision=highest, preferred_element_type=jnp.float32)
    scores = jnp.sum(whitened * whitened, axis=1) / bands
    return scores.reshape(lines_dev, pix_dev)


def solution(mesh):
    return jax.shard_map(
        shards,
        mesh=mesh,
        in_specs=(P("track", "cross", None),),
        out_specs=P("track", "cross"),
        check_vma=False,
    )
```

```python
import functools

import jax
import jax.numpy as jnp
from jax import lax
from jax.experimental import pallas as pl
from jax.sharding import PartitionSpec as P

HALF = 15


LOAD = 0.02


def with_halo(block, sides, width):
    for axis, dim in sides:
        count = lax.axis_size(axis)
        forward = [(i, i + 1) for i in range(count - 1)]
        backward = [(target, source) for source, target in forward]
        low = lax.ppermute(
            lax.slice_in_dim(block, block.shape[dim] - width, None, axis=dim), axis, forward
        )
        high = lax.ppermute(lax.slice_in_dim(block, 0, width, axis=dim), axis, backward)
        block = jnp.concatenate([low, block, high], axis=dim)
    return block


def band_matrix(rows_in, rows_out, dtype):
    source = jnp.arange(rows_in)[:, None]
    target = jnp.arange(rows_out)[None, :]
    inside = (source >= target) & (source <= target + 2 * HALF)
    return inside.astype(dtype)


def butterfly_sum(x, axis):
    count = lax.axis_size(axis)
    step = 1
    while step < count:
        pairs = [(i, i ^ step) for i in range(count)]
        x = x + lax.ppermute(x, axis, pairs)
        step *= 2
    return x


def pack_symmetric(c):
    h = c.shape[0] // 2
    row = jnp.arange(h)[:, None]
    col = jnp.arange(h)[None, :]
    c11, c12, c22 = c[:h, :h], c[:h, h:], c[h:, h:]
    mixed = jnp.where(col >= row, c11, c22)
    return jnp.concatenate([c12, mixed, jnp.diagonal(c22)[None, :]], axis=0)


def unpack_symmetric(p):
    h = p.shape[1]
    row = jnp.arange(h)[:, None]
    col = jnp.arange(h)[None, :]
    c12, mixed, d22 = p[:h], p[h:2 * h], p[2 * h]
    c11 = jnp.where(col >= row, mixed, mixed.T)
    c22 = jnp.where(col < row, mixed, mixed.T)
    c22 = jnp.where(col == row, d22[None, :], c22)
    top = jnp.concatenate([c11, c12], axis=1)
    bottom = jnp.concatenate([c12.T, c22], axis=1)
    return jnp.concatenate([top, bottom], axis=0)


def sweep_kernel(n, a_ref, o_ref):
    size = a_ref.shape[0]
    o_ref[...] = a_ref[...]
    rows = lax.broadcasted_iota(jnp.int32, (size, 1), 0)
    lanes = lax.broadcasted_iota(jnp.int32, (1, size), 1)
    sub8 = lax.broadcasted_iota(jnp.int32, (8, 1), 0)

    def body(k, carry):
        base = pl.multiple_of((k // 8) * 8, 8)
        slab = o_ref[pl.ds(base, 8), :]
        row = jnp.sum(jnp.where(sub8 == k - base, slab, 0.0), axis=0, keepdims=True)
        pivot = jnp.sum(jnp.where(lanes == k, row, 0.0), axis=1, keepdims=True)
        inv = 1.0 / pivot
        a = o_ref[...]
        col = jnp.sum(jnp.where(lanes == k, a, 0.0), axis=1, keepdims=True)
        u = col * inv
        scaled = row * inv
        at_row = rows == k
        at_col = lanes == k
        edge = jnp.where(at_col, jnp.where(at_row, -inv, u), scaled)
        o_ref[...] = jnp.where(at_row | at_col, edge, a - u * row)
        return carry

    lax.fori_loop(0, n, body, 0)


def spd_inverse(a):
    n = a.shape[0]
    size = -(-n // 128) * 128
    padded = jnp.eye(size, dtype=jnp.float32).at[:n, :n].set(a)
    swept = pl.pallas_call(
        functools.partial(sweep_kernel, n),
        out_shape=jax.ShapeDtypeStruct((size, size), jnp.float32),
    )(padded)
    return -swept[:n, :n]


def window_count(first, local, total):
    index = first + jnp.arange(local)
    upper = jnp.minimum(index + HALF, total - 1)
    lower = jnp.maximum(index - HALF, 0)
    return (upper - lower + 1).astype(jnp.float32)


def sum_pixels(values, width, dtype):
    weights = band_matrix(width + 2 * HALF, width, dtype)
    return jnp.einsum(
        "lqb,qp->lpb", values, weights, precision=None, preferred_element_type=jnp.float32
    )


def sum_lines(values, height, dtype, precision):
    weights = band_matrix(height + 2 * HALF, height, dtype)
    return jnp.einsum(
        "kpb,kl->lpb", values, weights, precision=precision, preferred_element_type=jnp.float32
    )


def shards(cube):
    lines_dev, pix_dev, bands = cube.shape
    n_track = lax.axis_size("track")
    n_cross = lax.axis_size("cross")
    total_lines = lines_dev * n_track
    total_pix = pix_dev * n_cross
    highest = lax.Precision.HIGHEST
    extended = with_halo(cube, (("track", 0), ("cross", 1)), HALF)
    across = sum_pixels(extended, pix_dev, jnp.bfloat16)
    window = sum_lines(across, lines_dev, jnp.float32, highest)
    line_count = window_count(lax.axis_index("track") * lines_dev, lines_dev, total_lines)
    pixel_count = window_count(lax.axis_index("cross") * pix_dev, pix_dev, total_pix)
    count = line_count[:, None, None] * pixel_count[None, :, None]
    residual = cube.astype(jnp.float32) - window / count
    flat = residual.reshape(lines_dev * pix_dev, bands)
    flat_bf = flat.astype(jnp.bfloat16)
    partial_cov = jnp.dot(flat_bf.T, flat_bf, preferred_element_type=jnp.float32)
    packed = butterfly_sum(butterfly_sum(pack_symmetric(partial_cov), "cross"), "track")
    covariance = unpack_symmetric(packed) / (total_lines * total_pix)
    identity = jnp.eye(bands, dtype=jnp.float32)
    loaded = covariance + LOAD * (jnp.trace(covariance) / bands) * identity
    inverse = spd_inverse(loaded)
    solved = jnp.dot(flat, inverse, precision=highest, preferred_element_type=jnp.float32)
    scores = jnp.sum(flat * solved, axis=1) / bands
    return scores.reshape(lines_dev, pix_dev)


def solution(mesh):
    return jax.shard_map(
        shards,
        mesh=mesh,
        in_specs=(P("track", "cross", None),),
        out_specs=P("track", "cross"),
        check_vma=False,
    )
```

```python
import functools

import jax
import jax.numpy as jnp
from jax import lax
from jax.experimental import pallas as pl
from jax.experimental.layout import Layout, with_layout_constraint
from jax.sharding import PartitionSpec as P

HALF = 15


LOAD = 0.02


def with_halo(block, sides, width):
    for axis, dim in sides:
        count = lax.axis_size(axis)
        forward = [(i, i + 1) for i in range(count - 1)]
        backward = [(target, source) for source, target in forward]
        low = lax.ppermute(
            lax.slice_in_dim(block, block.shape[dim] - width, None, axis=dim), axis, forward
        )
        high = lax.ppermute(lax.slice_in_dim(block, 0, width, axis=dim), axis, backward)
        block = jnp.concatenate([low, block, high], axis=dim)
    return block


def band_matrix(rows_in, rows_out, dtype):
    source = jnp.arange(rows_in)[:, None]
    target = jnp.arange(rows_out)[None, :]
    inside = (source >= target) & (source <= target + 2 * HALF)
    return inside.astype(dtype)


def butterfly_sum(x, axis):
    count = lax.axis_size(axis)
    step = 1
    while step < count:
        pairs = [(i, i ^ step) for i in range(count)]
        x = x + lax.ppermute(x, axis, pairs)
        step *= 2
    return x


def pack_symmetric(c):
    h = c.shape[0] // 2
    row = jnp.arange(h)[:, None]
    col = jnp.arange(h)[None, :]
    c11, c12, c22 = c[:h, :h], c[:h, h:], c[h:, h:]
    mixed = jnp.where(col >= row, c11, c22)
    return jnp.concatenate([c12, mixed, jnp.diagonal(c22)[None, :]], axis=0)


def unpack_symmetric(p):
    h = p.shape[1]
    row = jnp.arange(h)[:, None]
    col = jnp.arange(h)[None, :]
    c12, mixed, d22 = p[:h], p[h:2 * h], p[2 * h]
    c11 = jnp.where(col >= row, mixed, mixed.T)
    c22 = jnp.where(col < row, mixed, mixed.T)
    c22 = jnp.where(col == row, d22[None, :], c22)
    top = jnp.concatenate([c11, c12], axis=1)
    bottom = jnp.concatenate([c12.T, c22], axis=1)
    return jnp.concatenate([top, bottom], axis=0)


def sweep_kernel(n, a_ref, o_ref):
    size = a_ref.shape[0]
    o_ref[...] = a_ref[...]
    rows = lax.broadcasted_iota(jnp.int32, (size, 1), 0)
    lanes = lax.broadcasted_iota(jnp.int32, (1, size), 1)
    sub8 = lax.broadcasted_iota(jnp.int32, (8, 1), 0)

    def body(k, carry):
        base = pl.multiple_of((k // 8) * 8, 8)
        slab = o_ref[pl.ds(base, 8), :]
        row = jnp.sum(jnp.where(sub8 == k - base, slab, 0.0), axis=0, keepdims=True)
        pivot = jnp.sum(jnp.where(lanes == k, row, 0.0), axis=1, keepdims=True)
        inv = 1.0 / pivot
        a = o_ref[...]
        col = jnp.sum(jnp.where(lanes == k, a, 0.0), axis=1, keepdims=True)
        u = col * inv
        scaled = row * inv
        at_row = rows == k
        at_col = lanes == k
        edge = jnp.where(at_col, jnp.where(at_row, -inv, u), scaled)
        o_ref[...] = jnp.where(at_row | at_col, edge, a - u * row)
        return carry

    lax.fori_loop(0, n, body, 0)


def spd_inverse(a):
    n = a.shape[0]
    size = -(-n // 128) * 128
    padded = jnp.eye(size, dtype=jnp.float32).at[:n, :n].set(a)
    swept = pl.pallas_call(
        functools.partial(sweep_kernel, n),
        out_shape=jax.ShapeDtypeStruct((size, size), jnp.float32),
    )(padded)
    return -swept[:n, :n]


def window_count(first, local, total):
    index = first + jnp.arange(local)
    upper = jnp.minimum(index + HALF, total - 1)
    lower = jnp.maximum(index - HALF, 0)
    return (upper - lower + 1).astype(jnp.float32)


def sum_pixels(values, width, dtype):
    weights = band_matrix(width + 2 * HALF, width, dtype)
    return jnp.einsum(
        "lqb,qp->lpb", values, weights, precision=None, preferred_element_type=jnp.float32
    )


def sum_lines(values, height, dtype, precision):
    weights = band_matrix(height + 2 * HALF, height, dtype)
    return jnp.einsum(
        "kpb,kl->lpb", values, weights, precision=precision, preferred_element_type=jnp.float32
    )


def neighbour_pairs(n_track, n_cross, dt, dc):
    pairs = []
    for t in range(n_track):
        for c in range(n_cross):
            if 0 <= t + dt < n_track and 0 <= c + dc < n_cross:
                pairs.append(((t + dt) * n_cross + c + dc, t * n_cross + c))
    return pairs


def halos(cube):
    n_track = lax.axis_size("track")
    n_cross = lax.axis_size("cross")
    both = ("track", "cross")

    def fetch(piece, dt, dc):
        if dt == 0:
            pairs = [(c + dc, c) for c in range(n_cross) if 0 <= c + dc < n_cross]
            return lax.ppermute(piece, "cross", pairs)
        if dc == 0:
            pairs = [(t + dt, t) for t in range(n_track) if 0 <= t + dt < n_track]
            return lax.ppermute(piece, "track", pairs)
        return lax.ppermute(piece, both, neighbour_pairs(n_track, n_cross, dt, dc))

    first, last = slice(0, HALF), slice(-HALF, None)
    top = fetch(cube[last], -1, 0)
    bottom = fetch(cube[first], 1, 0)
    left = fetch(cube[:, last], 0, -1)
    right = fetch(cube[:, first], 0, 1)
    top_left = fetch(cube[last, last], -1, -1)
    top_right = fetch(cube[last, first], -1, 1)
    bottom_left = fetch(cube[first, last], 1, -1)
    bottom_right = fetch(cube[first, first], 1, 1)
    middle = jnp.concatenate([top, cube, bottom], axis=0)
    left = jnp.concatenate([top_left, left, bottom_left], axis=0)
    right = jnp.concatenate([top_right, right, bottom_right], axis=0)
    return left, middle, right


def pixel_weights(width):
    target = jnp.arange(width)[:, None]
    middle = jnp.abs(jnp.arange(width)[None, :] - target) <= HALF
    side = jnp.arange(HALF)[None, :]
    left = side >= target
    right = side <= target + HALF - width
    return left, middle, right


def contract_pixels(weights, values):
    return lax.dot_general(
        weights.astype(values.dtype), values, (((1,), (1,)), ((), ())),
        preferred_element_type=jnp.float32,
    )


def shards(cube):
    lines_dev, pix_dev, bands = cube.shape
    n_track = lax.axis_size("track")
    n_cross = lax.axis_size("cross")
    total_lines = lines_dev * n_track
    total_pix = pix_dev * n_cross
    highest = lax.Precision.HIGHEST
    left, middle, right = halos(cube)
    w_left, w_mid, w_right = pixel_weights(pix_dev)
    across = contract_pixels(w_mid, middle)
    across = across + contract_pixels(w_left, left) + contract_pixels(w_right, right)
    line_weights = band_matrix(lines_dev + 2 * HALF, lines_dev, jnp.float32).T
    window = lax.dot_general(
        line_weights, across, (((1,), (1,)), ((), ())),
        precision=highest, preferred_element_type=jnp.float32,
    )
    window = with_layout_constraint(window, Layout((0, 1, 2)))
    line_count = window_count(lax.axis_index("track") * lines_dev, lines_dev, total_lines)
    pixel_count = window_count(lax.axis_index("cross") * pix_dev, pix_dev, total_pix)
    count = line_count[:, None, None] * pixel_count[None, :, None]
    residual = cube.astype(jnp.float32) - window / count
    flat = residual.reshape(lines_dev * pix_dev, bands)
    flat_bf = flat.astype(jnp.bfloat16)
    partial_cov = jnp.dot(flat_bf.T, flat_bf, preferred_element_type=jnp.float32)
    packed = butterfly_sum(butterfly_sum(pack_symmetric(partial_cov), "cross"), "track")
    covariance = unpack_symmetric(packed) / (total_lines * total_pix)
    identity = jnp.eye(bands, dtype=jnp.float32)
    loaded = covariance + LOAD * (jnp.trace(covariance) / bands) * identity
    inverse = spd_inverse(loaded)
    solved = jnp.dot(flat, inverse, precision=highest, preferred_element_type=jnp.float32)
    scores = jnp.sum(flat * solved, axis=1) / bands
    return scores.reshape(lines_dev, pix_dev)


def solution(mesh):
    return jax.shard_map(
        shards,
        mesh=mesh,
        in_specs=(P("track", "cross", None),),
        out_specs=P("track", "cross"),
        check_vma=False,
    )
```

```python
import functools

import jax
import jax.numpy as jnp
from jax import lax
from jax.experimental import pallas as pl
from jax.experimental.layout import Layout, with_layout_constraint
from jax.sharding import PartitionSpec as P

HALF = 15


LOAD = 0.02


def with_halo(block, sides, width):
    for axis, dim in sides:
        count = lax.axis_size(axis)
        forward = [(i, i + 1) for i in range(count - 1)]
        backward = [(target, source) for source, target in forward]
        low = lax.ppermute(
            lax.slice_in_dim(block, block.shape[dim] - width, None, axis=dim), axis, forward
        )
        high = lax.ppermute(lax.slice_in_dim(block, 0, width, axis=dim), axis, backward)
        block = jnp.concatenate([low, block, high], axis=dim)
    return block


def band_matrix(rows_in, rows_out, dtype):
    source = jnp.arange(rows_in)[:, None]
    target = jnp.arange(rows_out)[None, :]
    inside = (source >= target) & (source <= target + 2 * HALF)
    return inside.astype(dtype)


def butterfly_sum(x, axis):
    count = lax.axis_size(axis)
    step = 1
    while step < count:
        pairs = [(i, i ^ step) for i in range(count)]
        x = x + lax.ppermute(x, axis, pairs)
        step *= 2
    return x


def pack_symmetric(c):
    h = c.shape[0] // 2
    row = jnp.arange(h)[:, None]
    col = jnp.arange(h)[None, :]
    c11, c12, c22 = c[:h, :h], c[:h, h:], c[h:, h:]
    mixed = jnp.where(col >= row, c11, c22)
    return jnp.concatenate([c12, mixed, jnp.diagonal(c22)[None, :]], axis=0)


def unpack_symmetric(p):
    h = p.shape[1]
    row = jnp.arange(h)[:, None]
    col = jnp.arange(h)[None, :]
    c12, mixed, d22 = p[:h], p[h:2 * h], p[2 * h]
    c11 = jnp.where(col >= row, mixed, mixed.T)
    c22 = jnp.where(col < row, mixed, mixed.T)
    c22 = jnp.where(col == row, d22[None, :], c22)
    top = jnp.concatenate([c11, c12], axis=1)
    bottom = jnp.concatenate([c12.T, c22], axis=1)
    return jnp.concatenate([top, bottom], axis=0)


def sweep_kernel(n, a_ref, o_ref):
    size = a_ref.shape[0]
    o_ref[...] = a_ref[...]
    rows = lax.broadcasted_iota(jnp.int32, (size, 1), 0)
    lanes = lax.broadcasted_iota(jnp.int32, (1, size), 1)
    sub8 = lax.broadcasted_iota(jnp.int32, (8, 1), 0)

    def body(k, carry):
        base = pl.multiple_of((k // 8) * 8, 8)
        slab = o_ref[pl.ds(base, 8), :]
        row = jnp.sum(jnp.where(sub8 == k - base, slab, 0.0), axis=0, keepdims=True)
        pivot = jnp.sum(jnp.where(lanes == k, row, 0.0), axis=1, keepdims=True)
        inv = 1.0 / pivot
        a = o_ref[...]
        col = jnp.sum(jnp.where(lanes == k, a, 0.0), axis=1, keepdims=True)
        u = col * inv
        scaled = row * inv
        at_row = rows == k
        at_col = lanes == k
        edge = jnp.where(at_col, jnp.where(at_row, -inv, u), scaled)
        o_ref[...] = jnp.where(at_row | at_col, edge, a - u * row)
        return carry

    lax.fori_loop(0, n, body, 0)


def spd_inverse(a):
    n = a.shape[0]
    size = -(-n // 128) * 128
    padded = jnp.eye(size, dtype=jnp.float32).at[:n, :n].set(a)
    swept = pl.pallas_call(
        functools.partial(sweep_kernel, n),
        out_shape=jax.ShapeDtypeStruct((size, size), jnp.float32),
    )(padded)
    return -swept[:n, :n]


def window_count(first, local, total):
    index = first + jnp.arange(local)
    upper = jnp.minimum(index + HALF, total - 1)
    lower = jnp.maximum(index - HALF, 0)
    return (upper - lower + 1).astype(jnp.float32)


def sum_pixels(values, width, dtype):
    weights = band_matrix(width + 2 * HALF, width, dtype)
    return jnp.einsum(
        "lqb,qp->lpb", values, weights, precision=None, preferred_element_type=jnp.float32
    )


def sum_lines(values, height, dtype, precision):
    weights = band_matrix(height + 2 * HALF, height, dtype)
    return jnp.einsum(
        "kpb,kl->lpb", values, weights, precision=precision, preferred_element_type=jnp.float32
    )


def neighbour_pairs(n_track, n_cross, dt, dc):
    pairs = []
    for t in range(n_track):
        for c in range(n_cross):
            if 0 <= t + dt < n_track and 0 <= c + dc < n_cross:
                pairs.append(((t + dt) * n_cross + c + dc, t * n_cross + c))
    return pairs


def halos(cube):
    n_track = lax.axis_size("track")
    n_cross = lax.axis_size("cross")
    both = ("track", "cross")

    def fetch(piece, dt, dc):
        if dt == 0:
            pairs = [(c + dc, c) for c in range(n_cross) if 0 <= c + dc < n_cross]
            return lax.ppermute(piece, "cross", pairs)
        if dc == 0:
            pairs = [(t + dt, t) for t in range(n_track) if 0 <= t + dt < n_track]
            return lax.ppermute(piece, "track", pairs)
        return lax.ppermute(piece, both, neighbour_pairs(n_track, n_cross, dt, dc))

    first, last = slice(0, HALF), slice(-HALF, None)
    top = fetch(cube[last], -1, 0)
    bottom = fetch(cube[first], 1, 0)
    left = fetch(cube[:, last], 0, -1)
    right = fetch(cube[:, first], 0, 1)
    top_left = fetch(cube[last, last], -1, -1)
    top_right = fetch(cube[last, first], -1, 1)
    bottom_left = fetch(cube[first, last], 1, -1)
    bottom_right = fetch(cube[first, first], 1, 1)
    middle = jnp.concatenate([top, cube, bottom], axis=0)
    left = jnp.concatenate([top_left, left, bottom_left], axis=0)
    right = jnp.concatenate([top_right, right, bottom_right], axis=0)
    return left, middle, right


def pixel_weights(width):
    target = jnp.arange(width)[:, None]
    middle = jnp.abs(jnp.arange(width)[None, :] - target) <= HALF
    side = jnp.arange(HALF)[None, :]
    left = side >= target
    right = side <= target + HALF - width
    return left, middle, right


def contract_pixels(weights, values):
    return lax.dot_general(
        weights.astype(values.dtype), values, (((1,), (1,)), ((), ())),
        preferred_element_type=jnp.float32,
    )


def shards(cube):
    lines_dev, pix_dev, bands = cube.shape
    n_track = lax.axis_size("track")
    n_cross = lax.axis_size("cross")
    total_lines = lines_dev * n_track
    total_pix = pix_dev * n_cross
    highest = lax.Precision.HIGHEST
    left, middle, right = halos(cube)
    w_left, w_mid, w_right = pixel_weights(pix_dev)
    across = contract_pixels(w_mid, middle)
    across = across + contract_pixels(w_left, left) + contract_pixels(w_right, right)
    line_weights = band_matrix(lines_dev + 2 * HALF, lines_dev, jnp.bfloat16).T
    window = None
    rest = across
    for _ in range(3):
        rounded = lax.reduce_precision(rest, exponent_bits=8, mantissa_bits=7)
        part = rounded.astype(jnp.bfloat16)
        rest = rest - rounded
        term = lax.dot_general(
            line_weights, part, (((1,), (1,)), ((), ())), preferred_element_type=jnp.float32
        )
        window = term if window is None else window + term
    line_count = window_count(lax.axis_index("track") * lines_dev, lines_dev, total_lines)
    pixel_count = window_count(lax.axis_index("cross") * pix_dev, pix_dev, total_pix)
    count = line_count[:, None, None] * pixel_count[None, :, None]
    residual = cube.astype(jnp.float32) - window / count
    residual_bf = residual.astype(jnp.bfloat16)
    partial_cov = jnp.einsum(
        "lpj,lpk->jk", residual_bf, residual_bf, preferred_element_type=jnp.float32
    )
    packed = butterfly_sum(butterfly_sum(pack_symmetric(partial_cov), "cross"), "track")
    covariance = unpack_symmetric(packed) / (total_lines * total_pix)
    identity = jnp.eye(bands, dtype=jnp.float32)
    loaded = covariance + LOAD * (jnp.trace(covariance) / bands) * identity
    inverse = spd_inverse(loaded)
    solved = jnp.einsum(
        "lpb,bj->lpj", residual, inverse, precision=highest, preferred_element_type=jnp.float32
    )
    scores = jnp.sum(residual * solved, axis=2) / bands
    return scores


def solution(mesh):
    return jax.shard_map(
        shards,
        mesh=mesh,
        in_specs=(P("track", "cross", None),),
        out_specs=P("track", "cross"),
        check_vma=False,
    )
```

```python
import functools

import jax
import jax.numpy as jnp
from jax import lax
from jax.experimental import pallas as pl
from jax.experimental.layout import Layout, with_layout_constraint
from jax.sharding import PartitionSpec as P

HALF = 15


LOAD = 0.02


def with_halo(block, sides, width):
    for axis, dim in sides:
        count = lax.axis_size(axis)
        forward = [(i, i + 1) for i in range(count - 1)]
        backward = [(target, source) for source, target in forward]
        low = lax.ppermute(
            lax.slice_in_dim(block, block.shape[dim] - width, None, axis=dim), axis, forward
        )
        high = lax.ppermute(lax.slice_in_dim(block, 0, width, axis=dim), axis, backward)
        block = jnp.concatenate([low, block, high], axis=dim)
    return block


def band_matrix(rows_in, rows_out, dtype):
    source = jnp.arange(rows_in)[:, None]
    target = jnp.arange(rows_out)[None, :]
    inside = (source >= target) & (source <= target + 2 * HALF)
    return inside.astype(dtype)


def butterfly_sum(x, axis):
    count = lax.axis_size(axis)
    step = 1
    while step < count:
        pairs = [(i, i ^ step) for i in range(count)]
        x = x + lax.ppermute(x, axis, pairs)
        step *= 2
    return x


def pack_symmetric(c):
    h = c.shape[0] // 2
    row = jnp.arange(h)[:, None]
    col = jnp.arange(h)[None, :]
    c11, c12, c22 = c[:h, :h], c[:h, h:], c[h:, h:]
    mixed = jnp.where(col >= row, c11, c22)
    return jnp.concatenate([c12, mixed, jnp.diagonal(c22)[None, :]], axis=0)


def unpack_symmetric(p):
    h = p.shape[1]
    row = jnp.arange(h)[:, None]
    col = jnp.arange(h)[None, :]
    c12, mixed, d22 = p[:h], p[h:2 * h], p[2 * h]
    c11 = jnp.where(col >= row, mixed, mixed.T)
    c22 = jnp.where(col < row, mixed, mixed.T)
    c22 = jnp.where(col == row, d22[None, :], c22)
    top = jnp.concatenate([c11, c12], axis=1)
    bottom = jnp.concatenate([c12.T, c22], axis=1)
    return jnp.concatenate([top, bottom], axis=0)


def sweep_kernel(n, a_ref, o_ref):
    size = a_ref.shape[0]
    o_ref[...] = a_ref[...]
    rows = lax.broadcasted_iota(jnp.int32, (size, 1), 0)
    lanes = lax.broadcasted_iota(jnp.int32, (1, size), 1)
    sub8 = lax.broadcasted_iota(jnp.int32, (8, 1), 0)

    def body(k, carry):
        base = pl.multiple_of((k // 8) * 8, 8)
        slab = o_ref[pl.ds(base, 8), :]
        row = jnp.sum(jnp.where(sub8 == k - base, slab, 0.0), axis=0, keepdims=True)
        pivot = jnp.sum(jnp.where(lanes == k, row, 0.0), axis=1, keepdims=True)
        inv = 1.0 / pivot
        a = o_ref[...]
        col = jnp.sum(jnp.where(lanes == k, a, 0.0), axis=1, keepdims=True)
        u = col * inv
        scaled = row * inv
        at_row = rows == k
        at_col = lanes == k
        edge = jnp.where(at_col, jnp.where(at_row, -inv, u), scaled)
        o_ref[...] = jnp.where(at_row | at_col, edge, a - u * row)
        return carry

    lax.fori_loop(0, n, body, 0)


def spd_inverse(a):
    n = a.shape[0]
    size = -(-n // 128) * 128
    padded = jnp.eye(size, dtype=jnp.float32).at[:n, :n].set(a)
    swept = pl.pallas_call(
        functools.partial(sweep_kernel, n),
        out_shape=jax.ShapeDtypeStruct((size, size), jnp.float32),
    )(padded)
    return -swept[:n, :n]


def window_count(first, local, total):
    index = first + jnp.arange(local)
    upper = jnp.minimum(index + HALF, total - 1)
    lower = jnp.maximum(index - HALF, 0)
    return (upper - lower + 1).astype(jnp.float32)


def sum_pixels(values, width, dtype):
    weights = band_matrix(width + 2 * HALF, width, dtype)
    return jnp.einsum(
        "lqb,qp->lpb", values, weights, precision=None, preferred_element_type=jnp.float32
    )


def sum_lines(values, height, dtype, precision):
    weights = band_matrix(height + 2 * HALF, height, dtype)
    return jnp.einsum(
        "kpb,kl->lpb", values, weights, precision=precision, preferred_element_type=jnp.float32
    )


def neighbour_pairs(n_track, n_cross, dt, dc):
    pairs = []
    for t in range(n_track):
        for c in range(n_cross):
            if 0 <= t + dt < n_track and 0 <= c + dc < n_cross:
                pairs.append(((t + dt) * n_cross + c + dc, t * n_cross + c))
    return pairs


def halos(planes):
    n_track = lax.axis_size("track")
    n_cross = lax.axis_size("cross")
    both = ("track", "cross")

    def fetch(piece, dt, dc):
        if dt == 0:
            pairs = [(c + dc, c) for c in range(n_cross) if 0 <= c + dc < n_cross]
            return lax.ppermute(piece, "cross", pairs)
        if dc == 0:
            pairs = [(t + dt, t) for t in range(n_track) if 0 <= t + dt < n_track]
            return lax.ppermute(piece, "track", pairs)
        return lax.ppermute(piece, both, neighbour_pairs(n_track, n_cross, dt, dc))

    first, last = slice(0, HALF), slice(-HALF, None)
    sides = {
        "left": fetch(planes[last], 0, -1),
        "right": fetch(planes[first], 0, 1),
    }
    tops = {
        "left": fetch(planes[last, :, last], -1, -1),
        "middle": fetch(planes[:, :, last], -1, 0),
        "right": fetch(planes[first, :, last], -1, 1),
    }
    bottoms = {
        "left": fetch(planes[last, :, first], 1, -1),
        "middle": fetch(planes[:, :, first], 1, 0),
        "right": fetch(planes[first, :, first], 1, 1),
    }
    return sides, tops, bottoms


def line_weights(lines):
    target = jnp.arange(lines)[None, :]
    middle = jnp.abs(jnp.arange(lines)[:, None] - target) <= HALF
    side = jnp.arange(HALF)[:, None]
    top = target <= side
    bottom = target >= lines - HALF + side
    return [w.astype(jnp.bfloat16) for w in (top, middle, bottom)]


def sum_lines(top, middle, bottom, weights):
    total = None
    for values, w in zip((top, middle, bottom), weights):
        term = jnp.einsum("qbk,kl->qbl", values, w, preferred_element_type=jnp.float32)
        total = term if total is None else total + term
    return total


def pixel_window_kernel(left_ref, middle_ref, right_ref, out_ref):
    refs = [(left_ref, q) for q in range(left_ref.shape[0])]
    refs += [(middle_ref, q) for q in range(middle_ref.shape[0])]
    refs += [(right_ref, q) for q in range(right_ref.shape[0])]

    def plane(q):
        ref, i = refs[q]
        return ref[i]

    span = 2 * HALF + 1
    running = plane(0)
    for q in range(1, span):
        running = running + plane(q)
    out_ref[0] = running
    for p in range(1, out_ref.shape[0]):
        running = running + plane(p + span - 1) - plane(p - 1)
        out_ref[p] = running


def sum_pixels(left, middle, right):
    width, bands, lines = middle.shape
    block = 32 if bands % 32 == 0 else bands
    spec = lambda n: pl.BlockSpec((n, block, lines), lambda i: (0, i, 0))
    return pl.pallas_call(
        pixel_window_kernel,
        grid=(bands // block,),
        in_specs=[spec(left.shape[0]), spec(width), spec(right.shape[0])],
        out_specs=spec(width),
        out_shape=jax.ShapeDtypeStruct((width, bands, lines), jnp.float32),
    )(left, middle, right)


def shards(cube):
    lines_dev, pix_dev, bands = cube.shape
    n_track = lax.axis_size("track")
    n_cross = lax.axis_size("cross")
    total_lines = lines_dev * n_track
    total_pix = pix_dev * n_cross
    highest = lax.Precision.HIGHEST
    planes = jnp.transpose(cube, (1, 2, 0))
    sides, tops, bottoms = halos(planes)
    weights = line_weights(lines_dev)
    middle = sum_lines(tops["middle"], planes, bottoms["middle"], weights)
    left = sum_lines(tops["left"], sides["left"], bottoms["left"], weights)
    right = sum_lines(tops["right"], sides["right"], bottoms["right"], weights)
    window = sum_pixels(left, middle, right)
    line_count = window_count(lax.axis_index("track") * lines_dev, lines_dev, total_lines)
    pixel_count = window_count(lax.axis_index("cross") * pix_dev, pix_dev, total_pix)
    count = pixel_count[:, None, None] * line_count[None, None, :]
    residual = planes.astype(jnp.float32) - window / count
    residual_bf = residual.astype(jnp.bfloat16)
    partial_cov = jnp.einsum(
        "pjl,pkl->jk", residual_bf, residual_bf, preferred_element_type=jnp.float32
    )
    packed = butterfly_sum(butterfly_sum(pack_symmetric(partial_cov), "cross"), "track")
    covariance = unpack_symmetric(packed) / (total_lines * total_pix)
    identity = jnp.eye(bands, dtype=jnp.float32)
    loaded = covariance + LOAD * (jnp.trace(covariance) / bands) * identity
    inverse = spd_inverse(loaded)
    solved = jnp.einsum(
        "pbl,bj->pjl", residual, inverse, precision=highest, preferred_element_type=jnp.float32
    )
    scores = jnp.sum(residual * solved, axis=1) / bands
    return scores.T


def solution(mesh):
    return jax.shard_map(
        shards,
        mesh=mesh,
        in_specs=(P("track", "cross", None),),
        out_specs=P("track", "cross"),
        check_vma=False,
    )
```

```python
import functools

import jax
import jax.numpy as jnp
from jax import lax
from jax.experimental import pallas as pl
from jax.experimental.layout import Layout, with_layout_constraint
from jax.sharding import PartitionSpec as P

HALF = 15


LOAD = 0.02


def with_halo(block, sides, width):
    for axis, dim in sides:
        count = lax.axis_size(axis)
        forward = [(i, i + 1) for i in range(count - 1)]
        backward = [(target, source) for source, target in forward]
        low = lax.ppermute(
            lax.slice_in_dim(block, block.shape[dim] - width, None, axis=dim), axis, forward
        )
        high = lax.ppermute(lax.slice_in_dim(block, 0, width, axis=dim), axis, backward)
        block = jnp.concatenate([low, block, high], axis=dim)
    return block


def band_matrix(rows_in, rows_out, dtype):
    source = jnp.arange(rows_in)[:, None]
    target = jnp.arange(rows_out)[None, :]
    inside = (source >= target) & (source <= target + 2 * HALF)
    return inside.astype(dtype)


def butterfly_sum(x, axis):
    count = lax.axis_size(axis)
    step = 1
    while step < count:
        pairs = [(i, i ^ step) for i in range(count)]
        x = x + lax.ppermute(x, axis, pairs)
        step *= 2
    return x


def ring_sum(x, axis, stride):
    count = lax.axis_size(axis)
    groups = count // stride
    total = x
    for shift in range(1, groups):
        pairs = [
            (i, (i + shift * stride) % count) for i in range(count)
        ]
        total = total + lax.ppermute(x, axis, pairs)
    return total


def pack_symmetric(c):
    h = c.shape[0] // 2
    row = jnp.arange(h)[:, None]
    col = jnp.arange(h)[None, :]
    c11, c12, c22 = c[:h, :h], c[:h, h:], c[h:, h:]
    mixed = jnp.where(col >= row, c11, c22)
    return jnp.concatenate([c12, mixed, jnp.diagonal(c22)[None, :]], axis=0)


def unpack_symmetric(p):
    h = p.shape[1]
    row = jnp.arange(h)[:, None]
    col = jnp.arange(h)[None, :]
    c12, mixed, d22 = p[:h], p[h:2 * h], p[2 * h]
    c11 = jnp.where(col >= row, mixed, mixed.T)
    c22 = jnp.where(col < row, mixed, mixed.T)
    c22 = jnp.where(col == row, d22[None, :], c22)
    top = jnp.concatenate([c11, c12], axis=1)
    bottom = jnp.concatenate([c12.T, c22], axis=1)
    return jnp.concatenate([top, bottom], axis=0)


def sweep_kernel(n, a_ref, o_ref):
    size = a_ref.shape[0]
    o_ref[...] = a_ref[...]
    rows = lax.broadcasted_iota(jnp.int32, (size, 1), 0)
    lanes = lax.broadcasted_iota(jnp.int32, (1, size), 1)
    sub8 = lax.broadcasted_iota(jnp.int32, (8, 1), 0)

    def body(k, carry):
        base = pl.multiple_of((k // 8) * 8, 8)
        slab = o_ref[pl.ds(base, 8), :]
        row = jnp.sum(jnp.where(sub8 == k - base, slab, 0.0), axis=0, keepdims=True)
        pivot = jnp.sum(jnp.where(lanes == k, row, 0.0), axis=1, keepdims=True)
        inv = 1.0 / pivot
        a = o_ref[...]
        col = jnp.sum(jnp.where(lanes == k, a, 0.0), axis=1, keepdims=True)
        u = col * inv
        scaled = row * inv
        at_row = rows == k
        at_col = lanes == k
        edge = jnp.where(at_col, jnp.where(at_row, -inv, u), scaled)
        o_ref[...] = jnp.where(at_row | at_col, edge, a - u * row)
        return carry

    lax.fori_loop(0, n, body, 0)


def spd_inverse(a):
    n = a.shape[0]
    size = -(-n // 128) * 128
    padded = jnp.eye(size, dtype=jnp.float32).at[:n, :n].set(a)
    swept = pl.pallas_call(
        functools.partial(sweep_kernel, n),
        out_shape=jax.ShapeDtypeStruct((size, size), jnp.float32),
    )(padded)
    return -swept[:n, :n]


def window_count(first, local, total):
    index = first + jnp.arange(local)
    upper = jnp.minimum(index + HALF, total - 1)
    lower = jnp.maximum(index - HALF, 0)
    return (upper - lower + 1).astype(jnp.float32)


def sum_pixels(values, width, dtype):
    weights = band_matrix(width + 2 * HALF, width, dtype)
    return jnp.einsum(
        "lqb,qp->lpb", values, weights, precision=None, preferred_element_type=jnp.float32
    )


def sum_lines(values, height, dtype, precision):
    weights = band_matrix(height + 2 * HALF, height, dtype)
    return jnp.einsum(
        "kpb,kl->lpb", values, weights, precision=precision, preferred_element_type=jnp.float32
    )


def neighbour_pairs(n_track, n_cross, dt, dc):
    pairs = []
    for t in range(n_track):
        for c in range(n_cross):
            if 0 <= t + dt < n_track and 0 <= c + dc < n_cross:
                pairs.append(((t + dt) * n_cross + c + dc, t * n_cross + c))
    return pairs


def halos(planes):
    n_track = lax.axis_size("track")
    n_cross = lax.axis_size("cross")
    both = ("track", "cross")

    def fetch(piece, dt, dc):
        if dt == 0:
            pairs = [(c + dc, c) for c in range(n_cross) if 0 <= c + dc < n_cross]
            return lax.ppermute(piece, "cross", pairs)
        if dc == 0:
            pairs = [(t + dt, t) for t in range(n_track) if 0 <= t + dt < n_track]
            return lax.ppermute(piece, "track", pairs)
        return lax.ppermute(piece, both, neighbour_pairs(n_track, n_cross, dt, dc))

    first, last = slice(0, HALF), slice(-HALF, None)
    sides = {
        "left": fetch(planes[last], 0, -1),
        "right": fetch(planes[first], 0, 1),
    }
    tops = {
        "left": fetch(planes[last, :, last], -1, -1),
        "middle": fetch(planes[:, :, last], -1, 0),
        "right": fetch(planes[first, :, last], -1, 1),
    }
    bottoms = {
        "left": fetch(planes[last, :, first], 1, -1),
        "middle": fetch(planes[:, :, first], 1, 0),
        "right": fetch(planes[first, :, first], 1, 1),
    }
    return sides, tops, bottoms


def line_weights(lines):
    target = jnp.arange(lines)[None, :]
    middle = jnp.abs(jnp.arange(lines)[:, None] - target) <= HALF
    side = jnp.arange(HALF)[:, None]
    top = target <= side
    bottom = target >= lines - HALF + side
    return [w.astype(jnp.bfloat16) for w in (top, middle, bottom)]


def sum_lines(top, middle, bottom, weights):
    total = None
    for values, w in zip((top, middle, bottom), weights):
        term = jnp.einsum("qbk,kl->qbl", values, w, preferred_element_type=jnp.float32)
        total = term if total is None else total + term
    return total


def pixel_window_kernel(left_ref, middle_ref, right_ref, out_ref):
    refs = [(left_ref, q) for q in range(left_ref.shape[0])]
    refs += [(middle_ref, q) for q in range(middle_ref.shape[0])]
    refs += [(right_ref, q) for q in range(right_ref.shape[0])]

    def plane(q):
        ref, i = refs[q]
        return ref[i]

    span = 2 * HALF + 1
    running = plane(0)
    for q in range(1, span):
        running = running + plane(q)
    out_ref[0] = running
    for p in range(1, out_ref.shape[0]):
        running = running + plane(p + span - 1) - plane(p - 1)
        out_ref[p] = running


def sum_pixels(left, middle, right):
    width, bands, lines = middle.shape
    block = 32 if bands % 32 == 0 else bands
    spec = lambda n: pl.BlockSpec((n, block, lines), lambda i: (0, i, 0))
    return pl.pallas_call(
        pixel_window_kernel,
        grid=(bands // block,),
        in_specs=[spec(left.shape[0]), spec(width), spec(right.shape[0])],
        out_specs=spec(width),
        out_shape=jax.ShapeDtypeStruct((width, bands, lines), jnp.float32),
    )(left, middle, right)


def shards(cube):
    lines_dev, pix_dev, bands = cube.shape
    n_track = lax.axis_size("track")
    n_cross = lax.axis_size("cross")
    total_lines = lines_dev * n_track
    total_pix = pix_dev * n_cross
    highest = lax.Precision.HIGHEST
    planes = jnp.transpose(cube, (1, 2, 0))
    sides, tops, bottoms = halos(planes)
    weights = line_weights(lines_dev)
    middle = sum_lines(tops["middle"], planes, bottoms["middle"], weights)
    left = sum_lines(tops["left"], sides["left"], bottoms["left"], weights)
    right = sum_lines(tops["right"], sides["right"], bottoms["right"], weights)
    window = sum_pixels(left, middle, right)
    line_count = window_count(lax.axis_index("track") * lines_dev, lines_dev, total_lines)
    pixel_count = window_count(lax.axis_index("cross") * pix_dev, pix_dev, total_pix)
    count = pixel_count[:, None, None] * line_count[None, None, :]
    residual = planes.astype(jnp.float32) - window / count
    residual_bf = residual.astype(jnp.bfloat16)
    partial_cov = jnp.einsum(
        "pjl,pkl->jk", residual_bf, residual_bf, preferred_element_type=jnp.float32
    )
    packed = pack_symmetric(partial_cov)
    packed = packed + lax.ppermute(packed, "cross", [(i, i ^ 1) for i in range(n_cross)])
    packed = ring_sum(ring_sum(packed, "cross", 2), "track", 1)
    covariance = unpack_symmetric(packed) / (total_lines * total_pix)
    identity = jnp.eye(bands, dtype=jnp.float32)
    loaded = covariance + LOAD * (jnp.trace(covariance) / bands) * identity
    inverse = spd_inverse(loaded)
    solved = jnp.einsum(
        "pbl,bj->pjl", residual, inverse, precision=highest, preferred_element_type=jnp.float32
    )
    scores = jnp.sum(residual * solved, axis=1) / bands
    return scores.T


def solution(mesh):
    return jax.shard_map(
        shards,
        mesh=mesh,
        in_specs=(P("track", "cross", None),),
        out_specs=P("track", "cross"),
        check_vma=False,
    )
```

```python
import functools

import jax
import jax.numpy as jnp
from jax import lax
from jax.experimental import pallas as pl
from jax.experimental.layout import Layout, with_layout_constraint
from jax.sharding import PartitionSpec as P

HALF = 15


LOAD = 0.02


def with_halo(block, sides, width):
    for axis, dim in sides:
        count = lax.axis_size(axis)
        forward = [(i, i + 1) for i in range(count - 1)]
        backward = [(target, source) for source, target in forward]
        low = lax.ppermute(
            lax.slice_in_dim(block, block.shape[dim] - width, None, axis=dim), axis, forward
        )
        high = lax.ppermute(lax.slice_in_dim(block, 0, width, axis=dim), axis, backward)
        block = jnp.concatenate([low, block, high], axis=dim)
    return block


def band_matrix(rows_in, rows_out, dtype):
    source = jnp.arange(rows_in)[:, None]
    target = jnp.arange(rows_out)[None, :]
    inside = (source >= target) & (source <= target + 2 * HALF)
    return inside.astype(dtype)


def butterfly_sum(x, axis):
    count = lax.axis_size(axis)
    step = 1
    while step < count:
        pairs = [(i, i ^ step) for i in range(count)]
        x = x + lax.ppermute(x, axis, pairs)
        step *= 2
    return x


def ring_sum(x, axis, stride):
    count = lax.axis_size(axis)
    groups = count // stride
    total = x
    for shift in range(1, groups):
        pairs = [
            (i, (i + shift * stride) % count) for i in range(count)
        ]
        total = total + lax.ppermute(x, axis, pairs)
    return total


def pack_symmetric(c):
    h = c.shape[0] // 2
    row = jnp.arange(h)[:, None]
    col = jnp.arange(h)[None, :]
    c11, c12, c22 = c[:h, :h], c[:h, h:], c[h:, h:]
    mixed = jnp.where(col >= row, c11, c22)
    return jnp.concatenate([c12, mixed, jnp.diagonal(c22)[None, :]], axis=0)


def unpack_symmetric(p):
    h = p.shape[1]
    row = jnp.arange(h)[:, None]
    col = jnp.arange(h)[None, :]
    c12, mixed, d22 = p[:h], p[h:2 * h], p[2 * h]
    c11 = jnp.where(col >= row, mixed, mixed.T)
    c22 = jnp.where(col < row, mixed, mixed.T)
    c22 = jnp.where(col == row, d22[None, :], c22)
    top = jnp.concatenate([c11, c12], axis=1)
    bottom = jnp.concatenate([c12.T, c22], axis=1)
    return jnp.concatenate([top, bottom], axis=0)


def sweep_kernel(n, a_ref, o_ref):
    size = a_ref.shape[0]
    o_ref[...] = a_ref[...]
    rows = lax.broadcasted_iota(jnp.int32, (size, 1), 0)
    lanes = lax.broadcasted_iota(jnp.int32, (1, size), 1)
    sub8 = lax.broadcasted_iota(jnp.int32, (8, 1), 0)

    def body(k, carry):
        base = pl.multiple_of((k // 8) * 8, 8)
        slab = o_ref[pl.ds(base, 8), :]
        row = jnp.sum(jnp.where(sub8 == k - base, slab, 0.0), axis=0, keepdims=True)
        pivot = jnp.sum(jnp.where(lanes == k, row, 0.0), axis=1, keepdims=True)
        inv = 1.0 / pivot
        a = o_ref[...]
        col = jnp.sum(jnp.where(lanes == k, a, 0.0), axis=1, keepdims=True)
        u = col * inv
        scaled = row * inv
        at_row = rows == k
        at_col = lanes == k
        edge = jnp.where(at_col, jnp.where(at_row, -inv, u), scaled)
        o_ref[...] = jnp.where(at_row | at_col, edge, a - u * row)
        return carry

    lax.fori_loop(0, n, body, 0)


def spd_inverse(a):
    n = a.shape[0]
    size = -(-n // 128) * 128
    padded = jnp.eye(size, dtype=jnp.float32).at[:n, :n].set(a)
    swept = pl.pallas_call(
        functools.partial(sweep_kernel, n),
        out_shape=jax.ShapeDtypeStruct((size, size), jnp.float32),
    )(padded)
    return -swept[:n, :n]


def window_count(first, local, total):
    index = first + jnp.arange(local)
    upper = jnp.minimum(index + HALF, total - 1)
    lower = jnp.maximum(index - HALF, 0)
    return (upper - lower + 1).astype(jnp.float32)


def sum_pixels(values, width, dtype):
    weights = band_matrix(width + 2 * HALF, width, dtype)
    return jnp.einsum(
        "lqb,qp->lpb", values, weights, precision=None, preferred_element_type=jnp.float32
    )


def sum_lines(values, height, dtype, precision):
    weights = band_matrix(height + 2 * HALF, height, dtype)
    return jnp.einsum(
        "kpb,kl->lpb", values, weights, precision=precision, preferred_element_type=jnp.float32
    )


def neighbour_pairs(n_track, n_cross, dt, dc):
    pairs = []
    for t in range(n_track):
        for c in range(n_cross):
            if 0 <= t + dt < n_track and 0 <= c + dc < n_cross:
                pairs.append(((t + dt) * n_cross + c + dc, t * n_cross + c))
    return pairs


def halos(planes):
    n_track = lax.axis_size("track")
    n_cross = lax.axis_size("cross")
    both = ("track", "cross")

    def fetch(piece, dt, dc):
        if dt == 0:
            pairs = [(c + dc, c) for c in range(n_cross) if 0 <= c + dc < n_cross]
            return lax.ppermute(piece, "cross", pairs)
        if dc == 0:
            pairs = [(t + dt, t) for t in range(n_track) if 0 <= t + dt < n_track]
            return lax.ppermute(piece, "track", pairs)
        return lax.ppermute(piece, both, neighbour_pairs(n_track, n_cross, dt, dc))

    first, last = slice(0, HALF), slice(-HALF, None)
    left = fetch(planes[last], 0, -1)
    right = fetch(planes[first], 0, 1)
    parts = (left, planes, right)
    top = fetch(jnp.concatenate([p[:, :, last] for p in parts], axis=0), -1, 0)
    bottom = fetch(jnp.concatenate([p[:, :, first] for p in parts], axis=0), 1, 0)
    width = planes.shape[0]
    cuts = {"left": slice(0, HALF), "middle": slice(HALF, HALF + width), "right": slice(HALF + width, None)}
    sides = {"left": left, "right": right}
    tops = {name: top[cut] for name, cut in cuts.items()}
    bottoms = {name: bottom[cut] for name, cut in cuts.items()}
    return sides, tops, bottoms


def line_weights(lines):
    target = jnp.arange(lines)[None, :]
    middle = jnp.abs(jnp.arange(lines)[:, None] - target) <= HALF
    side = jnp.arange(HALF)[:, None]
    top = target <= side
    bottom = target >= lines - HALF + side
    return [w.astype(jnp.bfloat16) for w in (top, middle, bottom)]


def sum_lines(top, middle, bottom, weights):
    total = None
    for values, w in zip((top, middle, bottom), weights):
        term = jnp.einsum("qbk,kl->qbl", values, w, preferred_element_type=jnp.float32)
        total = term if total is None else total + term
    return total


def pixel_window_kernel(left_ref, middle_ref, right_ref, out_ref):
    refs = [(left_ref, q) for q in range(left_ref.shape[0])]
    refs += [(middle_ref, q) for q in range(middle_ref.shape[0])]
    refs += [(right_ref, q) for q in range(right_ref.shape[0])]

    def plane(q):
        ref, i = refs[q]
        return ref[i]

    span = 2 * HALF + 1
    running = plane(0)
    for q in range(1, span):
        running = running + plane(q)
    out_ref[0] = running
    for p in range(1, out_ref.shape[0]):
        running = running + plane(p + span - 1) - plane(p - 1)
        out_ref[p] = running


def sum_pixels(left, middle, right):
    width, bands, lines = middle.shape
    block = 32 if bands % 32 == 0 else bands
    spec = lambda n: pl.BlockSpec((n, block, lines), lambda i: (0, i, 0))
    return pl.pallas_call(
        pixel_window_kernel,
        grid=(bands // block,),
        in_specs=[spec(left.shape[0]), spec(width), spec(right.shape[0])],
        out_specs=spec(width),
        out_shape=jax.ShapeDtypeStruct((width, bands, lines), jnp.float32),
    )(left, middle, right)


def shards(cube):
    lines_dev, pix_dev, bands = cube.shape
    n_track = lax.axis_size("track")
    n_cross = lax.axis_size("cross")
    total_lines = lines_dev * n_track
    total_pix = pix_dev * n_cross
    highest = lax.Precision.HIGHEST
    planes = jnp.transpose(cube, (1, 2, 0))
    sides, tops, bottoms = halos(planes)
    weights = line_weights(lines_dev)
    middle = sum_lines(tops["middle"], planes, bottoms["middle"], weights)
    left = sum_lines(tops["left"], sides["left"], bottoms["left"], weights)
    right = sum_lines(tops["right"], sides["right"], bottoms["right"], weights)
    window = sum_pixels(left, middle, right)
    line_count = window_count(lax.axis_index("track") * lines_dev, lines_dev, total_lines)
    pixel_count = window_count(lax.axis_index("cross") * pix_dev, pix_dev, total_pix)
    count = pixel_count[:, None, None] * line_count[None, None, :]
    residual = planes.astype(jnp.float32) - window / count
    residual_bf = residual.astype(jnp.bfloat16)
    partial_cov = jnp.einsum(
        "pjl,pkl->jk", residual_bf, residual_bf, preferred_element_type=jnp.float32
    )
    packed = pack_symmetric(partial_cov)
    packed = packed + lax.ppermute(packed, "cross", [(i, i ^ 1) for i in range(n_cross)])
    packed = ring_sum(ring_sum(packed, "cross", 2), "track", 1)
    covariance = unpack_symmetric(packed) / (total_lines * total_pix)
    identity = jnp.eye(bands, dtype=jnp.float32)
    loaded = covariance + LOAD * (jnp.trace(covariance) / bands) * identity
    inverse = spd_inverse(loaded)
    solved = jnp.einsum(
        "pbl,bj->pjl", residual, inverse, precision=highest, preferred_element_type=jnp.float32
    )
    scores = jnp.sum(residual * solved, axis=1) / bands
    return scores.T


def solution(mesh):
    return jax.shard_map(
        shards,
        mesh=mesh,
        in_specs=(P("track", "cross", None),),
        out_specs=P("track", "cross"),
        check_vma=False,
    )
```

```python
import functools

import jax
import jax.numpy as jnp
from jax import lax
from jax.experimental import pallas as pl
from jax.experimental.layout import Layout, with_layout_constraint
from jax.sharding import PartitionSpec as P

HALF = 15


LOAD = 0.02


def with_halo(block, sides, width):
    for axis, dim in sides:
        count = lax.axis_size(axis)
        forward = [(i, i + 1) for i in range(count - 1)]
        backward = [(target, source) for source, target in forward]
        low = lax.ppermute(
            lax.slice_in_dim(block, block.shape[dim] - width, None, axis=dim), axis, forward
        )
        high = lax.ppermute(lax.slice_in_dim(block, 0, width, axis=dim), axis, backward)
        block = jnp.concatenate([low, block, high], axis=dim)
    return block


def band_matrix(rows_in, rows_out, dtype):
    source = jnp.arange(rows_in)[:, None]
    target = jnp.arange(rows_out)[None, :]
    inside = (source >= target) & (source <= target + 2 * HALF)
    return inside.astype(dtype)


def butterfly_sum(x, axis):
    count = lax.axis_size(axis)
    step = 1
    while step < count:
        pairs = [(i, i ^ step) for i in range(count)]
        x = x + lax.ppermute(x, axis, pairs)
        step *= 2
    return x


def ring_sum(x, axis, stride):
    count = lax.axis_size(axis)
    groups = count // stride
    total = x
    for shift in range(1, groups):
        pairs = [
            (i, (i + shift * stride) % count) for i in range(count)
        ]
        total = total + lax.ppermute(x, axis, pairs)
    return total


def pack_symmetric(c):
    h = c.shape[0] // 2
    row = jnp.arange(h)[:, None]
    col = jnp.arange(h)[None, :]
    c11, c12, c22 = c[:h, :h], c[:h, h:], c[h:, h:]
    mixed = jnp.where(col >= row, c11, c22)
    return jnp.concatenate([c12, mixed, jnp.diagonal(c22)[None, :]], axis=0)


def unpack_symmetric(p):
    h = p.shape[1]
    row = jnp.arange(h)[:, None]
    col = jnp.arange(h)[None, :]
    c12, mixed, d22 = p[:h], p[h:2 * h], p[2 * h]
    c11 = jnp.where(col >= row, mixed, mixed.T)
    c22 = jnp.where(col < row, mixed, mixed.T)
    c22 = jnp.where(col == row, d22[None, :], c22)
    top = jnp.concatenate([c11, c12], axis=1)
    bottom = jnp.concatenate([c12.T, c22], axis=1)
    return jnp.concatenate([top, bottom], axis=0)


def sweep_kernel(n, a_ref, o_ref):
    size = a_ref.shape[0]
    o_ref[...] = a_ref[...]
    rows = lax.broadcasted_iota(jnp.int32, (size, 1), 0)
    lanes = lax.broadcasted_iota(jnp.int32, (1, size), 1)
    sub8 = lax.broadcasted_iota(jnp.int32, (8, 1), 0)

    def body(k, carry):
        base = pl.multiple_of((k // 8) * 8, 8)
        slab = o_ref[pl.ds(base, 8), :]
        row = jnp.sum(jnp.where(sub8 == k - base, slab, 0.0), axis=0, keepdims=True)
        pivot = jnp.sum(jnp.where(lanes == k, row, 0.0), axis=1, keepdims=True)
        inv = 1.0 / pivot
        a = o_ref[...]
        col = jnp.sum(jnp.where(lanes == k, a, 0.0), axis=1, keepdims=True)
        u = col * inv
        scaled = row * inv
        at_row = rows == k
        at_col = lanes == k
        edge = jnp.where(at_col, jnp.where(at_row, -inv, u), scaled)
        o_ref[...] = jnp.where(at_row | at_col, edge, a - u * row)
        return carry

    lax.fori_loop(0, n, body, 0)


def spd_inverse(a):
    n = a.shape[0]
    size = -(-n // 128) * 128
    padded = jnp.eye(size, dtype=jnp.float32).at[:n, :n].set(a)
    swept = pl.pallas_call(
        functools.partial(sweep_kernel, n),
        out_shape=jax.ShapeDtypeStruct((size, size), jnp.float32),
    )(padded)
    return -swept[:n, :n]


def window_count(first, local, total):
    index = first + jnp.arange(local)
    upper = jnp.minimum(index + HALF, total - 1)
    lower = jnp.maximum(index - HALF, 0)
    return (upper - lower + 1).astype(jnp.float32)


def sum_pixels(values, width, dtype):
    weights = band_matrix(width + 2 * HALF, width, dtype)
    return jnp.einsum(
        "lqb,qp->lpb", values, weights, precision=None, preferred_element_type=jnp.float32
    )


def sum_lines(values, height, dtype, precision):
    weights = band_matrix(height + 2 * HALF, height, dtype)
    return jnp.einsum(
        "kpb,kl->lpb", values, weights, precision=precision, preferred_element_type=jnp.float32
    )


def neighbour_pairs(n_track, n_cross, dt, dc):
    pairs = []
    for t in range(n_track):
        for c in range(n_cross):
            if 0 <= t + dt < n_track and 0 <= c + dc < n_cross:
                pairs.append(((t + dt) * n_cross + c + dc, t * n_cross + c))
    return pairs


def halos(planes):
    n_track = lax.axis_size("track")
    n_cross = lax.axis_size("cross")
    both = ("track", "cross")

    def fetch(piece, dt, dc):
        if dt == 0:
            pairs = [(c + dc, c) for c in range(n_cross) if 0 <= c + dc < n_cross]
            return lax.ppermute(piece, "cross", pairs)
        if dc == 0:
            pairs = [(t + dt, t) for t in range(n_track) if 0 <= t + dt < n_track]
            return lax.ppermute(piece, "track", pairs)
        return lax.ppermute(piece, both, neighbour_pairs(n_track, n_cross, dt, dc))

    first, last = slice(0, HALF), slice(-HALF, None)
    sides = {
        "left": fetch(planes[last], 0, -1),
        "right": fetch(planes[first], 0, 1),
    }
    top = fetch(planes[:, :, last], -1, 0)
    bottom = fetch(planes[:, :, first], 1, 0)
    tops = {
        "left": fetch(top[last], 0, -1),
        "middle": top,
        "right": fetch(top[first], 0, 1),
    }
    bottoms = {
        "left": fetch(bottom[last], 0, -1),
        "middle": bottom,
        "right": fetch(bottom[first], 0, 1),
    }
    return sides, tops, bottoms


def line_weights(lines):
    target = jnp.arange(lines)[None, :]
    middle = jnp.abs(jnp.arange(lines)[:, None] - target) <= HALF
    side = jnp.arange(HALF)[:, None]
    top = target <= side
    bottom = target >= lines - HALF + side
    return [w.astype(jnp.bfloat16) for w in (top, middle, bottom)]


def sum_lines(top, middle, bottom, weights):
    total = None
    for values, w in zip((top, middle, bottom), weights):
        term = jnp.einsum("qbk,kl->qbl", values, w, preferred_element_type=jnp.float32)
        total = term if total is None else total + term
    return total


def pixel_window_kernel(left_ref, middle_ref, right_ref, out_ref):
    refs = [(left_ref, q) for q in range(left_ref.shape[0])]
    refs += [(middle_ref, q) for q in range(middle_ref.shape[0])]
    refs += [(right_ref, q) for q in range(right_ref.shape[0])]

    def plane(q):
        ref, i = refs[q]
        return ref[i]

    span = 2 * HALF + 1
    running = plane(0)
    for q in range(1, span):
        running = running + plane(q)
    out_ref[0] = running
    for p in range(1, out_ref.shape[0]):
        running = running + plane(p + span - 1) - plane(p - 1)
        out_ref[p] = running


def sum_pixels(left, middle, right):
    width, bands, lines = middle.shape
    block = 32 if bands % 32 == 0 else bands
    spec = lambda n: pl.BlockSpec((n, block, lines), lambda i: (0, i, 0))
    return pl.pallas_call(
        pixel_window_kernel,
        grid=(bands // block,),
        in_specs=[spec(left.shape[0]), spec(width), spec(right.shape[0])],
        out_specs=spec(width),
        out_shape=jax.ShapeDtypeStruct((width, bands, lines), jnp.float32),
    )(left, middle, right)


def shards(cube):
    lines_dev, pix_dev, bands = cube.shape
    n_track = lax.axis_size("track")
    n_cross = lax.axis_size("cross")
    total_lines = lines_dev * n_track
    total_pix = pix_dev * n_cross
    highest = lax.Precision.HIGHEST
    planes = jnp.transpose(cube, (1, 2, 0))
    sides, tops, bottoms = halos(planes)
    weights = line_weights(lines_dev)
    middle = sum_lines(tops["middle"], planes, bottoms["middle"], weights)
    left = sum_lines(tops["left"], sides["left"], bottoms["left"], weights)
    right = sum_lines(tops["right"], sides["right"], bottoms["right"], weights)
    window = sum_pixels(left, middle, right)
    line_count = window_count(lax.axis_index("track") * lines_dev, lines_dev, total_lines)
    pixel_count = window_count(lax.axis_index("cross") * pix_dev, pix_dev, total_pix)
    count = pixel_count[:, None, None] * line_count[None, None, :]
    residual = planes.astype(jnp.float32) - window / count
    residual_bf = residual.astype(jnp.bfloat16)
    partial_cov = jnp.einsum(
        "pjl,pkl->jk", residual_bf, residual_bf, preferred_element_type=jnp.float32
    )
    packed = pack_symmetric(partial_cov)
    packed = packed + lax.ppermute(packed, "cross", [(i, i ^ 1) for i in range(n_cross)])
    packed = ring_sum(ring_sum(packed, "cross", 2), "track", 1)
    covariance = unpack_symmetric(packed) / (total_lines * total_pix)
    identity = jnp.eye(bands, dtype=jnp.float32)
    loaded = covariance + LOAD * (jnp.trace(covariance) / bands) * identity
    inverse = spd_inverse(loaded)
    solved = jnp.einsum(
        "pbl,bj->pjl", residual, inverse, precision=highest, preferred_element_type=jnp.float32
    )
    scores = jnp.sum(residual * solved, axis=1) / bands
    return scores.T


def solution(mesh):
    return jax.shard_map(
        shards,
        mesh=mesh,
        in_specs=(P("track", "cross", None),),
        out_specs=P("track", "cross"),
        check_vma=False,
    )
```

```python
import functools

import jax
import jax.numpy as jnp
from jax import lax
from jax.experimental import pallas as pl
from jax.experimental.layout import Layout, with_layout_constraint
from jax.sharding import PartitionSpec as P

HALF = 15


LOAD = 0.02


def with_halo(block, sides, width):
    for axis, dim in sides:
        count = lax.axis_size(axis)
        forward = [(i, i + 1) for i in range(count - 1)]
        backward = [(target, source) for source, target in forward]
        low = lax.ppermute(
            lax.slice_in_dim(block, block.shape[dim] - width, None, axis=dim), axis, forward
        )
        high = lax.ppermute(lax.slice_in_dim(block, 0, width, axis=dim), axis, backward)
        block = jnp.concatenate([low, block, high], axis=dim)
    return block


def band_matrix(rows_in, rows_out, dtype):
    source = jnp.arange(rows_in)[:, None]
    target = jnp.arange(rows_out)[None, :]
    inside = (source >= target) & (source <= target + 2 * HALF)
    return inside.astype(dtype)


def butterfly_sum(x, axis):
    count = lax.axis_size(axis)
    step = 1
    while step < count:
        pairs = [(i, i ^ step) for i in range(count)]
        x = x + lax.ppermute(x, axis, pairs)
        step *= 2
    return x


def ring_sum(x, axis, stride):
    count = lax.axis_size(axis)
    groups = count // stride
    total = x
    for shift in range(1, groups):
        pairs = [
            (i, (i + shift * stride) % count) for i in range(count)
        ]
        total = total + lax.ppermute(x, axis, pairs)
    return total


def pack_symmetric(c):
    h = c.shape[0] // 2
    row = jnp.arange(h)[:, None]
    col = jnp.arange(h)[None, :]
    c11, c12, c22 = c[:h, :h], c[:h, h:], c[h:, h:]
    mixed = jnp.where(col >= row, c11, c22)
    return jnp.concatenate([c12, mixed, jnp.diagonal(c22)[None, :]], axis=0)


def unpack_symmetric(p):
    h = p.shape[1]
    row = jnp.arange(h)[:, None]
    col = jnp.arange(h)[None, :]
    c12, mixed, d22 = p[:h], p[h:2 * h], p[2 * h]
    c11 = jnp.where(col >= row, mixed, mixed.T)
    c22 = jnp.where(col < row, mixed, mixed.T)
    c22 = jnp.where(col == row, d22[None, :], c22)
    top = jnp.concatenate([c11, c12], axis=1)
    bottom = jnp.concatenate([c12.T, c22], axis=1)
    return jnp.concatenate([top, bottom], axis=0)


def sweep_kernel(n, a_ref, o_ref):
    size = a_ref.shape[0]
    o_ref[...] = a_ref[...]
    rows = lax.broadcasted_iota(jnp.int32, (size, 1), 0)
    lanes = lax.broadcasted_iota(jnp.int32, (1, size), 1)
    sub8 = lax.broadcasted_iota(jnp.int32, (8, 1), 0)

    def body(k, carry):
        base = pl.multiple_of((k // 8) * 8, 8)
        slab = o_ref[pl.ds(base, 8), :]
        row = jnp.sum(jnp.where(sub8 == k - base, slab, 0.0), axis=0, keepdims=True)
        pivot = jnp.sum(jnp.where(lanes == k, row, 0.0), axis=1, keepdims=True)
        inv = 1.0 / pivot
        a = o_ref[...]
        col = jnp.sum(jnp.where(lanes == k, a, 0.0), axis=1, keepdims=True)
        u = col * inv
        scaled = row * inv
        at_row = rows == k
        at_col = lanes == k
        edge = jnp.where(at_col, jnp.where(at_row, -inv, u), scaled)
        o_ref[...] = jnp.where(at_row | at_col, edge, a - u * row)
        return carry

    lax.fori_loop(0, n, body, 0)


def spd_inverse(a):
    n = a.shape[0]
    size = -(-n // 128) * 128
    padded = jnp.eye(size, dtype=jnp.float32).at[:n, :n].set(a)
    swept = pl.pallas_call(
        functools.partial(sweep_kernel, n),
        out_shape=jax.ShapeDtypeStruct((size, size), jnp.float32),
    )(padded)
    return -swept[:n, :n]


def window_count(first, local, total):
    index = first + jnp.arange(local)
    upper = jnp.minimum(index + HALF, total - 1)
    lower = jnp.maximum(index - HALF, 0)
    return (upper - lower + 1).astype(jnp.float32)


def sum_pixels(values, width, dtype):
    weights = band_matrix(width + 2 * HALF, width, dtype)
    return jnp.einsum(
        "lqb,qp->lpb", values, weights, precision=None, preferred_element_type=jnp.float32
    )


def sum_lines(values, height, dtype, precision):
    weights = band_matrix(height + 2 * HALF, height, dtype)
    return jnp.einsum(
        "kpb,kl->lpb", values, weights, precision=precision, preferred_element_type=jnp.float32
    )


def neighbour_pairs(n_track, n_cross, dt, dc):
    pairs = []
    for t in range(n_track):
        for c in range(n_cross):
            if 0 <= t + dt < n_track and 0 <= c + dc < n_cross:
                pairs.append(((t + dt) * n_cross + c + dc, t * n_cross + c))
    return pairs


def halos(planes):
    n_track = lax.axis_size("track")
    n_cross = lax.axis_size("cross")
    both = ("track", "cross")

    def fetch(piece, dt, dc):
        if dt == 0:
            pairs = [(c + dc, c) for c in range(n_cross) if 0 <= c + dc < n_cross]
            return lax.ppermute(piece, "cross", pairs)
        if dc == 0:
            pairs = [(t + dt, t) for t in range(n_track) if 0 <= t + dt < n_track]
            return lax.ppermute(piece, "track", pairs)
        return lax.ppermute(piece, both, neighbour_pairs(n_track, n_cross, dt, dc))

    first, last = slice(0, HALF), slice(-HALF, None)
    sides = {
        "left": fetch(planes[last], 0, -1),
        "right": fetch(planes[first], 0, 1),
    }
    top = fetch(planes[:, :, last], -1, 0)
    bottom = fetch(planes[:, :, first], 1, 0)
    tops = {
        "left": fetch(top[last], 0, -1),
        "middle": top,
        "right": fetch(top[first], 0, 1),
    }
    bottoms = {
        "left": fetch(bottom[last], 0, -1),
        "middle": bottom,
        "right": fetch(bottom[first], 0, 1),
    }
    return sides, tops, bottoms


def line_weights(lines):
    target = jnp.arange(lines)[None, :]
    middle = jnp.abs(jnp.arange(lines)[:, None] - target) <= HALF
    side = jnp.arange(HALF)[:, None]
    top = target <= side
    bottom = target >= lines - HALF + side
    return [w.astype(jnp.bfloat16) for w in (top, middle, bottom)]


def sum_lines(top, middle, bottom, weights):
    total = None
    for values, w in zip((top, middle, bottom), weights):
        term = jnp.einsum("qbk,kl->qbl", values, w, preferred_element_type=jnp.float32)
        total = term if total is None else total + term
    return total


def residual_kernel(left_ref, middle_ref, right_ref, x_ref, count_ref, out_ref, out_bf_ref):
    refs = [(left_ref, q) for q in range(left_ref.shape[0])]
    refs += [(middle_ref, q) for q in range(middle_ref.shape[0])]
    refs += [(right_ref, q) for q in range(right_ref.shape[0])]

    def plane(q):
        ref, i = refs[q]
        return ref[i]

    def emit(p, running):
        value = x_ref[p].astype(jnp.float32) - running / count_ref[p]
        out_ref[p] = value
        out_bf_ref[p] = value.astype(jnp.bfloat16)

    span = 2 * HALF + 1
    running = plane(0)
    for q in range(1, span):
        running = running + plane(q)
    emit(0, running)
    for p in range(1, out_ref.shape[0]):
        running = running + plane(p + span - 1) - plane(p - 1)
        emit(p, running)


def residuals(left, middle, right, planes, count):
    width, bands, lines = middle.shape
    block = 32 if bands % 32 == 0 else bands
    spec = lambda n: pl.BlockSpec((n, block, lines), lambda i: (0, i, 0))
    count_spec = pl.BlockSpec((width, 1, lines), lambda i: (0, 0, 0))
    return pl.pallas_call(
        residual_kernel,
        grid=(bands // block,),
        in_specs=[spec(left.shape[0]), spec(width), spec(right.shape[0]), spec(width), count_spec],
        out_specs=[spec(width), spec(width)],
        out_shape=[
            jax.ShapeDtypeStruct((width, bands, lines), jnp.float32),
            jax.ShapeDtypeStruct((width, bands, lines), jnp.bfloat16),
        ],
    )(left, middle, right, planes, count)


def shards(cube):
    lines_dev, pix_dev, bands = cube.shape
    n_track = lax.axis_size("track")
    n_cross = lax.axis_size("cross")
    total_lines = lines_dev * n_track
    total_pix = pix_dev * n_cross
    highest = lax.Precision.HIGHEST
    planes = jnp.transpose(cube, (1, 2, 0))
    sides, tops, bottoms = halos(planes)
    weights = line_weights(lines_dev)
    middle = sum_lines(tops["middle"], planes, bottoms["middle"], weights)
    left = sum_lines(tops["left"], sides["left"], bottoms["left"], weights)
    right = sum_lines(tops["right"], sides["right"], bottoms["right"], weights)
    line_count = window_count(lax.axis_index("track") * lines_dev, lines_dev, total_lines)
    pixel_count = window_count(lax.axis_index("cross") * pix_dev, pix_dev, total_pix)
    count = pixel_count[:, None, None] * line_count[None, None, :]
    residual, residual_bf = residuals(left, middle, right, planes, count)
    partial_cov = jnp.einsum(
        "pjl,pkl->jk", residual_bf, residual_bf, preferred_element_type=jnp.float32
    )
    packed = pack_symmetric(partial_cov)
    packed = packed + lax.ppermute(packed, "cross", [(i, i ^ 1) for i in range(n_cross)])
    packed = ring_sum(ring_sum(packed, "cross", 2), "track", 1)
    covariance = unpack_symmetric(packed) / (total_lines * total_pix)
    identity = jnp.eye(bands, dtype=jnp.float32)
    loaded = covariance + LOAD * (jnp.trace(covariance) / bands) * identity
    inverse = spd_inverse(loaded)
    solved = jnp.einsum(
        "pbl,bj->pjl", residual, inverse, precision=highest, preferred_element_type=jnp.float32
    )
    scores = jnp.sum(residual * solved, axis=1) / bands
    return scores.T


def solution(mesh):
    return jax.shard_map(
        shards,
        mesh=mesh,
        in_specs=(P("track", "cross", None),),
        out_specs=P("track", "cross"),
        check_vma=False,
    )
```

```python
import functools

import jax
import jax.numpy as jnp
from jax import lax
from jax.experimental import pallas as pl
from jax.experimental.layout import Layout, with_layout_constraint
from jax.sharding import PartitionSpec as P

HALF = 15


LOAD = 0.02


def with_halo(block, sides, width):
    for axis, dim in sides:
        count = lax.axis_size(axis)
        forward = [(i, i + 1) for i in range(count - 1)]
        backward = [(target, source) for source, target in forward]
        low = lax.ppermute(
            lax.slice_in_dim(block, block.shape[dim] - width, None, axis=dim), axis, forward
        )
        high = lax.ppermute(lax.slice_in_dim(block, 0, width, axis=dim), axis, backward)
        block = jnp.concatenate([low, block, high], axis=dim)
    return block


def band_matrix(rows_in, rows_out, dtype):
    source = jnp.arange(rows_in)[:, None]
    target = jnp.arange(rows_out)[None, :]
    inside = (source >= target) & (source <= target + 2 * HALF)
    return inside.astype(dtype)


def butterfly_sum(x, axis):
    count = lax.axis_size(axis)
    step = 1
    while step < count:
        pairs = [(i, i ^ step) for i in range(count)]
        x = x + lax.ppermute(x, axis, pairs)
        step *= 2
    return x


def ring_sum(x, axis, stride):
    count = lax.axis_size(axis)
    groups = count // stride
    total = x
    for shift in range(1, groups):
        pairs = [
            (i, (i + shift * stride) % count) for i in range(count)
        ]
        total = total + lax.ppermute(x, axis, pairs)
    return total


def pack_symmetric(c):
    h = c.shape[0] // 2
    row = jnp.arange(h)[:, None]
    col = jnp.arange(h)[None, :]
    c11, c12, c22 = c[:h, :h], c[:h, h:], c[h:, h:]
    mixed = jnp.where(col >= row, c11, c22)
    return jnp.concatenate([c12, mixed, jnp.diagonal(c22)[None, :]], axis=0)


def unpack_symmetric(p):
    h = p.shape[1]
    row = jnp.arange(h)[:, None]
    col = jnp.arange(h)[None, :]
    c12, mixed, d22 = p[:h], p[h:2 * h], p[2 * h]
    c11 = jnp.where(col >= row, mixed, mixed.T)
    c22 = jnp.where(col < row, mixed, mixed.T)
    c22 = jnp.where(col == row, d22[None, :], c22)
    top = jnp.concatenate([c11, c12], axis=1)
    bottom = jnp.concatenate([c12.T, c22], axis=1)
    return jnp.concatenate([top, bottom], axis=0)


def sweep_kernel(n, a_ref, o_ref):
    size = a_ref.shape[0]
    o_ref[...] = a_ref[...]
    rows = lax.broadcasted_iota(jnp.int32, (size, 1), 0)
    lanes = lax.broadcasted_iota(jnp.int32, (1, size), 1)
    sub8 = lax.broadcasted_iota(jnp.int32, (8, 1), 0)

    def body(k, carry):
        base = pl.multiple_of((k // 8) * 8, 8)
        slab = o_ref[pl.ds(base, 8), :]
        row = jnp.sum(jnp.where(sub8 == k - base, slab, 0.0), axis=0, keepdims=True)
        pivot = jnp.sum(jnp.where(lanes == k, row, 0.0), axis=1, keepdims=True)
        inv = 1.0 / pivot
        a = o_ref[...]
        col = jnp.sum(jnp.where(lanes == k, a, 0.0), axis=1, keepdims=True)
        u = col * inv
        scaled = row * inv
        at_row = rows == k
        at_col = lanes == k
        edge = jnp.where(at_col, jnp.where(at_row, -inv, u), scaled)
        o_ref[...] = jnp.where(at_row | at_col, edge, a - u * row)
        return carry

    lax.fori_loop(0, n, body, 0)


def spd_inverse(a):
    n = a.shape[0]
    size = -(-n // 128) * 128
    padded = jnp.eye(size, dtype=jnp.float32).at[:n, :n].set(a)
    swept = pl.pallas_call(
        functools.partial(sweep_kernel, n),
        out_shape=jax.ShapeDtypeStruct((size, size), jnp.float32),
    )(padded)
    return -swept[:n, :n]


def window_count(first, local, total):
    index = first + jnp.arange(local)
    upper = jnp.minimum(index + HALF, total - 1)
    lower = jnp.maximum(index - HALF, 0)
    return (upper - lower + 1).astype(jnp.float32)


def sum_pixels(values, width, dtype):
    weights = band_matrix(width + 2 * HALF, width, dtype)
    return jnp.einsum(
        "lqb,qp->lpb", values, weights, precision=None, preferred_element_type=jnp.float32
    )


def sum_lines(values, height, dtype, precision):
    weights = band_matrix(height + 2 * HALF, height, dtype)
    return jnp.einsum(
        "kpb,kl->lpb", values, weights, precision=precision, preferred_element_type=jnp.float32
    )


def neighbour_pairs(n_track, n_cross, dt, dc):
    pairs = []
    for t in range(n_track):
        for c in range(n_cross):
            if 0 <= t + dt < n_track and 0 <= c + dc < n_cross:
                pairs.append(((t + dt) * n_cross + c + dc, t * n_cross + c))
    return pairs


def halos(planes):
    n_track = lax.axis_size("track")
    n_cross = lax.axis_size("cross")
    both = ("track", "cross")

    def fetch(piece, dt, dc):
        if dt == 0:
            pairs = [(c + dc, c) for c in range(n_cross) if 0 <= c + dc < n_cross]
            return lax.ppermute(piece, "cross", pairs)
        if dc == 0:
            pairs = [(t + dt, t) for t in range(n_track) if 0 <= t + dt < n_track]
            return lax.ppermute(piece, "track", pairs)
        return lax.ppermute(piece, both, neighbour_pairs(n_track, n_cross, dt, dc))

    first, last = slice(0, HALF), slice(-HALF, None)
    sides = {
        "left": fetch(planes[last], 0, -1),
        "right": fetch(planes[first], 0, 1),
    }
    tile = min(128, planes.shape[2])
    top = fetch(planes[:, :, -tile:], -1, 0)
    bottom = fetch(planes[:, :, :tile], 1, 0)
    tops = {
        "left": fetch(top[last][:, :, last], 0, -1),
        "middle": top,
        "right": fetch(top[first][:, :, last], 0, 1),
    }
    bottoms = {
        "left": fetch(bottom[last][:, :, first], 0, -1),
        "middle": bottom,
        "right": fetch(bottom[first][:, :, first], 0, 1),
    }
    return sides, tops, bottoms


def line_weights(lines, rows):
    target = jnp.arange(lines)[None, :]
    middle = jnp.abs(jnp.arange(lines)[:, None] - target) <= HALF
    side = jnp.arange(rows)[:, None]
    top = side >= target + rows - HALF
    bottom = side <= target + HALF - lines
    return [w.astype(jnp.bfloat16) for w in (top, middle, bottom)]


def sum_lines(top, middle, bottom, weights):
    total = None
    for values, w in zip((top, middle, bottom), weights):
        term = jnp.einsum("qbk,kl->qbl", values, w, preferred_element_type=jnp.float32)
        total = term if total is None else total + term
    return total


def residual_kernel(left_ref, middle_ref, right_ref, x_ref, count_ref, out_ref, out_bf_ref):
    refs = [(left_ref, q) for q in range(left_ref.shape[0])]
    refs += [(middle_ref, q) for q in range(middle_ref.shape[0])]
    refs += [(right_ref, q) for q in range(right_ref.shape[0])]

    def plane(q):
        ref, i = refs[q]
        return ref[i]

    def emit(p, running):
        value = x_ref[p].astype(jnp.float32) - running / count_ref[p]
        out_ref[p] = value
        out_bf_ref[p] = value.astype(jnp.bfloat16)

    span = 2 * HALF + 1
    running = plane(0)
    for q in range(1, span):
        running = running + plane(q)
    emit(0, running)
    for p in range(1, out_ref.shape[0]):
        running = running + plane(p + span - 1) - plane(p - 1)
        emit(p, running)


def residuals(left, middle, right, planes, count):
    width, bands, lines = middle.shape
    block = 32 if bands % 32 == 0 else bands
    spec = lambda n: pl.BlockSpec((n, block, lines), lambda i: (0, i, 0))
    count_spec = pl.BlockSpec((width, 1, lines), lambda i: (0, 0, 0))
    return pl.pallas_call(
        residual_kernel,
        grid=(bands // block,),
        in_specs=[spec(left.shape[0]), spec(width), spec(right.shape[0]), spec(width), count_spec],
        out_specs=[spec(width), spec(width)],
        out_shape=[
            jax.ShapeDtypeStruct((width, bands, lines), jnp.float32),
            jax.ShapeDtypeStruct((width, bands, lines), jnp.bfloat16),
        ],
    )(left, middle, right, planes, count)


def shards(cube):
    lines_dev, pix_dev, bands = cube.shape
    n_track = lax.axis_size("track")
    n_cross = lax.axis_size("cross")
    total_lines = lines_dev * n_track
    total_pix = pix_dev * n_cross
    highest = lax.Precision.HIGHEST
    planes = jnp.transpose(cube, (1, 2, 0))
    sides, tops, bottoms = halos(planes)
    wide = line_weights(lines_dev, tops["middle"].shape[2])
    narrow = line_weights(lines_dev, HALF)
    middle = sum_lines(tops["middle"], planes, bottoms["middle"], wide)
    left = sum_lines(tops["left"], sides["left"], bottoms["left"], narrow)
    right = sum_lines(tops["right"], sides["right"], bottoms["right"], narrow)
    line_count = window_count(lax.axis_index("track") * lines_dev, lines_dev, total_lines)
    pixel_count = window_count(lax.axis_index("cross") * pix_dev, pix_dev, total_pix)
    count = pixel_count[:, None, None] * line_count[None, None, :]
    residual, residual_bf = residuals(left, middle, right, planes, count)
    partial_cov = jnp.einsum(
        "pjl,pkl->jk", residual_bf, residual_bf, preferred_element_type=jnp.float32
    )
    packed = pack_symmetric(partial_cov)
    packed = packed + lax.ppermute(packed, "cross", [(i, i ^ 1) for i in range(n_cross)])
    packed = ring_sum(ring_sum(packed, "cross", 2), "track", 1)
    covariance = unpack_symmetric(packed) / (total_lines * total_pix)
    identity = jnp.eye(bands, dtype=jnp.float32)
    loaded = covariance + LOAD * (jnp.trace(covariance) / bands) * identity
    inverse = spd_inverse(loaded)
    solved = jnp.einsum(
        "pbl,bj->pjl", residual, inverse, precision=highest, preferred_element_type=jnp.float32
    )
    scores = jnp.sum(residual * solved, axis=1) / bands
    return scores.T


def solution(mesh):
    return jax.shard_map(
        shards,
        mesh=mesh,
        in_specs=(P("track", "cross", None),),
        out_specs=P("track", "cross"),
        check_vma=False,
    )
```

```python
import functools

import jax
import jax.numpy as jnp
from jax import lax
from jax.experimental import pallas as pl
from jax.experimental.layout import Layout, with_layout_constraint
from jax.sharding import PartitionSpec as P

HALF = 15


LOAD = 0.02


def with_halo(block, sides, width):
    for axis, dim in sides:
        count = lax.axis_size(axis)
        forward = [(i, i + 1) for i in range(count - 1)]
        backward = [(target, source) for source, target in forward]
        low = lax.ppermute(
            lax.slice_in_dim(block, block.shape[dim] - width, None, axis=dim), axis, forward
        )
        high = lax.ppermute(lax.slice_in_dim(block, 0, width, axis=dim), axis, backward)
        block = jnp.concatenate([low, block, high], axis=dim)
    return block


def band_matrix(rows_in, rows_out, dtype):
    source = jnp.arange(rows_in)[:, None]
    target = jnp.arange(rows_out)[None, :]
    inside = (source >= target) & (source <= target + 2 * HALF)
    return inside.astype(dtype)


def butterfly_sum(x, axis):
    count = lax.axis_size(axis)
    step = 1
    while step < count:
        pairs = [(i, i ^ step) for i in range(count)]
        x = x + lax.ppermute(x, axis, pairs)
        step *= 2
    return x


def ring_sum(x, axis, stride):
    count = lax.axis_size(axis)
    groups = count // stride
    total = x
    for shift in range(1, groups):
        pairs = [
            (i, (i + shift * stride) % count) for i in range(count)
        ]
        total = total + lax.ppermute(x, axis, pairs)
    return total


def pack_symmetric(c):
    h = c.shape[0] // 2
    row = jnp.arange(h)[:, None]
    col = jnp.arange(h)[None, :]
    c11, c12, c22 = c[:h, :h], c[:h, h:], c[h:, h:]
    mixed = jnp.where(col >= row, c11, c22)
    return jnp.concatenate([c12, mixed, jnp.diagonal(c22)[None, :]], axis=0)


def unpack_symmetric(p):
    h = p.shape[1]
    row = jnp.arange(h)[:, None]
    col = jnp.arange(h)[None, :]
    c12, mixed, d22 = p[:h], p[h:2 * h], p[2 * h]
    c11 = jnp.where(col >= row, mixed, mixed.T)
    c22 = jnp.where(col < row, mixed, mixed.T)
    c22 = jnp.where(col == row, d22[None, :], c22)
    top = jnp.concatenate([c11, c12], axis=1)
    bottom = jnp.concatenate([c12.T, c22], axis=1)
    return jnp.concatenate([top, bottom], axis=0)


def sweep_kernel(n, a_ref, o_ref):
    size = a_ref.shape[0]
    o_ref[...] = a_ref[...]
    rows = lax.broadcasted_iota(jnp.int32, (size, 1), 0)
    lanes = lax.broadcasted_iota(jnp.int32, (1, size), 1)
    sub8 = lax.broadcasted_iota(jnp.int32, (8, 1), 0)

    def pick(v, j):
        return jnp.sum(jnp.where(lanes == j, v, 0.0), axis=1, keepdims=True)

    def body(m, carry):
        k = 2 * m
        base = pl.multiple_of((k // 8) * 8, 8)
        slab = o_ref[pl.ds(base, 8), :]
        r0 = jnp.sum(jnp.where(sub8 == k - base, slab, 0.0), axis=0, keepdims=True)
        r1 = jnp.sum(jnp.where(sub8 == k + 1 - base, slab, 0.0), axis=0, keepdims=True)
        a00, a01, a11 = pick(r0, k), pick(r0, k + 1), pick(r1, k + 1)
        det = a00 * a11 - a01 * a01
        p00, p01, p11 = a11 / det, -a01 / det, a00 / det
        a = o_ref[...]
        c0 = jnp.sum(jnp.where(lanes == k, a, 0.0), axis=1, keepdims=True)
        c1 = jnp.sum(jnp.where(lanes == k + 1, a, 0.0), axis=1, keepdims=True)
        u0 = c0 * p00 + c1 * p01
        u1 = c0 * p01 + c1 * p11
        s0 = r0 * p00 + r1 * p01
        s1 = r0 * p01 + r1 * p11
        main = a - u0 * r0 - u1 * r1
        row0, row1 = rows == k, rows == k + 1
        col0, col1 = lanes == k, lanes == k + 1
        in_rows = row0 | row1
        in_cols = col0 | col1
        corner = jnp.where(row0, jnp.where(col0, -p00, -p01), jnp.where(col0, -p01, -p11))
        side_cols = jnp.where(col0, u0, u1)
        side_rows = jnp.where(row0, s0, s1)
        edge = jnp.where(in_rows, jnp.where(in_cols, corner, side_rows), side_cols)
        o_ref[...] = jnp.where(in_rows | in_cols, edge, main)
        return carry

    lax.fori_loop(0, n // 2, body, 0)


def spd_inverse(a):
    n = a.shape[0]
    assert n % 2 == 0
    size = -(-n // 128) * 128
    padded = jnp.eye(size, dtype=jnp.float32).at[:n, :n].set(a)
    swept = pl.pallas_call(
        functools.partial(sweep_kernel, n),
        out_shape=jax.ShapeDtypeStruct((size, size), jnp.float32),
    )(padded)
    return -swept[:n, :n]


def window_count(first, local, total):
    index = first + jnp.arange(local)
    upper = jnp.minimum(index + HALF, total - 1)
    lower = jnp.maximum(index - HALF, 0)
    return (upper - lower + 1).astype(jnp.float32)


def sum_pixels(values, width, dtype):
    weights = band_matrix(width + 2 * HALF, width, dtype)
    return jnp.einsum(
        "lqb,qp->lpb", values, weights, precision=None, preferred_element_type=jnp.float32
    )


def sum_lines(values, height, dtype, precision):
    weights = band_matrix(height + 2 * HALF, height, dtype)
    return jnp.einsum(
        "kpb,kl->lpb", values, weights, precision=precision, preferred_element_type=jnp.float32
    )


def neighbour_pairs(n_track, n_cross, dt, dc):
    pairs = []
    for t in range(n_track):
        for c in range(n_cross):
            if 0 <= t + dt < n_track and 0 <= c + dc < n_cross:
                pairs.append(((t + dt) * n_cross + c + dc, t * n_cross + c))
    return pairs


def halos(planes):
    n_track = lax.axis_size("track")
    n_cross = lax.axis_size("cross")
    both = ("track", "cross")

    def fetch(piece, dt, dc):
        if dt == 0:
            pairs = [(c + dc, c) for c in range(n_cross) if 0 <= c + dc < n_cross]
            return lax.ppermute(piece, "cross", pairs)
        if dc == 0:
            pairs = [(t + dt, t) for t in range(n_track) if 0 <= t + dt < n_track]
            return lax.ppermute(piece, "track", pairs)
        return lax.ppermute(piece, both, neighbour_pairs(n_track, n_cross, dt, dc))

    first, last = slice(0, HALF), slice(-HALF, None)
    sides = {
        "left": fetch(planes[last], 0, -1),
        "right": fetch(planes[first], 0, 1),
    }
    top = fetch(planes[:, :, last], -1, 0)
    bottom = fetch(planes[:, :, first], 1, 0)
    tops = {
        "left": fetch(top[last], 0, -1),
        "middle": top,
        "right": fetch(top[first], 0, 1),
    }
    bottoms = {
        "left": fetch(bottom[last], 0, -1),
        "middle": bottom,
        "right": fetch(bottom[first], 0, 1),
    }
    return sides, tops, bottoms


def line_weights(lines):
    target = jnp.arange(lines)[None, :]
    middle = jnp.abs(jnp.arange(lines)[:, None] - target) <= HALF
    side = jnp.arange(HALF)[:, None]
    top = target <= side
    bottom = target >= lines - HALF + side
    return [w.astype(jnp.bfloat16) for w in (top, middle, bottom)]


def sum_lines(top, middle, bottom, weights):
    total = None
    for values, w in zip((top, middle, bottom), weights):
        term = jnp.einsum("qbk,kl->qbl", values, w, preferred_element_type=jnp.float32)
        total = term if total is None else total + term
    return total


def residual_kernel(left_ref, middle_ref, right_ref, x_ref, count_ref, out_ref, out_bf_ref):
    refs = [(left_ref, q) for q in range(left_ref.shape[0])]
    refs += [(middle_ref, q) for q in range(middle_ref.shape[0])]
    refs += [(right_ref, q) for q in range(right_ref.shape[0])]

    def plane(q):
        ref, i = refs[q]
        return ref[i]

    def emit(p, running):
        value = x_ref[p].astype(jnp.float32) - running / count_ref[p]
        out_ref[p] = value
        out_bf_ref[p] = value.astype(jnp.bfloat16)

    span = 2 * HALF + 1
    running = plane(0)
    for q in range(1, span):
        running = running + plane(q)
    emit(0, running)
    for p in range(1, out_ref.shape[0]):
        running = running + plane(p + span - 1) - plane(p - 1)
        emit(p, running)


def residuals(left, middle, right, planes, count):
    width, bands, lines = middle.shape
    block = 32 if bands % 32 == 0 else bands
    spec = lambda n: pl.BlockSpec((n, block, lines), lambda i: (0, i, 0))
    count_spec = pl.BlockSpec((width, 1, lines), lambda i: (0, 0, 0))
    return pl.pallas_call(
        residual_kernel,
        grid=(bands // block,),
        in_specs=[spec(left.shape[0]), spec(width), spec(right.shape[0]), spec(width), count_spec],
        out_specs=[spec(width), spec(width)],
        out_shape=[
            jax.ShapeDtypeStruct((width, bands, lines), jnp.float32),
            jax.ShapeDtypeStruct((width, bands, lines), jnp.bfloat16),
        ],
    )(left, middle, right, planes, count)


def shards(cube):
    lines_dev, pix_dev, bands = cube.shape
    n_track = lax.axis_size("track")
    n_cross = lax.axis_size("cross")
    total_lines = lines_dev * n_track
    total_pix = pix_dev * n_cross
    highest = lax.Precision.HIGHEST
    planes = jnp.transpose(cube, (1, 2, 0))
    sides, tops, bottoms = halos(planes)
    weights = line_weights(lines_dev)
    middle = sum_lines(tops["middle"], planes, bottoms["middle"], weights)
    left = sum_lines(tops["left"], sides["left"], bottoms["left"], weights)
    right = sum_lines(tops["right"], sides["right"], bottoms["right"], weights)
    line_count = window_count(lax.axis_index("track") * lines_dev, lines_dev, total_lines)
    pixel_count = window_count(lax.axis_index("cross") * pix_dev, pix_dev, total_pix)
    count = pixel_count[:, None, None] * line_count[None, None, :]
    residual, residual_bf = residuals(left, middle, right, planes, count)
    partial_cov = jnp.einsum(
        "pjl,pkl->jk", residual_bf, residual_bf, preferred_element_type=jnp.float32
    )
    packed = pack_symmetric(partial_cov)
    packed = packed + lax.ppermute(packed, "cross", [(i, i ^ 1) for i in range(n_cross)])
    packed = ring_sum(ring_sum(packed, "cross", 2), "track", 1)
    covariance = unpack_symmetric(packed) / (total_lines * total_pix)
    identity = jnp.eye(bands, dtype=jnp.float32)
    loaded = covariance + LOAD * (jnp.trace(covariance) / bands) * identity
    inverse = spd_inverse(loaded)
    solved = jnp.einsum(
        "pbl,bj->pjl", residual, inverse, precision=highest, preferred_element_type=jnp.float32
    )
    scores = jnp.sum(residual * solved, axis=1) / bands
    return scores.T


def solution(mesh):
    return jax.shard_map(
        shards,
        mesh=mesh,
        in_specs=(P("track", "cross", None),),
        out_specs=P("track", "cross"),
        check_vma=False,
    )
```

```python
import functools

import jax
import jax.numpy as jnp
from jax import lax
from jax.experimental import pallas as pl
from jax.experimental.layout import Layout, with_layout_constraint
from jax.sharding import PartitionSpec as P

HALF = 15


LOAD = 0.02


def with_halo(block, sides, width):
    for axis, dim in sides:
        count = lax.axis_size(axis)
        forward = [(i, i + 1) for i in range(count - 1)]
        backward = [(target, source) for source, target in forward]
        low = lax.ppermute(
            lax.slice_in_dim(block, block.shape[dim] - width, None, axis=dim), axis, forward
        )
        high = lax.ppermute(lax.slice_in_dim(block, 0, width, axis=dim), axis, backward)
        block = jnp.concatenate([low, block, high], axis=dim)
    return block


def band_matrix(rows_in, rows_out, dtype):
    source = jnp.arange(rows_in)[:, None]
    target = jnp.arange(rows_out)[None, :]
    inside = (source >= target) & (source <= target + 2 * HALF)
    return inside.astype(dtype)


def butterfly_sum(x, axis):
    count = lax.axis_size(axis)
    step = 1
    while step < count:
        pairs = [(i, i ^ step) for i in range(count)]
        x = x + lax.ppermute(x, axis, pairs)
        step *= 2
    return x


def ring_sum(x, axis, stride):
    count = lax.axis_size(axis)
    groups = count // stride
    total = x
    for shift in range(1, groups):
        pairs = [
            (i, (i + shift * stride) % count) for i in range(count)
        ]
        total = total + lax.ppermute(x, axis, pairs)
    return total


def pack_symmetric(c):
    h = c.shape[0] // 2
    row = jnp.arange(h)[:, None]
    col = jnp.arange(h)[None, :]
    c11, c12, c22 = c[:h, :h], c[:h, h:], c[h:, h:]
    mixed = jnp.where(col >= row, c11, c22)
    return jnp.concatenate([c12, mixed, jnp.diagonal(c22)[None, :]], axis=0)


def unpack_symmetric(p):
    h = p.shape[1]
    row = jnp.arange(h)[:, None]
    col = jnp.arange(h)[None, :]
    c12, mixed, d22 = p[:h], p[h:2 * h], p[2 * h]
    c11 = jnp.where(col >= row, mixed, mixed.T)
    c22 = jnp.where(col < row, mixed, mixed.T)
    c22 = jnp.where(col == row, d22[None, :], c22)
    top = jnp.concatenate([c11, c12], axis=1)
    bottom = jnp.concatenate([c12.T, c22], axis=1)
    return jnp.concatenate([top, bottom], axis=0)


def sweep_kernel(n, a_ref, o_ref):
    size = o_ref.shape[0]
    rows = lax.broadcasted_iota(jnp.int32, (size, 1), 0)
    lanes = lax.broadcasted_iota(jnp.int32, (1, size), 1)
    o_ref[...] = jnp.where(rows == lanes, 1.0, 0.0).astype(jnp.float32)
    o_ref[:n, :n] = a_ref[...]
    sub8 = lax.broadcasted_iota(jnp.int32, (8, 1), 0)

    def pick(v, j):
        return jnp.sum(jnp.where(lanes == j, v, 0.0), axis=1, keepdims=True)

    def body(m, carry):
        k = 2 * m
        base = pl.multiple_of((k // 8) * 8, 8)
        slab = o_ref[pl.ds(base, 8), :]
        r0 = jnp.sum(jnp.where(sub8 == k - base, slab, 0.0), axis=0, keepdims=True)
        r1 = jnp.sum(jnp.where(sub8 == k + 1 - base, slab, 0.0), axis=0, keepdims=True)
        a00, a01, a11 = pick(r0, k), pick(r0, k + 1), pick(r1, k + 1)
        det = a00 * a11 - a01 * a01
        p00, p01, p11 = a11 / det, -a01 / det, a00 / det
        a = o_ref[...]
        c0 = jnp.sum(jnp.where(lanes == k, a, 0.0), axis=1, keepdims=True)
        c1 = jnp.sum(jnp.where(lanes == k + 1, a, 0.0), axis=1, keepdims=True)
        u0 = c0 * p00 + c1 * p01
        u1 = c0 * p01 + c1 * p11
        s0 = r0 * p00 + r1 * p01
        s1 = r0 * p01 + r1 * p11
        main = a - u0 * r0 - u1 * r1
        row0, row1 = rows == k, rows == k + 1
        col0, col1 = lanes == k, lanes == k + 1
        in_rows = row0 | row1
        in_cols = col0 | col1
        corner = jnp.where(row0, jnp.where(col0, -p00, -p01), jnp.where(col0, -p01, -p11))
        side_cols = jnp.where(col0, u0, u1)
        side_rows = jnp.where(row0, s0, s1)
        edge = jnp.where(in_rows, jnp.where(in_cols, corner, side_rows), side_cols)
        o_ref[...] = jnp.where(in_rows | in_cols, edge, main)
        return carry

    lax.fori_loop(0, n // 2, body, 0)


def spd_inverse(a):
    n = a.shape[0]
    assert n % 2 == 0
    size = -(-n // 128) * 128
    swept = pl.pallas_call(
        functools.partial(sweep_kernel, n),
        out_shape=jax.ShapeDtypeStruct((size, size), jnp.float32),
    )(a)
    return -swept[:n, :n]


def window_count(first, local, total):
    index = first + jnp.arange(local)
    upper = jnp.minimum(index + HALF, total - 1)
    lower = jnp.maximum(index - HALF, 0)
    return (upper - lower + 1).astype(jnp.float32)


def sum_pixels(values, width, dtype):
    weights = band_matrix(width + 2 * HALF, width, dtype)
    return jnp.einsum(
        "lqb,qp->lpb", values, weights, precision=None, preferred_element_type=jnp.float32
    )


def sum_lines(values, height, dtype, precision):
    weights = band_matrix(height + 2 * HALF, height, dtype)
    return jnp.einsum(
        "kpb,kl->lpb", values, weights, precision=precision, preferred_element_type=jnp.float32
    )


def neighbour_pairs(n_track, n_cross, dt, dc):
    pairs = []
    for t in range(n_track):
        for c in range(n_cross):
            if 0 <= t + dt < n_track and 0 <= c + dc < n_cross:
                pairs.append(((t + dt) * n_cross + c + dc, t * n_cross + c))
    return pairs


def halos(planes):
    n_track = lax.axis_size("track")
    n_cross = lax.axis_size("cross")
    both = ("track", "cross")

    def fetch(piece, dt, dc):
        if dt == 0:
            pairs = [(c + dc, c) for c in range(n_cross) if 0 <= c + dc < n_cross]
            return lax.ppermute(piece, "cross", pairs)
        if dc == 0:
            pairs = [(t + dt, t) for t in range(n_track) if 0 <= t + dt < n_track]
            return lax.ppermute(piece, "track", pairs)
        return lax.ppermute(piece, both, neighbour_pairs(n_track, n_cross, dt, dc))

    first, last = slice(0, HALF), slice(-HALF, None)
    sides = {
        "left": fetch(planes[last], 0, -1),
        "right": fetch(planes[first], 0, 1),
    }
    top = fetch(planes[:, :, last], -1, 0)
    bottom = fetch(planes[:, :, first], 1, 0)
    tops = {
        "left": fetch(top[last], 0, -1),
        "middle": top,
        "right": fetch(top[first], 0, 1),
    }
    bottoms = {
        "left": fetch(bottom[last], 0, -1),
        "middle": bottom,
        "right": fetch(bottom[first], 0, 1),
    }
    return sides, tops, bottoms


def line_weights(lines):
    target = jnp.arange(lines)[None, :]
    middle = jnp.abs(jnp.arange(lines)[:, None] - target) <= HALF
    side = jnp.arange(HALF)[:, None]
    top = target <= side
    bottom = target >= lines - HALF + side
    return [w.astype(jnp.bfloat16) for w in (top, middle, bottom)]


def sum_lines(top, middle, bottom, weights):
    total = None
    for values, w in zip((top, middle, bottom), weights):
        term = jnp.einsum("qbk,kl->qbl", values, w, preferred_element_type=jnp.float32)
        total = term if total is None else total + term
    return total


def residual_kernel(left_ref, middle_ref, right_ref, x_ref, count_ref, out_ref, out_bf_ref):
    refs = [(left_ref, q) for q in range(left_ref.shape[0])]
    refs += [(middle_ref, q) for q in range(middle_ref.shape[0])]
    refs += [(right_ref, q) for q in range(right_ref.shape[0])]

    def plane(q):
        ref, i = refs[q]
        return ref[i]

    def emit(p, running):
        value = x_ref[p].astype(jnp.float32) - running / count_ref[p]
        out_ref[p] = value
        out_bf_ref[p] = value.astype(jnp.bfloat16)

    span = 2 * HALF + 1
    running = plane(0)
    for q in range(1, span):
        running = running + plane(q)
    emit(0, running)
    for p in range(1, out_ref.shape[0]):
        running = running + plane(p + span - 1) - plane(p - 1)
        emit(p, running)


def residuals(left, middle, right, planes, count):
    width, bands, lines = middle.shape
    block = 32 if bands % 32 == 0 else bands
    spec = lambda n: pl.BlockSpec((n, block, lines), lambda i: (0, i, 0))
    count_spec = pl.BlockSpec((width, 1, lines), lambda i: (0, 0, 0))
    return pl.pallas_call(
        residual_kernel,
        grid=(bands // block,),
        in_specs=[spec(left.shape[0]), spec(width), spec(right.shape[0]), spec(width), count_spec],
        out_specs=[spec(width), spec(width)],
        out_shape=[
            jax.ShapeDtypeStruct((width, bands, lines), jnp.float32),
            jax.ShapeDtypeStruct((width, bands, lines), jnp.bfloat16),
        ],
    )(left, middle, right, planes, count)


def shards(cube):
    lines_dev, pix_dev, bands = cube.shape
    n_track = lax.axis_size("track")
    n_cross = lax.axis_size("cross")
    total_lines = lines_dev * n_track
    total_pix = pix_dev * n_cross
    highest = lax.Precision.HIGHEST
    planes = jnp.transpose(cube, (1, 2, 0))
    sides, tops, bottoms = halos(planes)
    weights = line_weights(lines_dev)
    middle = sum_lines(tops["middle"], planes, bottoms["middle"], weights)
    left = sum_lines(tops["left"], sides["left"], bottoms["left"], weights)
    right = sum_lines(tops["right"], sides["right"], bottoms["right"], weights)
    line_count = window_count(lax.axis_index("track") * lines_dev, lines_dev, total_lines)
    pixel_count = window_count(lax.axis_index("cross") * pix_dev, pix_dev, total_pix)
    count = pixel_count[:, None, None] * line_count[None, None, :]
    residual, residual_bf = residuals(left, middle, right, planes, count)
    partial_cov = jnp.einsum(
        "pjl,pkl->jk", residual_bf, residual_bf, preferred_element_type=jnp.float32
    )
    packed = pack_symmetric(partial_cov)
    packed = packed + lax.ppermute(packed, "cross", [(i, i ^ 1) for i in range(n_cross)])
    packed = ring_sum(ring_sum(packed, "cross", 2), "track", 1)
    covariance = unpack_symmetric(packed) / (total_lines * total_pix)
    identity = jnp.eye(bands, dtype=jnp.float32)
    loaded = covariance + LOAD * (jnp.trace(covariance) / bands) * identity
    inverse = spd_inverse(loaded)
    solved = jnp.einsum(
        "pbl,bj->pjl", residual, inverse, precision=highest, preferred_element_type=jnp.float32
    )
    scores = jnp.sum(residual * solved, axis=1) / bands
    return scores.T


def solution(mesh):
    return jax.shard_map(
        shards,
        mesh=mesh,
        in_specs=(P("track", "cross", None),),
        out_specs=P("track", "cross"),
        check_vma=False,
    )
```

```python
import functools

import jax
import jax.numpy as jnp
from jax import lax
from jax.experimental import pallas as pl
from jax.experimental.layout import Layout, with_layout_constraint
from jax.sharding import PartitionSpec as P

HALF = 15


LOAD = 0.02


def with_halo(block, sides, width):
    for axis, dim in sides:
        count = lax.axis_size(axis)
        forward = [(i, i + 1) for i in range(count - 1)]
        backward = [(target, source) for source, target in forward]
        low = lax.ppermute(
            lax.slice_in_dim(block, block.shape[dim] - width, None, axis=dim), axis, forward
        )
        high = lax.ppermute(lax.slice_in_dim(block, 0, width, axis=dim), axis, backward)
        block = jnp.concatenate([low, block, high], axis=dim)
    return block


def band_matrix(rows_in, rows_out, dtype):
    source = jnp.arange(rows_in)[:, None]
    target = jnp.arange(rows_out)[None, :]
    inside = (source >= target) & (source <= target + 2 * HALF)
    return inside.astype(dtype)


def butterfly_sum(x, axis):
    count = lax.axis_size(axis)
    step = 1
    while step < count:
        pairs = [(i, i ^ step) for i in range(count)]
        x = x + lax.ppermute(x, axis, pairs)
        step *= 2
    return x


def ring_sum(x, axis, stride):
    count = lax.axis_size(axis)
    groups = count // stride
    total = x
    for shift in range(1, groups):
        pairs = [
            (i, (i + shift * stride) % count) for i in range(count)
        ]
        total = total + lax.ppermute(x, axis, pairs)
    return total


def pack_symmetric(c):
    h = c.shape[0] // 2
    row = jnp.arange(h)[:, None]
    col = jnp.arange(h)[None, :]
    c11, c12, c22 = c[:h, :h], c[:h, h:], c[h:, h:]
    mixed = jnp.where(col >= row, c11, c22)
    return jnp.concatenate([c12, mixed, jnp.diagonal(c22)[None, :]], axis=0)


def unpack_symmetric(p):
    h = p.shape[1]
    row = jnp.arange(h)[:, None]
    col = jnp.arange(h)[None, :]
    c12, mixed, d22 = p[:h], p[h:2 * h], p[2 * h]
    c11 = jnp.where(col >= row, mixed, mixed.T)
    c22 = jnp.where(col < row, mixed, mixed.T)
    c22 = jnp.where(col == row, d22[None, :], c22)
    top = jnp.concatenate([c11, c12], axis=1)
    bottom = jnp.concatenate([c12.T, c22], axis=1)
    return jnp.concatenate([top, bottom], axis=0)


def sweep_kernel(n, a_ref, o_ref):
    size = o_ref.shape[0]
    rows = lax.broadcasted_iota(jnp.int32, (size, 1), 0)
    lanes = lax.broadcasted_iota(jnp.int32, (1, size), 1)
    o_ref[...] = jnp.where(rows == lanes, 1.0, 0.0).astype(jnp.float32)
    o_ref[:n, :n] = a_ref[...]
    sub8 = lax.broadcasted_iota(jnp.int32, (8, 1), 0)

    def pick(v, j):
        return jnp.sum(jnp.where(lanes == j, v, 0.0), axis=1, keepdims=True)

    def body(m, carry):
        k = 2 * m
        base = pl.multiple_of((k // 8) * 8, 8)
        slab = o_ref[pl.ds(base, 8), :]
        r0 = jnp.sum(jnp.where(sub8 == k - base, slab, 0.0), axis=0, keepdims=True)
        r1 = jnp.sum(jnp.where(sub8 == k + 1 - base, slab, 0.0), axis=0, keepdims=True)
        a00, a01, a11 = pick(r0, k), pick(r0, k + 1), pick(r1, k + 1)
        det = a00 * a11 - a01 * a01
        p00, p01, p11 = a11 / det, -a01 / det, a00 / det
        a = o_ref[...]
        c0 = jnp.sum(jnp.where(lanes == k, a, 0.0), axis=1, keepdims=True)
        c1 = jnp.sum(jnp.where(lanes == k + 1, a, 0.0), axis=1, keepdims=True)
        u0 = c0 * p00 + c1 * p01
        u1 = c0 * p01 + c1 * p11
        s0 = r0 * p00 + r1 * p01
        s1 = r0 * p01 + r1 * p11
        main = a - u0 * r0 - u1 * r1
        row0, row1 = rows == k, rows == k + 1
        col0, col1 = lanes == k, lanes == k + 1
        in_rows = row0 | row1
        in_cols = col0 | col1
        corner = jnp.where(row0, jnp.where(col0, -p00, -p01), jnp.where(col0, -p01, -p11))
        side_cols = jnp.where(col0, u0, u1)
        side_rows = jnp.where(row0, s0, s1)
        edge = jnp.where(in_rows, jnp.where(in_cols, corner, side_rows), side_cols)
        o_ref[...] = jnp.where(in_rows | in_cols, edge, main)
        return carry

    lax.fori_loop(0, n // 2, body, 0)


def spd_inverse(a):
    n = a.shape[0]
    assert n % 2 == 0
    size = -(-n // 128) * 128
    swept = pl.pallas_call(
        functools.partial(sweep_kernel, n),
        out_shape=jax.ShapeDtypeStruct((size, size), jnp.float32),
    )(a)
    return -swept[:n, :n]


def window_count(first, local, total):
    index = first + jnp.arange(local)
    upper = jnp.minimum(index + HALF, total - 1)
    lower = jnp.maximum(index - HALF, 0)
    return (upper - lower + 1).astype(jnp.float32)


def sum_pixels(values, width, dtype):
    weights = band_matrix(width + 2 * HALF, width, dtype)
    return jnp.einsum(
        "lqb,qp->lpb", values, weights, precision=None, preferred_element_type=jnp.float32
    )


def sum_lines(values, height, dtype, precision):
    weights = band_matrix(height + 2 * HALF, height, dtype)
    return jnp.einsum(
        "kpb,kl->lpb", values, weights, precision=precision, preferred_element_type=jnp.float32
    )


def neighbour_pairs(n_track, n_cross, dt, dc):
    pairs = []
    for t in range(n_track):
        for c in range(n_cross):
            if 0 <= t + dt < n_track and 0 <= c + dc < n_cross:
                pairs.append(((t + dt) * n_cross + c + dc, t * n_cross + c))
    return pairs


def halos(planes):
    n_track = lax.axis_size("track")
    n_cross = lax.axis_size("cross")
    both = ("track", "cross")

    def fetch(piece, dt, dc):
        if dt == 0:
            pairs = [(c + dc, c) for c in range(n_cross) if 0 <= c + dc < n_cross]
            return lax.ppermute(piece, "cross", pairs)
        if dc == 0:
            pairs = [(t + dt, t) for t in range(n_track) if 0 <= t + dt < n_track]
            return lax.ppermute(piece, "track", pairs)
        return lax.ppermute(piece, both, neighbour_pairs(n_track, n_cross, dt, dc))

    first, last = slice(0, HALF), slice(-HALF, None)
    sides = {
        "left": fetch(planes[last], 0, -1),
        "right": fetch(planes[first], 0, 1),
    }
    top = fetch(planes[:, :, last], -1, 0)
    bottom = fetch(planes[:, :, first], 1, 0)
    from_left = fetch(jnp.stack([top[last], bottom[last]]), 0, -1)
    from_right = fetch(jnp.stack([top[first], bottom[first]]), 0, 1)
    tops = {"left": from_left[0], "middle": top, "right": from_right[0]}
    bottoms = {"left": from_left[1], "middle": bottom, "right": from_right[1]}
    return sides, tops, bottoms


def line_weights(lines):
    target = jnp.arange(lines)[None, :]
    middle = jnp.abs(jnp.arange(lines)[:, None] - target) <= HALF
    side = jnp.arange(HALF)[:, None]
    top = target <= side
    bottom = target >= lines - HALF + side
    return [w.astype(jnp.bfloat16) for w in (top, middle, bottom)]


def sum_lines(top, middle, bottom, weights):
    total = None
    for values, w in zip((top, middle, bottom), weights):
        term = jnp.einsum("qbk,kl->qbl", values, w, preferred_element_type=jnp.float32)
        total = term if total is None else total + term
    return total


def residual_kernel(left_ref, middle_ref, right_ref, x_ref, count_ref, out_ref, out_bf_ref):
    refs = [(left_ref, q) for q in range(left_ref.shape[0])]
    refs += [(middle_ref, q) for q in range(middle_ref.shape[0])]
    refs += [(right_ref, q) for q in range(right_ref.shape[0])]

    def plane(q):
        ref, i = refs[q]
        return ref[i]

    def emit(p, running):
        value = x_ref[p].astype(jnp.float32) - running / count_ref[p]
        out_ref[p] = value
        out_bf_ref[p] = value.astype(jnp.bfloat16)

    span = 2 * HALF + 1
    running = plane(0)
    for q in range(1, span):
        running = running + plane(q)
    emit(0, running)
    for p in range(1, out_ref.shape[0]):
        running = running + plane(p + span - 1) - plane(p - 1)
        emit(p, running)


def residuals(left, middle, right, planes, count):
    width, bands, lines = middle.shape
    block = 32 if bands % 32 == 0 else bands
    spec = lambda n: pl.BlockSpec((n, block, lines), lambda i: (0, i, 0))
    count_spec = pl.BlockSpec((width, 1, lines), lambda i: (0, 0, 0))
    return pl.pallas_call(
        residual_kernel,
        grid=(bands // block,),
        in_specs=[spec(left.shape[0]), spec(width), spec(right.shape[0]), spec(width), count_spec],
        out_specs=[spec(width), spec(width)],
        out_shape=[
            jax.ShapeDtypeStruct((width, bands, lines), jnp.float32),
            jax.ShapeDtypeStruct((width, bands, lines), jnp.bfloat16),
        ],
    )(left, middle, right, planes, count)


def shards(cube):
    lines_dev, pix_dev, bands = cube.shape
    n_track = lax.axis_size("track")
    n_cross = lax.axis_size("cross")
    total_lines = lines_dev * n_track
    total_pix = pix_dev * n_cross
    highest = lax.Precision.HIGHEST
    planes = jnp.transpose(cube, (1, 2, 0))
    sides, tops, bottoms = halos(planes)
    weights = line_weights(lines_dev)
    middle = sum_lines(tops["middle"], planes, bottoms["middle"], weights)
    left = sum_lines(tops["left"], sides["left"], bottoms["left"], weights)
    right = sum_lines(tops["right"], sides["right"], bottoms["right"], weights)
    line_count = window_count(lax.axis_index("track") * lines_dev, lines_dev, total_lines)
    pixel_count = window_count(lax.axis_index("cross") * pix_dev, pix_dev, total_pix)
    count = pixel_count[:, None, None] * line_count[None, None, :]
    residual, residual_bf = residuals(left, middle, right, planes, count)
    partial_cov = jnp.einsum(
        "pjl,pkl->jk", residual_bf, residual_bf, preferred_element_type=jnp.float32
    )
    packed = pack_symmetric(partial_cov)
    packed = packed + lax.ppermute(packed, "cross", [(i, i ^ 1) for i in range(n_cross)])
    packed = ring_sum(ring_sum(packed, "cross", 2), "track", 1)
    covariance = unpack_symmetric(packed) / (total_lines * total_pix)
    identity = jnp.eye(bands, dtype=jnp.float32)
    loaded = covariance + LOAD * (jnp.trace(covariance) / bands) * identity
    inverse = spd_inverse(loaded)
    solved = jnp.einsum(
        "pbl,bj->pjl", residual, inverse, precision=highest, preferred_element_type=jnp.float32
    )
    scores = jnp.sum(residual * solved, axis=1) / bands
    return scores.T


def solution(mesh):
    return jax.shard_map(
        shards,
        mesh=mesh,
        in_specs=(P("track", "cross", None),),
        out_specs=P("track", "cross"),
        check_vma=False,
    )
```

```python
import functools

import jax
import jax.numpy as jnp
from jax import lax
from jax.experimental import pallas as pl
from jax.experimental.layout import Layout, with_layout_constraint
from jax.sharding import PartitionSpec as P

HALF = 15


LOAD = 0.02


def with_halo(block, sides, width):
    for axis, dim in sides:
        count = lax.axis_size(axis)
        forward = [(i, i + 1) for i in range(count - 1)]
        backward = [(target, source) for source, target in forward]
        low = lax.ppermute(
            lax.slice_in_dim(block, block.shape[dim] - width, None, axis=dim), axis, forward
        )
        high = lax.ppermute(lax.slice_in_dim(block, 0, width, axis=dim), axis, backward)
        block = jnp.concatenate([low, block, high], axis=dim)
    return block


def band_matrix(rows_in, rows_out, dtype):
    source = jnp.arange(rows_in)[:, None]
    target = jnp.arange(rows_out)[None, :]
    inside = (source >= target) & (source <= target + 2 * HALF)
    return inside.astype(dtype)


def butterfly_sum(x, axis):
    count = lax.axis_size(axis)
    step = 1
    while step < count:
        pairs = [(i, i ^ step) for i in range(count)]
        x = x + lax.ppermute(x, axis, pairs)
        step *= 2
    return x


def ring_sum(x, axis, stride):
    count = lax.axis_size(axis)
    groups = count // stride
    total = x
    for shift in range(1, groups):
        pairs = [
            (i, (i + shift * stride) % count) for i in range(count)
        ]
        total = total + lax.ppermute(x, axis, pairs)
    return total


def pack_symmetric(c):
    h = c.shape[0] // 2
    row = jnp.arange(h)[:, None]
    col = jnp.arange(h)[None, :]
    c11, c12, c22 = c[:h, :h], c[:h, h:], c[h:, h:]
    mixed = jnp.where(col >= row, c11, c22)
    return jnp.concatenate([c12, mixed, jnp.diagonal(c22)[None, :]], axis=0)


def unpack_symmetric(p):
    h = p.shape[1]
    row = jnp.arange(h)[:, None]
    col = jnp.arange(h)[None, :]
    c12, mixed, d22 = p[:h], p[h:2 * h], p[2 * h]
    c11 = jnp.where(col >= row, mixed, mixed.T)
    c22 = jnp.where(col < row, mixed, mixed.T)
    c22 = jnp.where(col == row, d22[None, :], c22)
    top = jnp.concatenate([c11, c12], axis=1)
    bottom = jnp.concatenate([c12.T, c22], axis=1)
    return jnp.concatenate([top, bottom], axis=0)


def sweep_kernel(n, a_ref, o_ref):
    size = o_ref.shape[0]
    rows = lax.broadcasted_iota(jnp.int32, (size, 1), 0)
    lanes = lax.broadcasted_iota(jnp.int32, (1, size), 1)
    o_ref[...] = jnp.where(rows == lanes, 1.0, 0.0).astype(jnp.float32)
    o_ref[:n, :n] = a_ref[...]
    sub8 = lax.broadcasted_iota(jnp.int32, (8, 1), 0)

    def pick(v, j):
        return jnp.sum(jnp.where(lanes == j, v, 0.0), axis=1, keepdims=True)

    def body(m, carry):
        k = 2 * m
        base = pl.multiple_of((k // 8) * 8, 8)
        slab = o_ref[pl.ds(base, 8), :]
        r0 = jnp.sum(jnp.where(sub8 == k - base, slab, 0.0), axis=0, keepdims=True)
        r1 = jnp.sum(jnp.where(sub8 == k + 1 - base, slab, 0.0), axis=0, keepdims=True)
        a00, a01, a11 = pick(r0, k), pick(r0, k + 1), pick(r1, k + 1)
        det = a00 * a11 - a01 * a01
        p00, p01, p11 = a11 / det, -a01 / det, a00 / det
        a = o_ref[...]
        c0 = jnp.sum(jnp.where(lanes == k, a, 0.0), axis=1, keepdims=True)
        c1 = jnp.sum(jnp.where(lanes == k + 1, a, 0.0), axis=1, keepdims=True)
        u0 = c0 * p00 + c1 * p01
        u1 = c0 * p01 + c1 * p11
        s0 = r0 * p00 + r1 * p01
        s1 = r0 * p01 + r1 * p11
        main = a - u0 * r0 - u1 * r1
        row0, row1 = rows == k, rows == k + 1
        col0, col1 = lanes == k, lanes == k + 1
        in_rows = row0 | row1
        in_cols = col0 | col1
        corner = jnp.where(row0, jnp.where(col0, -p00, -p01), jnp.where(col0, -p01, -p11))
        side_cols = jnp.where(col0, u0, u1)
        side_rows = jnp.where(row0, s0, s1)
        edge = jnp.where(in_rows, jnp.where(in_cols, corner, side_rows), side_cols)
        o_ref[...] = jnp.where(in_rows | in_cols, edge, main)
        return carry

    lax.fori_loop(0, n // 2, body, 0)


def spd_inverse(a):
    n = a.shape[0]
    assert n % 2 == 0
    size = -(-n // 128) * 128
    swept = pl.pallas_call(
        functools.partial(sweep_kernel, n),
        out_shape=jax.ShapeDtypeStruct((size, size), jnp.float32),
    )(a)
    return -swept[:n, :n]


def window_count(first, local, total):
    index = first + jnp.arange(local)
    upper = jnp.minimum(index + HALF, total - 1)
    lower = jnp.maximum(index - HALF, 0)
    return (upper - lower + 1).astype(jnp.float32)


def sum_pixels(values, width, dtype):
    weights = band_matrix(width + 2 * HALF, width, dtype)
    return jnp.einsum(
        "lqb,qp->lpb", values, weights, precision=None, preferred_element_type=jnp.float32
    )


def sum_lines(values, height, dtype, precision):
    weights = band_matrix(height + 2 * HALF, height, dtype)
    return jnp.einsum(
        "kpb,kl->lpb", values, weights, precision=precision, preferred_element_type=jnp.float32
    )


def neighbour_pairs(n_track, n_cross, dt, dc):
    pairs = []
    for t in range(n_track):
        for c in range(n_cross):
            if 0 <= t + dt < n_track and 0 <= c + dc < n_cross:
                pairs.append(((t + dt) * n_cross + c + dc, t * n_cross + c))
    return pairs


def halos(planes):
    n_track = lax.axis_size("track")
    n_cross = lax.axis_size("cross")
    both = ("track", "cross")

    def fetch(piece, dt, dc):
        if dt == 0:
            pairs = [(c + dc, c) for c in range(n_cross) if 0 <= c + dc < n_cross]
            return lax.ppermute(piece, "cross", pairs)
        if dc == 0:
            pairs = [(t + dt, t) for t in range(n_track) if 0 <= t + dt < n_track]
            return lax.ppermute(piece, "track", pairs)
        return lax.ppermute(piece, both, neighbour_pairs(n_track, n_cross, dt, dc))

    first, last = slice(0, HALF), slice(-HALF, None)
    sides = {
        "left": fetch(planes[last], 0, -1),
        "right": fetch(planes[first], 0, 1),
    }
    top = fetch(planes[:, :, last], -1, 0)
    bottom = fetch(planes[:, :, first], 1, 0)
    tops = {
        "left": fetch(top[last], 0, -1),
        "middle": top,
        "right": fetch(top[first], 0, 1),
    }
    bottoms = {
        "left": fetch(bottom[last], 0, -1),
        "middle": bottom,
        "right": fetch(bottom[first], 0, 1),
    }
    return sides, tops, bottoms


def line_weights(lines):
    target = jnp.arange(lines)[None, :]
    middle = jnp.abs(jnp.arange(lines)[:, None] - target) <= HALF
    side = jnp.arange(HALF)[:, None]
    top = target <= side
    bottom = target >= lines - HALF + side
    return [w.astype(jnp.bfloat16) for w in (top, middle, bottom)]


def sum_lines(top, middle, bottom, weights):
    total = None
    for values, w in zip((top, middle, bottom), weights):
        term = jnp.einsum("qbk,kl->qbl", values, w, preferred_element_type=jnp.float32)
        total = term if total is None else total + term
    return total


def residual_kernel(left_ref, middle_ref, right_ref, x_ref, count_ref, out_ref, out_bf_ref):
    refs = [(left_ref, q) for q in range(left_ref.shape[0])]
    refs += [(middle_ref, q) for q in range(middle_ref.shape[0])]
    refs += [(right_ref, q) for q in range(right_ref.shape[0])]

    def plane(q):
        ref, i = refs[q]
        return ref[i]

    def emit(p, running):
        value = x_ref[p].astype(jnp.float32) - running / count_ref[p]
        out_ref[p] = value
        out_bf_ref[p] = value.astype(jnp.bfloat16)

    span = 2 * HALF + 1
    running = plane(0)
    for q in range(1, span):
        running = running + plane(q)
    emit(0, running)
    for p in range(1, out_ref.shape[0]):
        running = running + plane(p + span - 1) - plane(p - 1)
        emit(p, running)


def residuals(left, middle, right, planes, count):
    width, bands, lines = middle.shape
    block = next((b for b in (56, 32, 16, 8) if bands % b == 0), bands)
    spec = lambda n: pl.BlockSpec((n, block, lines), lambda i: (0, i, 0))
    count_spec = pl.BlockSpec((width, 1, lines), lambda i: (0, 0, 0))
    return pl.pallas_call(
        residual_kernel,
        grid=(bands // block,),
        in_specs=[spec(left.shape[0]), spec(width), spec(right.shape[0]), spec(width), count_spec],
        out_specs=[spec(width), spec(width)],
        out_shape=[
            jax.ShapeDtypeStruct((width, bands, lines), jnp.float32),
            jax.ShapeDtypeStruct((width, bands, lines), jnp.bfloat16),
        ],
    )(left, middle, right, planes, count)


def shards(cube):
    lines_dev, pix_dev, bands = cube.shape
    n_track = lax.axis_size("track")
    n_cross = lax.axis_size("cross")
    total_lines = lines_dev * n_track
    total_pix = pix_dev * n_cross
    highest = lax.Precision.HIGHEST
    planes = jnp.transpose(cube, (1, 2, 0))
    sides, tops, bottoms = halos(planes)
    weights = line_weights(lines_dev)
    middle = sum_lines(tops["middle"], planes, bottoms["middle"], weights)
    left = sum_lines(tops["left"], sides["left"], bottoms["left"], weights)
    right = sum_lines(tops["right"], sides["right"], bottoms["right"], weights)
    line_count = window_count(lax.axis_index("track") * lines_dev, lines_dev, total_lines)
    pixel_count = window_count(lax.axis_index("cross") * pix_dev, pix_dev, total_pix)
    count = pixel_count[:, None, None] * line_count[None, None, :]
    residual, residual_bf = residuals(left, middle, right, planes, count)
    partial_cov = jnp.einsum(
        "pjl,pkl->jk", residual_bf, residual_bf, preferred_element_type=jnp.float32
    )
    packed = pack_symmetric(partial_cov)
    packed = packed + lax.ppermute(packed, "cross", [(i, i ^ 1) for i in range(n_cross)])
    packed = ring_sum(ring_sum(packed, "cross", 2), "track", 1)
    covariance = unpack_symmetric(packed) / (total_lines * total_pix)
    identity = jnp.eye(bands, dtype=jnp.float32)
    loaded = covariance + LOAD * (jnp.trace(covariance) / bands) * identity
    inverse = spd_inverse(loaded)
    solved = jnp.einsum(
        "pbl,bj->pjl", residual, inverse, precision=highest, preferred_element_type=jnp.float32
    )
    scores = jnp.sum(residual * solved, axis=1) / bands
    return scores.T


def solution(mesh):
    return jax.shard_map(
        shards,
        mesh=mesh,
        in_specs=(P("track", "cross", None),),
        out_specs=P("track", "cross"),
        check_vma=False,
    )
```

```python
import functools

import jax
import jax.numpy as jnp
from jax import lax
from jax.experimental import pallas as pl
from jax.experimental.layout import Layout, with_layout_constraint
from jax.sharding import PartitionSpec as P

HALF = 15


LOAD = 0.02


def with_halo(block, sides, width):
    for axis, dim in sides:
        count = lax.axis_size(axis)
        forward = [(i, i + 1) for i in range(count - 1)]
        backward = [(target, source) for source, target in forward]
        low = lax.ppermute(
            lax.slice_in_dim(block, block.shape[dim] - width, None, axis=dim), axis, forward
        )
        high = lax.ppermute(lax.slice_in_dim(block, 0, width, axis=dim), axis, backward)
        block = jnp.concatenate([low, block, high], axis=dim)
    return block


def band_matrix(rows_in, rows_out, dtype):
    source = jnp.arange(rows_in)[:, None]
    target = jnp.arange(rows_out)[None, :]
    inside = (source >= target) & (source <= target + 2 * HALF)
    return inside.astype(dtype)


def butterfly_sum(x, axis):
    count = lax.axis_size(axis)
    step = 1
    while step < count:
        pairs = [(i, i ^ step) for i in range(count)]
        x = x + lax.ppermute(x, axis, pairs)
        step *= 2
    return x


def ring_sum(x, axis, stride):
    count = lax.axis_size(axis)
    groups = count // stride
    total = x
    for shift in range(1, groups):
        pairs = [
            (i, (i + shift * stride) % count) for i in range(count)
        ]
        total = total + lax.ppermute(x, axis, pairs)
    return total


def pack_symmetric(c):
    h = c.shape[0] // 2
    row = jnp.arange(h)[:, None]
    col = jnp.arange(h)[None, :]
    c11, c12, c22 = c[:h, :h], c[:h, h:], c[h:, h:]
    mixed = jnp.where(col >= row, c11, c22)
    return jnp.concatenate([c12, mixed, jnp.diagonal(c22)[None, :]], axis=0)


def unpack_symmetric(p):
    h = p.shape[1]
    row = jnp.arange(h)[:, None]
    col = jnp.arange(h)[None, :]
    c12, mixed, d22 = p[:h], p[h:2 * h], p[2 * h]
    c11 = jnp.where(col >= row, mixed, mixed.T)
    c22 = jnp.where(col < row, mixed, mixed.T)
    c22 = jnp.where(col == row, d22[None, :], c22)
    top = jnp.concatenate([c11, c12], axis=1)
    bottom = jnp.concatenate([c12.T, c22], axis=1)
    return jnp.concatenate([top, bottom], axis=0)


def sweep_kernel(n, a_ref, o_ref):
    size = o_ref.shape[0]
    rows = lax.broadcasted_iota(jnp.int32, (size, 1), 0)
    lanes = lax.broadcasted_iota(jnp.int32, (1, size), 1)
    o_ref[...] = jnp.where(rows == lanes, 1.0, 0.0).astype(jnp.float32)
    o_ref[:n, :n] = a_ref[...]
    sub8 = lax.broadcasted_iota(jnp.int32, (8, 1), 0)

    def pick(v, j):
        return jnp.sum(jnp.where(lanes == j, v, 0.0), axis=1, keepdims=True)

    def body(m, carry):
        k = 2 * m
        base = pl.multiple_of((k // 8) * 8, 8)
        slab = o_ref[pl.ds(base, 8), :]
        r0 = jnp.sum(jnp.where(sub8 == k - base, slab, 0.0), axis=0, keepdims=True)
        r1 = jnp.sum(jnp.where(sub8 == k + 1 - base, slab, 0.0), axis=0, keepdims=True)
        a00, a01, a11 = pick(r0, k), pick(r0, k + 1), pick(r1, k + 1)
        det = a00 * a11 - a01 * a01
        p00, p01, p11 = a11 / det, -a01 / det, a00 / det
        a = o_ref[...]
        c0 = jnp.sum(jnp.where(lanes == k, a, 0.0), axis=1, keepdims=True)
        c1 = jnp.sum(jnp.where(lanes == k + 1, a, 0.0), axis=1, keepdims=True)
        u0 = c0 * p00 + c1 * p01
        u1 = c0 * p01 + c1 * p11
        s0 = r0 * p00 + r1 * p01
        s1 = r0 * p01 + r1 * p11
        main = a - u0 * r0 - u1 * r1
        row0, row1 = rows == k, rows == k + 1
        col0, col1 = lanes == k, lanes == k + 1
        in_rows = row0 | row1
        in_cols = col0 | col1
        corner = jnp.where(row0, jnp.where(col0, -p00, -p01), jnp.where(col0, -p01, -p11))
        side_cols = jnp.where(col0, u0, u1)
        side_rows = jnp.where(row0, s0, s1)
        edge = jnp.where(in_rows, jnp.where(in_cols, corner, side_rows), side_cols)
        o_ref[...] = jnp.where(in_rows | in_cols, edge, main)
        return carry

    lax.fori_loop(0, n // 2, body, 0)


def spd_inverse(a):
    n = a.shape[0]
    assert n % 2 == 0
    size = -(-n // 128) * 128
    swept = pl.pallas_call(
        functools.partial(sweep_kernel, n),
        out_shape=jax.ShapeDtypeStruct((size, size), jnp.float32),
    )(a)
    return -swept[:n, :n]


def window_count(first, local, total):
    index = first + jnp.arange(local)
    upper = jnp.minimum(index + HALF, total - 1)
    lower = jnp.maximum(index - HALF, 0)
    return (upper - lower + 1).astype(jnp.float32)


def sum_pixels(values, width, dtype):
    weights = band_matrix(width + 2 * HALF, width, dtype)
    return jnp.einsum(
        "lqb,qp->lpb", values, weights, precision=None, preferred_element_type=jnp.float32
    )


def sum_lines(values, height, dtype, precision):
    weights = band_matrix(height + 2 * HALF, height, dtype)
    return jnp.einsum(
        "kpb,kl->lpb", values, weights, precision=precision, preferred_element_type=jnp.float32
    )


def neighbour_pairs(n_track, n_cross, dt, dc):
    pairs = []
    for t in range(n_track):
        for c in range(n_cross):
            if 0 <= t + dt < n_track and 0 <= c + dc < n_cross:
                pairs.append(((t + dt) * n_cross + c + dc, t * n_cross + c))
    return pairs


def halos(planes):
    n_track = lax.axis_size("track")
    n_cross = lax.axis_size("cross")
    both = ("track", "cross")

    def fetch(piece, dt, dc):
        if dt == 0:
            pairs = [(c + dc, c) for c in range(n_cross) if 0 <= c + dc < n_cross]
            return lax.ppermute(piece, "cross", pairs)
        if dc == 0:
            pairs = [(t + dt, t) for t in range(n_track) if 0 <= t + dt < n_track]
            return lax.ppermute(piece, "track", pairs)
        return lax.ppermute(piece, both, neighbour_pairs(n_track, n_cross, dt, dc))

    first, last = slice(0, HALF), slice(-HALF, None)
    to_right, to_left, planes = lax.optimization_barrier((planes[last], planes[first], planes))
    sides = {
        "left": fetch(to_right, 0, -1),
        "right": fetch(to_left, 0, 1),
    }
    top = fetch(planes[:, :, last], -1, 0)
    bottom = fetch(planes[:, :, first], 1, 0)
    tops = {
        "left": fetch(top[last], 0, -1),
        "middle": top,
        "right": fetch(top[first], 0, 1),
    }
    bottoms = {
        "left": fetch(bottom[last], 0, -1),
        "middle": bottom,
        "right": fetch(bottom[first], 0, 1),
    }
    return sides, tops, bottoms


def line_weights(lines):
    target = jnp.arange(lines)[None, :]
    middle = jnp.abs(jnp.arange(lines)[:, None] - target) <= HALF
    side = jnp.arange(HALF)[:, None]
    top = target <= side
    bottom = target >= lines - HALF + side
    return [w.astype(jnp.bfloat16) for w in (top, middle, bottom)]


def sum_lines(top, middle, bottom, weights):
    total = None
    for values, w in zip((top, middle, bottom), weights):
        term = jnp.einsum("qbk,kl->qbl", values, w, preferred_element_type=jnp.float32)
        total = term if total is None else total + term
    return total


def residual_kernel(left_ref, middle_ref, right_ref, x_ref, count_ref, out_ref, out_bf_ref):
    refs = [(left_ref, q) for q in range(left_ref.shape[0])]
    refs += [(middle_ref, q) for q in range(middle_ref.shape[0])]
    refs += [(right_ref, q) for q in range(right_ref.shape[0])]

    def plane(q):
        ref, i = refs[q]
        return ref[i]

    def emit(p, running):
        value = x_ref[p].astype(jnp.float32) - running / count_ref[p]
        out_ref[p] = value
        out_bf_ref[p] = value.astype(jnp.bfloat16)

    span = 2 * HALF + 1
    running = plane(0)
    for q in range(1, span):
        running = running + plane(q)
    emit(0, running)
    for p in range(1, out_ref.shape[0]):
        running = running + plane(p + span - 1) - plane(p - 1)
        emit(p, running)


def residuals(left, middle, right, planes, count):
    width, bands, lines = middle.shape
    block = next((b for b in (56, 32, 16, 8) if bands % b == 0), bands)
    spec = lambda n: pl.BlockSpec((n, block, lines), lambda i: (0, i, 0))
    count_spec = pl.BlockSpec((width, 1, lines), lambda i: (0, 0, 0))
    return pl.pallas_call(
        residual_kernel,
        grid=(bands // block,),
        in_specs=[spec(left.shape[0]), spec(width), spec(right.shape[0]), spec(width), count_spec],
        out_specs=[spec(width), spec(width)],
        out_shape=[
            jax.ShapeDtypeStruct((width, bands, lines), jnp.float32),
            jax.ShapeDtypeStruct((width, bands, lines), jnp.bfloat16),
        ],
    )(left, middle, right, planes, count)


def shards(cube):
    lines_dev, pix_dev, bands = cube.shape
    n_track = lax.axis_size("track")
    n_cross = lax.axis_size("cross")
    total_lines = lines_dev * n_track
    total_pix = pix_dev * n_cross
    highest = lax.Precision.HIGHEST
    planes = jnp.transpose(cube, (1, 2, 0))
    sides, tops, bottoms = halos(planes)
    weights = line_weights(lines_dev)
    middle = sum_lines(tops["middle"], planes, bottoms["middle"], weights)
    left = sum_lines(tops["left"], sides["left"], bottoms["left"], weights)
    right = sum_lines(tops["right"], sides["right"], bottoms["right"], weights)
    line_count = window_count(lax.axis_index("track") * lines_dev, lines_dev, total_lines)
    pixel_count = window_count(lax.axis_index("cross") * pix_dev, pix_dev, total_pix)
    count = pixel_count[:, None, None] * line_count[None, None, :]
    residual, residual_bf = residuals(left, middle, right, planes, count)
    partial_cov = jnp.einsum(
        "pjl,pkl->jk", residual_bf, residual_bf, preferred_element_type=jnp.float32
    )
    packed = pack_symmetric(partial_cov)
    packed = packed + lax.ppermute(packed, "cross", [(i, i ^ 1) for i in range(n_cross)])
    packed = ring_sum(ring_sum(packed, "cross", 2), "track", 1)
    covariance = unpack_symmetric(packed) / (total_lines * total_pix)
    identity = jnp.eye(bands, dtype=jnp.float32)
    loaded = covariance + LOAD * (jnp.trace(covariance) / bands) * identity
    inverse = spd_inverse(loaded)
    solved = jnp.einsum(
        "pbl,bj->pjl", residual, inverse, precision=highest, preferred_element_type=jnp.float32
    )
    scores = jnp.sum(residual * solved, axis=1) / bands
    return scores.T


def solution(mesh):
    return jax.shard_map(
        shards,
        mesh=mesh,
        in_specs=(P("track", "cross", None),),
        out_specs=P("track", "cross"),
        check_vma=False,
    )
```

```python
import functools

import jax
import jax.numpy as jnp
from jax import lax
from jax.experimental import pallas as pl
from jax.experimental.layout import Layout, with_layout_constraint
from jax.sharding import PartitionSpec as P

HALF = 15


LOAD = 0.02


def with_halo(block, sides, width):
    for axis, dim in sides:
        count = lax.axis_size(axis)
        forward = [(i, i + 1) for i in range(count - 1)]
        backward = [(target, source) for source, target in forward]
        low = lax.ppermute(
            lax.slice_in_dim(block, block.shape[dim] - width, None, axis=dim), axis, forward
        )
        high = lax.ppermute(lax.slice_in_dim(block, 0, width, axis=dim), axis, backward)
        block = jnp.concatenate([low, block, high], axis=dim)
    return block


def band_matrix(rows_in, rows_out, dtype):
    source = jnp.arange(rows_in)[:, None]
    target = jnp.arange(rows_out)[None, :]
    inside = (source >= target) & (source <= target + 2 * HALF)
    return inside.astype(dtype)


def butterfly_sum(x, axis):
    count = lax.axis_size(axis)
    step = 1
    while step < count:
        pairs = [(i, i ^ step) for i in range(count)]
        x = x + lax.ppermute(x, axis, pairs)
        step *= 2
    return x


def ring_sum(x, axis, stride):
    count = lax.axis_size(axis)
    groups = count // stride
    total = x
    for shift in range(1, groups):
        pairs = [
            (i, (i + shift * stride) % count) for i in range(count)
        ]
        total = total + lax.ppermute(x, axis, pairs)
    return total


def pack_symmetric(c):
    h = c.shape[0] // 2
    row = jnp.arange(h)[:, None]
    col = jnp.arange(h)[None, :]
    c11, c12, c22 = c[:h, :h], c[:h, h:], c[h:, h:]
    mixed = jnp.where(col >= row, c11, c22)
    diagonal = jnp.sum(jnp.where(col == row, c22, 0.0), axis=0, keepdims=True)
    return jnp.concatenate([c12, mixed, diagonal], axis=0)


def unpack_symmetric(p):
    h = p.shape[1]
    row = jnp.arange(h)[:, None]
    col = jnp.arange(h)[None, :]
    c12, mixed, d22 = p[:h], p[h:2 * h], p[2 * h]
    c11 = jnp.where(col >= row, mixed, mixed.T)
    c22 = jnp.where(col < row, mixed, mixed.T)
    c22 = jnp.where(col == row, d22[None, :], c22)
    top = jnp.concatenate([c11, c12], axis=1)
    bottom = jnp.concatenate([c12.T, c22], axis=1)
    return jnp.concatenate([top, bottom], axis=0)


def sweep_kernel(n, a_ref, o_ref):
    size = o_ref.shape[0]
    rows = lax.broadcasted_iota(jnp.int32, (size, 1), 0)
    lanes = lax.broadcasted_iota(jnp.int32, (1, size), 1)
    o_ref[...] = jnp.where(rows == lanes, 1.0, 0.0).astype(jnp.float32)
    o_ref[:n, :n] = a_ref[...]
    sub8 = lax.broadcasted_iota(jnp.int32, (8, 1), 0)

    def pick(v, j):
        return jnp.sum(jnp.where(lanes == j, v, 0.0), axis=1, keepdims=True)

    def body(m, carry):
        k = 2 * m
        base = pl.multiple_of((k // 8) * 8, 8)
        slab = o_ref[pl.ds(base, 8), :]
        r0 = jnp.sum(jnp.where(sub8 == k - base, slab, 0.0), axis=0, keepdims=True)
        r1 = jnp.sum(jnp.where(sub8 == k + 1 - base, slab, 0.0), axis=0, keepdims=True)
        a00, a01, a11 = pick(r0, k), pick(r0, k + 1), pick(r1, k + 1)
        det = a00 * a11 - a01 * a01
        p00, p01, p11 = a11 / det, -a01 / det, a00 / det
        a = o_ref[...]
        c0 = jnp.sum(jnp.where(lanes == k, a, 0.0), axis=1, keepdims=True)
        c1 = jnp.sum(jnp.where(lanes == k + 1, a, 0.0), axis=1, keepdims=True)
        u0 = c0 * p00 + c1 * p01
        u1 = c0 * p01 + c1 * p11
        s0 = r0 * p00 + r1 * p01
        s1 = r0 * p01 + r1 * p11
        main = a - u0 * r0 - u1 * r1
        row0, row1 = rows == k, rows == k + 1
        col0, col1 = lanes == k, lanes == k + 1
        in_rows = row0 | row1
        in_cols = col0 | col1
        corner = jnp.where(row0, jnp.where(col0, -p00, -p01), jnp.where(col0, -p01, -p11))
        side_cols = jnp.where(col0, u0, u1)
        side_rows = jnp.where(row0, s0, s1)
        edge = jnp.where(in_rows, jnp.where(in_cols, corner, side_rows), side_cols)
        o_ref[...] = jnp.where(in_rows | in_cols, edge, main)
        return carry

    lax.fori_loop(0, n // 2, body, 0)


def spd_inverse(a):
    n = a.shape[0]
    assert n % 2 == 0
    size = -(-n // 128) * 128
    swept = pl.pallas_call(
        functools.partial(sweep_kernel, n),
        out_shape=jax.ShapeDtypeStruct((size, size), jnp.float32),
    )(a)
    return -swept[:n, :n]


def window_count(first, local, total):
    index = first + jnp.arange(local)
    upper = jnp.minimum(index + HALF, total - 1)
    lower = jnp.maximum(index - HALF, 0)
    return (upper - lower + 1).astype(jnp.float32)


def sum_pixels(values, width, dtype):
    weights = band_matrix(width + 2 * HALF, width, dtype)
    return jnp.einsum(
        "lqb,qp->lpb", values, weights, precision=None, preferred_element_type=jnp.float32
    )


def sum_lines(values, height, dtype, precision):
    weights = band_matrix(height + 2 * HALF, height, dtype)
    return jnp.einsum(
        "kpb,kl->lpb", values, weights, precision=precision, preferred_element_type=jnp.float32
    )


def neighbour_pairs(n_track, n_cross, dt, dc):
    pairs = []
    for t in range(n_track):
        for c in range(n_cross):
            if 0 <= t + dt < n_track and 0 <= c + dc < n_cross:
                pairs.append(((t + dt) * n_cross + c + dc, t * n_cross + c))
    return pairs


def halos(planes):
    n_track = lax.axis_size("track")
    n_cross = lax.axis_size("cross")
    both = ("track", "cross")

    def fetch(piece, dt, dc):
        if dt == 0:
            pairs = [(c + dc, c) for c in range(n_cross) if 0 <= c + dc < n_cross]
            return lax.ppermute(piece, "cross", pairs)
        if dc == 0:
            pairs = [(t + dt, t) for t in range(n_track) if 0 <= t + dt < n_track]
            return lax.ppermute(piece, "track", pairs)
        return lax.ppermute(piece, both, neighbour_pairs(n_track, n_cross, dt, dc))

    first, last = slice(0, HALF), slice(-HALF, None)
    to_right, to_left, planes = lax.optimization_barrier((planes[last], planes[first], planes))
    sides = {
        "left": fetch(to_right, 0, -1),
        "right": fetch(to_left, 0, 1),
    }
    top = fetch(planes[:, :, last], -1, 0)
    bottom = fetch(planes[:, :, first], 1, 0)
    tops = {
        "left": fetch(top[last], 0, -1),
        "middle": top,
        "right": fetch(top[first], 0, 1),
    }
    bottoms = {
        "left": fetch(bottom[last], 0, -1),
        "middle": bottom,
        "right": fetch(bottom[first], 0, 1),
    }
    return sides, tops, bottoms


def line_weights(lines):
    target = jnp.arange(lines)[None, :]
    middle = jnp.abs(jnp.arange(lines)[:, None] - target) <= HALF
    side = jnp.arange(HALF)[:, None]
    top = target <= side
    bottom = target >= lines - HALF + side
    return [w.astype(jnp.bfloat16) for w in (top, middle, bottom)]


def sum_lines(top, middle, bottom, weights):
    total = None
    for values, w in zip((top, middle, bottom), weights):
        term = jnp.einsum("qbk,kl->qbl", values, w, preferred_element_type=jnp.float32)
        total = term if total is None else total + term
    return total


def residual_kernel(left_ref, middle_ref, right_ref, x_ref, count_ref, out_ref, out_bf_ref):
    refs = [(left_ref, q) for q in range(left_ref.shape[0])]
    refs += [(middle_ref, q) for q in range(middle_ref.shape[0])]
    refs += [(right_ref, q) for q in range(right_ref.shape[0])]

    def plane(q):
        ref, i = refs[q]
        return ref[i]

    def emit(p, running):
        value = x_ref[p].astype(jnp.float32) - running / count_ref[p]
        out_ref[p] = value
        out_bf_ref[p] = value.astype(jnp.bfloat16)

    span = 2 * HALF + 1
    running = plane(0)
    for q in range(1, span):
        running = running + plane(q)
    emit(0, running)
    for p in range(1, out_ref.shape[0]):
        running = running + plane(p + span - 1) - plane(p - 1)
        emit(p, running)


def residuals(left, middle, right, planes, count):
    width, bands, lines = middle.shape
    block = next((b for b in (56, 32, 16, 8) if bands % b == 0), bands)
    spec = lambda n: pl.BlockSpec((n, block, lines), lambda i: (0, i, 0))
    count_spec = pl.BlockSpec((width, 1, lines), lambda i: (0, 0, 0))
    return pl.pallas_call(
        residual_kernel,
        grid=(bands // block,),
        in_specs=[spec(left.shape[0]), spec(width), spec(right.shape[0]), spec(width), count_spec],
        out_specs=[spec(width), spec(width)],
        out_shape=[
            jax.ShapeDtypeStruct((width, bands, lines), jnp.float32),
            jax.ShapeDtypeStruct((width, bands, lines), jnp.bfloat16),
        ],
    )(left, middle, right, planes, count)


def shards(cube):
    lines_dev, pix_dev, bands = cube.shape
    n_track = lax.axis_size("track")
    n_cross = lax.axis_size("cross")
    total_lines = lines_dev * n_track
    total_pix = pix_dev * n_cross
    highest = lax.Precision.HIGHEST
    planes = jnp.transpose(cube, (1, 2, 0))
    sides, tops, bottoms = halos(planes)
    weights = line_weights(lines_dev)
    middle = sum_lines(tops["middle"], planes, bottoms["middle"], weights)
    left = sum_lines(tops["left"], sides["left"], bottoms["left"], weights)
    right = sum_lines(tops["right"], sides["right"], bottoms["right"], weights)
    line_count = window_count(lax.axis_index("track") * lines_dev, lines_dev, total_lines)
    pixel_count = window_count(lax.axis_index("cross") * pix_dev, pix_dev, total_pix)
    count = pixel_count[:, None, None] * line_count[None, None, :]
    residual, residual_bf = residuals(left, middle, right, planes, count)
    partial_cov = jnp.einsum(
        "pjl,pkl->jk", residual_bf, residual_bf, preferred_element_type=jnp.float32
    )
    packed = pack_symmetric(partial_cov)
    packed = packed + lax.ppermute(packed, "cross", [(i, i ^ 1) for i in range(n_cross)])
    packed = ring_sum(ring_sum(packed, "cross", 2), "track", 1)
    covariance = unpack_symmetric(packed) / (total_lines * total_pix)
    identity = jnp.eye(bands, dtype=jnp.float32)
    loaded = covariance + LOAD * (jnp.trace(covariance) / bands) * identity
    inverse = spd_inverse(loaded)
    solved = jnp.einsum(
        "pbl,bj->pjl", residual, inverse, precision=highest, preferred_element_type=jnp.float32
    )
    scores = jnp.sum(residual * solved, axis=1) / bands
    return scores.T


def solution(mesh):
    return jax.shard_map(
        shards,
        mesh=mesh,
        in_specs=(P("track", "cross", None),),
        out_specs=P("track", "cross"),
        check_vma=False,
    )
```

```python
import functools

import jax
import jax.numpy as jnp
from jax import lax
from jax.experimental import pallas as pl
from jax.experimental.layout import Layout, with_layout_constraint
from jax.sharding import PartitionSpec as P

HALF = 15


LOAD = 0.02


def with_halo(block, sides, width):
    for axis, dim in sides:
        count = lax.axis_size(axis)
        forward = [(i, i + 1) for i in range(count - 1)]
        backward = [(target, source) for source, target in forward]
        low = lax.ppermute(
            lax.slice_in_dim(block, block.shape[dim] - width, None, axis=dim), axis, forward
        )
        high = lax.ppermute(lax.slice_in_dim(block, 0, width, axis=dim), axis, backward)
        block = jnp.concatenate([low, block, high], axis=dim)
    return block


def band_matrix(rows_in, rows_out, dtype):
    source = jnp.arange(rows_in)[:, None]
    target = jnp.arange(rows_out)[None, :]
    inside = (source >= target) & (source <= target + 2 * HALF)
    return inside.astype(dtype)


def butterfly_sum(x, axis):
    count = lax.axis_size(axis)
    step = 1
    while step < count:
        pairs = [(i, i ^ step) for i in range(count)]
        x = x + lax.ppermute(x, axis, pairs)
        step *= 2
    return x


def ring_sum(x, axis, stride):
    count = lax.axis_size(axis)
    groups = count // stride
    total = x
    for shift in range(1, groups):
        pairs = [
            (i, (i + shift * stride) % count) for i in range(count)
        ]
        total = total + lax.ppermute(x, axis, pairs)
    return total


def pack_symmetric(c):
    h = c.shape[0] // 2
    row = jnp.arange(h)[:, None]
    col = jnp.arange(h)[None, :]
    c11, c12, c22 = c[:h, :h], c[:h, h:], c[h:, h:]
    mixed = jnp.where(col >= row, c11, c22)
    diagonal = jnp.sum(jnp.where(col == row, c22, 0.0), axis=0, keepdims=True)
    return jnp.concatenate([c12, mixed, diagonal], axis=0)


def unpack_symmetric(p):
    h = p.shape[1]
    row = jnp.arange(h)[:, None]
    col = jnp.arange(h)[None, :]
    c12, mixed, d22 = p[:h], p[h:2 * h], p[2 * h]
    c11 = jnp.where(col >= row, mixed, mixed.T)
    c22 = jnp.where(col < row, mixed, mixed.T)
    c22 = jnp.where(col == row, d22[None, :], c22)
    top = jnp.concatenate([c11, c12], axis=1)
    bottom = jnp.concatenate([c12.T, c22], axis=1)
    return jnp.concatenate([top, bottom], axis=0)


def sweep_kernel(n, load, a_ref, o_ref):
    size = o_ref.shape[0]
    rows = lax.broadcasted_iota(jnp.int32, (size, 1), 0)
    lanes = lax.broadcasted_iota(jnp.int32, (1, size), 1)
    o_ref[...] = jnp.where(rows == lanes, 1.0, 0.0).astype(jnp.float32)
    o_ref[:n, :n] = a_ref[...]
    if load:
        on_diagonal = (rows == lanes) & (rows < n)
        full = o_ref[...]
        trace = jnp.sum(jnp.where(on_diagonal, full, 0.0), axis=(0, 1), keepdims=True)
        o_ref[...] = jnp.where(on_diagonal, full + load * (trace / n), full)
    sub8 = lax.broadcasted_iota(jnp.int32, (8, 1), 0)

    def pick(v, j):
        return jnp.sum(jnp.where(lanes == j, v, 0.0), axis=1, keepdims=True)

    def body(m, carry):
        k = 2 * m
        base = pl.multiple_of((k // 8) * 8, 8)
        slab = o_ref[pl.ds(base, 8), :]
        r0 = jnp.sum(jnp.where(sub8 == k - base, slab, 0.0), axis=0, keepdims=True)
        r1 = jnp.sum(jnp.where(sub8 == k + 1 - base, slab, 0.0), axis=0, keepdims=True)
        a00, a01, a11 = pick(r0, k), pick(r0, k + 1), pick(r1, k + 1)
        det = a00 * a11 - a01 * a01
        p00, p01, p11 = a11 / det, -a01 / det, a00 / det
        a = o_ref[...]
        c0 = jnp.sum(jnp.where(lanes == k, a, 0.0), axis=1, keepdims=True)
        c1 = jnp.sum(jnp.where(lanes == k + 1, a, 0.0), axis=1, keepdims=True)
        u0 = c0 * p00 + c1 * p01
        u1 = c0 * p01 + c1 * p11
        s0 = r0 * p00 + r1 * p01
        s1 = r0 * p01 + r1 * p11
        main = a - u0 * r0 - u1 * r1
        row0, row1 = rows == k, rows == k + 1
        col0, col1 = lanes == k, lanes == k + 1
        in_rows = row0 | row1
        in_cols = col0 | col1
        corner = jnp.where(row0, jnp.where(col0, -p00, -p01), jnp.where(col0, -p01, -p11))
        side_cols = jnp.where(col0, u0, u1)
        side_rows = jnp.where(row0, s0, s1)
        edge = jnp.where(in_rows, jnp.where(in_cols, corner, side_rows), side_cols)
        o_ref[...] = jnp.where(in_rows | in_cols, edge, main)
        return carry

    lax.fori_loop(0, n // 2, body, 0)


def spd_inverse(a, load=0.0):
    n = a.shape[0]
    assert n % 2 == 0
    size = -(-n // 128) * 128
    swept = pl.pallas_call(
        functools.partial(sweep_kernel, n, load),
        out_shape=jax.ShapeDtypeStruct((size, size), jnp.float32),
    )(a)
    return -swept[:n, :n]


def window_count(first, local, total):
    index = first + jnp.arange(local)
    upper = jnp.minimum(index + HALF, total - 1)
    lower = jnp.maximum(index - HALF, 0)
    return (upper - lower + 1).astype(jnp.float32)


def sum_pixels(values, width, dtype):
    weights = band_matrix(width + 2 * HALF, width, dtype)
    return jnp.einsum(
        "lqb,qp->lpb", values, weights, precision=None, preferred_element_type=jnp.float32
    )


def sum_lines(values, height, dtype, precision):
    weights = band_matrix(height + 2 * HALF, height, dtype)
    return jnp.einsum(
        "kpb,kl->lpb", values, weights, precision=precision, preferred_element_type=jnp.float32
    )


def neighbour_pairs(n_track, n_cross, dt, dc):
    pairs = []
    for t in range(n_track):
        for c in range(n_cross):
            if 0 <= t + dt < n_track and 0 <= c + dc < n_cross:
                pairs.append(((t + dt) * n_cross + c + dc, t * n_cross + c))
    return pairs


def halos(planes):
    n_track = lax.axis_size("track")
    n_cross = lax.axis_size("cross")
    both = ("track", "cross")

    def fetch(piece, dt, dc):
        if dt == 0:
            pairs = [(c + dc, c) for c in range(n_cross) if 0 <= c + dc < n_cross]
            return lax.ppermute(piece, "cross", pairs)
        if dc == 0:
            pairs = [(t + dt, t) for t in range(n_track) if 0 <= t + dt < n_track]
            return lax.ppermute(piece, "track", pairs)
        return lax.ppermute(piece, both, neighbour_pairs(n_track, n_cross, dt, dc))

    first, last = slice(0, HALF), slice(-HALF, None)
    to_right, to_left, planes = lax.optimization_barrier((planes[last], planes[first], planes))
    sides = {
        "left": fetch(to_right, 0, -1),
        "right": fetch(to_left, 0, 1),
    }
    top = fetch(planes[:, :, last], -1, 0)
    bottom = fetch(planes[:, :, first], 1, 0)
    tops = {
        "left": fetch(top[last], 0, -1),
        "middle": top,
        "right": fetch(top[first], 0, 1),
    }
    bottoms = {
        "left": fetch(bottom[last], 0, -1),
        "middle": bottom,
        "right": fetch(bottom[first], 0, 1),
    }
    return sides, tops, bottoms


def line_weights(lines):
    target = jnp.arange(lines)[None, :]
    middle = jnp.abs(jnp.arange(lines)[:, None] - target) <= HALF
    side = jnp.arange(HALF)[:, None]
    top = target <= side
    bottom = target >= lines - HALF + side
    return [w.astype(jnp.bfloat16) for w in (top, middle, bottom)]


def sum_lines(top, middle, bottom, weights):
    total = None
    for values, w in zip((top, middle, bottom), weights):
        term = jnp.einsum("qbk,kl->qbl", values, w, preferred_element_type=jnp.float32)
        total = term if total is None else total + term
    return total


def residual_kernel(left_ref, middle_ref, right_ref, x_ref, count_ref, out_ref, out_bf_ref):
    refs = [(left_ref, q) for q in range(left_ref.shape[0])]
    refs += [(middle_ref, q) for q in range(middle_ref.shape[0])]
    refs += [(right_ref, q) for q in range(right_ref.shape[0])]

    def plane(q):
        ref, i = refs[q]
        return ref[i]

    def emit(p, running):
        value = x_ref[p].astype(jnp.float32) - running / count_ref[p]
        out_ref[p] = value
        out_bf_ref[p] = value.astype(jnp.bfloat16)

    span = 2 * HALF + 1
    running = plane(0)
    for q in range(1, span):
        running = running + plane(q)
    emit(0, running)
    for p in range(1, out_ref.shape[0]):
        running = running + plane(p + span - 1) - plane(p - 1)
        emit(p, running)


def residuals(left, middle, right, planes, count):
    width, bands, lines = middle.shape
    block = next((b for b in (56, 32, 16, 8) if bands % b == 0), bands)
    spec = lambda n: pl.BlockSpec((n, block, lines), lambda i: (0, i, 0))
    count_spec = pl.BlockSpec((width, 1, lines), lambda i: (0, 0, 0))
    return pl.pallas_call(
        residual_kernel,
        grid=(bands // block,),
        in_specs=[spec(left.shape[0]), spec(width), spec(right.shape[0]), spec(width), count_spec],
        out_specs=[spec(width), spec(width)],
        out_shape=[
            jax.ShapeDtypeStruct((width, bands, lines), jnp.float32),
            jax.ShapeDtypeStruct((width, bands, lines), jnp.bfloat16),
        ],
    )(left, middle, right, planes, count)


def shards(cube):
    lines_dev, pix_dev, bands = cube.shape
    n_track = lax.axis_size("track")
    n_cross = lax.axis_size("cross")
    total_lines = lines_dev * n_track
    total_pix = pix_dev * n_cross
    highest = lax.Precision.HIGHEST
    planes = jnp.transpose(cube, (1, 2, 0))
    sides, tops, bottoms = halos(planes)
    weights = line_weights(lines_dev)
    middle = sum_lines(tops["middle"], planes, bottoms["middle"], weights)
    left = sum_lines(tops["left"], sides["left"], bottoms["left"], weights)
    right = sum_lines(tops["right"], sides["right"], bottoms["right"], weights)
    line_count = window_count(lax.axis_index("track") * lines_dev, lines_dev, total_lines)
    pixel_count = window_count(lax.axis_index("cross") * pix_dev, pix_dev, total_pix)
    count = pixel_count[:, None, None] * line_count[None, None, :]
    residual, residual_bf = residuals(left, middle, right, planes, count)
    partial_cov = jnp.einsum(
        "pjl,pkl->jk", residual_bf, residual_bf, preferred_element_type=jnp.float32
    )
    packed = pack_symmetric(partial_cov)
    packed = packed + lax.ppermute(packed, "cross", [(i, i ^ 1) for i in range(n_cross)])
    packed = ring_sum(ring_sum(packed, "cross", 2), "track", 1)
    covariance = unpack_symmetric(packed) / (total_lines * total_pix)
    inverse = spd_inverse(covariance, LOAD)
    solved = jnp.einsum(
        "pbl,bj->pjl", residual, inverse, precision=highest, preferred_element_type=jnp.float32
    )
    scores = jnp.sum(residual * solved, axis=1) / bands
    return scores.T


def solution(mesh):
    return jax.shard_map(
        shards,
        mesh=mesh,
        in_specs=(P("track", "cross", None),),
        out_specs=P("track", "cross"),
        check_vma=False,
    )
```

```python
import functools

import jax
import jax.numpy as jnp
from jax import lax
from jax.experimental import pallas as pl
from jax.experimental.layout import Layout, with_layout_constraint
from jax.sharding import PartitionSpec as P

HALF = 15


LOAD = 0.02


def with_halo(block, sides, width):
    for axis, dim in sides:
        count = lax.axis_size(axis)
        forward = [(i, i + 1) for i in range(count - 1)]
        backward = [(target, source) for source, target in forward]
        low = lax.ppermute(
            lax.slice_in_dim(block, block.shape[dim] - width, None, axis=dim), axis, forward
        )
        high = lax.ppermute(lax.slice_in_dim(block, 0, width, axis=dim), axis, backward)
        block = jnp.concatenate([low, block, high], axis=dim)
    return block


def band_matrix(rows_in, rows_out, dtype):
    source = jnp.arange(rows_in)[:, None]
    target = jnp.arange(rows_out)[None, :]
    inside = (source >= target) & (source <= target + 2 * HALF)
    return inside.astype(dtype)


def butterfly_sum(x, axis):
    count = lax.axis_size(axis)
    step = 1
    while step < count:
        pairs = [(i, i ^ step) for i in range(count)]
        x = x + lax.ppermute(x, axis, pairs)
        step *= 2
    return x


def ring_sum(x, axis, stride):
    count = lax.axis_size(axis)
    groups = count // stride
    total = x
    for shift in range(1, groups):
        pairs = [
            (i, (i + shift * stride) % count) for i in range(count)
        ]
        total = total + lax.ppermute(x, axis, pairs)
    return total


def pack_symmetric(c):
    h = c.shape[0] // 2
    row = jnp.arange(h)[:, None]
    col = jnp.arange(h)[None, :]
    c11, c12, c22 = c[:h, :h], c[:h, h:], c[h:, h:]
    mixed = jnp.where(col >= row, c11, c22)
    diagonal = jnp.sum(jnp.where(col == row, c22, 0.0), axis=0, keepdims=True)
    return jnp.concatenate([c12, mixed, diagonal], axis=0)


def unpack_symmetric(p):
    h = p.shape[1]
    row = jnp.arange(h)[:, None]
    col = jnp.arange(h)[None, :]
    c12, mixed, d22 = p[:h], p[h:2 * h], p[2 * h]
    c11 = jnp.where(col >= row, mixed, mixed.T)
    c22 = jnp.where(col < row, mixed, mixed.T)
    c22 = jnp.where(col == row, d22[None, :], c22)
    top = jnp.concatenate([c11, c12], axis=1)
    bottom = jnp.concatenate([c12.T, c22], axis=1)
    return jnp.concatenate([top, bottom], axis=0)


def sweep_kernel(n, load, a_ref, o_ref):
    size = o_ref.shape[0]
    rows = lax.broadcasted_iota(jnp.int32, (size, 1), 0)
    lanes = lax.broadcasted_iota(jnp.int32, (1, size), 1)
    o_ref[...] = jnp.where(rows == lanes, 1.0, 0.0).astype(jnp.float32)
    o_ref[:n, :n] = a_ref[...]
    if load:
        on_diagonal = (rows == lanes) & (rows < n)
        full = o_ref[...]
        trace = jnp.sum(jnp.where(on_diagonal, full, 0.0), axis=(0, 1), keepdims=True)
        o_ref[...] = jnp.where(on_diagonal, full + load * (trace / n), full)
    sub8 = lax.broadcasted_iota(jnp.int32, (8, 1), 0)

    def pick(v, j):
        return jnp.sum(jnp.where(lanes == j, v, 0.0), axis=1, keepdims=True)

    def body(m, carry):
        k = 2 * m
        base = pl.multiple_of((k // 8) * 8, 8)
        slab = o_ref[pl.ds(base, 8), :]
        r0 = jnp.sum(jnp.where(sub8 == k - base, slab, 0.0), axis=0, keepdims=True)
        r1 = jnp.sum(jnp.where(sub8 == k + 1 - base, slab, 0.0), axis=0, keepdims=True)
        a00, a01, a11 = pick(r0, k), pick(r0, k + 1), pick(r1, k + 1)
        det = a00 * a11 - a01 * a01
        p00, p01, p11 = a11 / det, -a01 / det, a00 / det
        a = o_ref[...]
        c0 = jnp.sum(jnp.where(lanes == k, a, 0.0), axis=1, keepdims=True)
        c1 = jnp.sum(jnp.where(lanes == k + 1, a, 0.0), axis=1, keepdims=True)
        u0 = c0 * p00 + c1 * p01
        u1 = c0 * p01 + c1 * p11
        s0 = r0 * p00 + r1 * p01
        s1 = r0 * p01 + r1 * p11
        main = a - u0 * r0 - u1 * r1
        row0, row1 = rows == k, rows == k + 1
        col0, col1 = lanes == k, lanes == k + 1
        in_rows = row0 | row1
        in_cols = col0 | col1
        corner = jnp.where(row0, jnp.where(col0, -p00, -p01), jnp.where(col0, -p01, -p11))
        side_cols = jnp.where(col0, u0, u1)
        side_rows = jnp.where(row0, s0, s1)
        edge = jnp.where(in_rows, jnp.where(in_cols, corner, side_rows), side_cols)
        o_ref[...] = jnp.where(in_rows | in_cols, edge, main)
        return carry

    lax.fori_loop(0, n // 2, body, 0)


def spd_inverse(a, load=0.0):
    n = a.shape[0]
    assert n % 2 == 0
    size = -(-n // 128) * 128
    swept = pl.pallas_call(
        functools.partial(sweep_kernel, n, load),
        out_shape=jax.ShapeDtypeStruct((size, size), jnp.float32),
    )(a)
    return -swept[:n, :n]


def window_count(first, local, total):
    index = first + jnp.arange(local)
    upper = jnp.minimum(index + HALF, total - 1)
    lower = jnp.maximum(index - HALF, 0)
    return (upper - lower + 1).astype(jnp.float32)


def sum_pixels(values, width, dtype):
    weights = band_matrix(width + 2 * HALF, width, dtype)
    return jnp.einsum(
        "lqb,qp->lpb", values, weights, precision=None, preferred_element_type=jnp.float32
    )


def sum_lines(values, height, dtype, precision):
    weights = band_matrix(height + 2 * HALF, height, dtype)
    return jnp.einsum(
        "kpb,kl->lpb", values, weights, precision=precision, preferred_element_type=jnp.float32
    )


def neighbour_pairs(n_track, n_cross, dt, dc):
    pairs = []
    for t in range(n_track):
        for c in range(n_cross):
            if 0 <= t + dt < n_track and 0 <= c + dc < n_cross:
                pairs.append(((t + dt) * n_cross + c + dc, t * n_cross + c))
    return pairs


def halos(planes):
    n_track = lax.axis_size("track")
    n_cross = lax.axis_size("cross")
    both = ("track", "cross")

    def fetch(piece, dt, dc):
        if dt == 0:
            pairs = [(c + dc, c) for c in range(n_cross) if 0 <= c + dc < n_cross]
            return lax.ppermute(piece, "cross", pairs)
        if dc == 0:
            pairs = [(t + dt, t) for t in range(n_track) if 0 <= t + dt < n_track]
            return lax.ppermute(piece, "track", pairs)
        return lax.ppermute(piece, both, neighbour_pairs(n_track, n_cross, dt, dc))

    first, last = slice(0, HALF), slice(-HALF, None)
    to_right, to_left, planes = lax.optimization_barrier((planes[last], planes[first], planes))
    sides = {
        "left": fetch(to_right, 0, -1),
        "right": fetch(to_left, 0, 1),
    }
    top = fetch(planes[:, :, last], -1, 0)
    bottom = fetch(planes[:, :, first], 1, 0)
    tops = {
        "left": fetch(top[last], 0, -1),
        "middle": top,
        "right": fetch(top[first], 0, 1),
    }
    bottoms = {
        "left": fetch(bottom[last], 0, -1),
        "middle": bottom,
        "right": fetch(bottom[first], 0, 1),
    }
    return sides, tops, bottoms


def line_weights(lines):
    target = jnp.arange(lines)[None, :]
    middle = jnp.abs(jnp.arange(lines)[:, None] - target) <= HALF
    side = jnp.arange(HALF)[:, None]
    top = target <= side
    bottom = target >= lines - HALF + side
    return [w.astype(jnp.bfloat16) for w in (top, middle, bottom)]


def sum_lines(top, middle, bottom, weights):
    total = None
    for values, w in zip((top, middle, bottom), weights):
        term = jnp.einsum("qbk,kl->qbl", values, w, preferred_element_type=jnp.float32)
        total = term if total is None else total + term
    return total


def residual_kernel(left_ref, middle_ref, right_ref, x_ref, count_ref, out_ref, out_bf_ref):
    refs = [(left_ref, q) for q in range(left_ref.shape[0])]
    refs += [(middle_ref, q) for q in range(middle_ref.shape[0])]
    refs += [(right_ref, q) for q in range(right_ref.shape[0])]

    def plane(q):
        ref, i = refs[q]
        return ref[i]

    def emit(p, running):
        value = x_ref[p].astype(jnp.float32) - running / count_ref[p]
        out_ref[p] = value
        out_bf_ref[p] = value.astype(jnp.bfloat16)

    span = 2 * HALF + 1
    running = plane(0)
    for q in range(1, span):
        running = running + plane(q)
    emit(0, running)
    for p in range(1, out_ref.shape[0]):
        running = running + plane(p + span - 1) - plane(p - 1)
        emit(p, running)


def residuals(left, middle, right, planes, count):
    width, bands, lines = middle.shape
    block = next((b for b in (56, 32, 16, 8) if bands % b == 0), bands)
    spec = lambda n: pl.BlockSpec((n, block, lines), lambda i: (0, i, 0))
    count_spec = pl.BlockSpec((width, 1, lines), lambda i: (0, 0, 0))
    return pl.pallas_call(
        residual_kernel,
        grid=(bands // block,),
        in_specs=[spec(left.shape[0]), spec(width), spec(right.shape[0]), spec(width), count_spec],
        out_specs=[spec(width), spec(width)],
        out_shape=[
            jax.ShapeDtypeStruct((width, bands, lines), jnp.float32),
            jax.ShapeDtypeStruct((width, bands, lines), jnp.bfloat16),
        ],
    )(left, middle, right, planes, count)


def shards(cube):
    lines_dev, pix_dev, bands = cube.shape
    n_track = lax.axis_size("track")
    n_cross = lax.axis_size("cross")
    total_lines = lines_dev * n_track
    total_pix = pix_dev * n_cross
    highest = lax.Precision.HIGHEST
    planes = jnp.transpose(cube, (1, 2, 0))
    sides, tops, bottoms = halos(planes)
    weights = line_weights(lines_dev)
    middle = sum_lines(tops["middle"], planes, bottoms["middle"], weights)
    left = sum_lines(tops["left"], sides["left"], bottoms["left"], weights)
    right = sum_lines(tops["right"], sides["right"], bottoms["right"], weights)
    line_count = window_count(lax.axis_index("track") * lines_dev, lines_dev, total_lines)
    pixel_count = window_count(lax.axis_index("cross") * pix_dev, pix_dev, total_pix)
    count = pixel_count[:, None, None] * line_count[None, None, :]
    residual, residual_bf = residuals(left, middle, right, planes, count)
    partial_cov = jnp.einsum(
        "pjl,pkl->jk", residual_bf, residual_bf, preferred_element_type=jnp.float32
    )
    packed = pack_symmetric(partial_cov)
    packed = packed + lax.ppermute(packed, "cross", [(i, i ^ 1) for i in range(n_cross)])
    packed = butterfly_sum(ring_sum(packed, "cross", 2), "track")
    covariance = unpack_symmetric(packed) / (total_lines * total_pix)
    inverse = spd_inverse(covariance, LOAD)
    solved = jnp.einsum(
        "pbl,bj->pjl", residual, inverse, precision=highest, preferred_element_type=jnp.float32
    )
    scores = jnp.sum(residual * solved, axis=1) / bands
    return scores.T


def solution(mesh):
    return jax.shard_map(
        shards,
        mesh=mesh,
        in_specs=(P("track", "cross", None),),
        out_specs=P("track", "cross"),
        check_vma=False,
    )
```

```python
import functools

import jax
import jax.numpy as jnp
from jax import lax
from jax.experimental import pallas as pl
from jax.experimental.layout import Layout, with_layout_constraint
from jax.sharding import PartitionSpec as P

HALF = 15


LOAD = 0.02


def with_halo(block, sides, width):
    for axis, dim in sides:
        count = lax.axis_size(axis)
        forward = [(i, i + 1) for i in range(count - 1)]
        backward = [(target, source) for source, target in forward]
        low = lax.ppermute(
            lax.slice_in_dim(block, block.shape[dim] - width, None, axis=dim), axis, forward
        )
        high = lax.ppermute(lax.slice_in_dim(block, 0, width, axis=dim), axis, backward)
        block = jnp.concatenate([low, block, high], axis=dim)
    return block


def band_matrix(rows_in, rows_out, dtype):
    source = jnp.arange(rows_in)[:, None]
    target = jnp.arange(rows_out)[None, :]
    inside = (source >= target) & (source <= target + 2 * HALF)
    return inside.astype(dtype)


def butterfly_sum(x, axis):
    count = lax.axis_size(axis)
    step = 1
    while step < count:
        pairs = [(i, i ^ step) for i in range(count)]
        x = x + lax.ppermute(x, axis, pairs)
        step *= 2
    return x


def ring_sum(x, axis, stride):
    count = lax.axis_size(axis)
    groups = count // stride
    total = x
    for shift in range(1, groups):
        pairs = [
            (i, (i + shift * stride) % count) for i in range(count)
        ]
        total = total + lax.ppermute(x, axis, pairs)
    return total


def pack_symmetric(c):
    h = c.shape[0] // 2
    row = jnp.arange(h)[:, None]
    col = jnp.arange(h)[None, :]
    c11, c12, c22 = c[:h, :h], c[:h, h:], c[h:, h:]
    mixed = jnp.where(col >= row, c11, c22)
    diagonal = jnp.sum(jnp.where(col == row, c22, 0.0), axis=0, keepdims=True)
    return jnp.concatenate([c12, mixed, diagonal], axis=0)


def unpack_symmetric(p):
    h = p.shape[1]
    row = jnp.arange(h)[:, None]
    col = jnp.arange(h)[None, :]
    c12, mixed, d22 = p[:h], p[h:2 * h], p[2 * h]
    c11 = jnp.where(col >= row, mixed, mixed.T)
    c22 = jnp.where(col < row, mixed, mixed.T)
    c22 = jnp.where(col == row, d22[None, :], c22)
    top = jnp.concatenate([c11, c12], axis=1)
    bottom = jnp.concatenate([c12.T, c22], axis=1)
    return jnp.concatenate([top, bottom], axis=0)


def sweep_kernel(n, load, a_ref, o_ref):
    size = o_ref.shape[0]
    rows = lax.broadcasted_iota(jnp.int32, (size, 1), 0)
    lanes = lax.broadcasted_iota(jnp.int32, (1, size), 1)
    o_ref[...] = jnp.where(rows == lanes, 1.0, 0.0).astype(jnp.float32)
    o_ref[:n, :n] = a_ref[...]
    if load:
        on_diagonal = (rows == lanes) & (rows < n)
        full = o_ref[...]
        trace = jnp.sum(jnp.where(on_diagonal, full, 0.0), axis=(0, 1), keepdims=True)
        o_ref[...] = jnp.where(on_diagonal, full + load * (trace / n), full)
    sub8 = lax.broadcasted_iota(jnp.int32, (8, 1), 0)

    def pick(v, j):
        return jnp.sum(jnp.where(lanes == j, v, 0.0), axis=1, keepdims=True)

    def body(m, carry):
        k = 2 * m
        base = pl.multiple_of((k // 8) * 8, 8)
        slab = o_ref[pl.ds(base, 8), :]
        r0 = jnp.sum(jnp.where(sub8 == k - base, slab, 0.0), axis=0, keepdims=True)
        r1 = jnp.sum(jnp.where(sub8 == k + 1 - base, slab, 0.0), axis=0, keepdims=True)
        a00, a01, a11 = pick(r0, k), pick(r0, k + 1), pick(r1, k + 1)
        det = a00 * a11 - a01 * a01
        p00, p01, p11 = a11 / det, -a01 / det, a00 / det
        a = o_ref[...]
        c0 = jnp.sum(jnp.where(lanes == k, a, 0.0), axis=1, keepdims=True)
        c1 = jnp.sum(jnp.where(lanes == k + 1, a, 0.0), axis=1, keepdims=True)
        u0 = c0 * p00 + c1 * p01
        u1 = c0 * p01 + c1 * p11
        s0 = r0 * p00 + r1 * p01
        s1 = r0 * p01 + r1 * p11
        main = a - u0 * r0 - u1 * r1
        row0, row1 = rows == k, rows == k + 1
        col0, col1 = lanes == k, lanes == k + 1
        in_rows = row0 | row1
        in_cols = col0 | col1
        corner = jnp.where(row0, jnp.where(col0, -p00, -p01), jnp.where(col0, -p01, -p11))
        side_cols = jnp.where(col0, u0, u1)
        side_rows = jnp.where(row0, s0, s1)
        edge = jnp.where(in_rows, jnp.where(in_cols, corner, side_rows), side_cols)
        o_ref[...] = jnp.where(in_rows | in_cols, edge, main)
        return carry

    lax.fori_loop(0, n // 2, body, 0)


def spd_inverse(a, load=0.0):
    n = a.shape[0]
    assert n % 2 == 0
    size = -(-n // 128) * 128
    swept = pl.pallas_call(
        functools.partial(sweep_kernel, n, load),
        out_shape=jax.ShapeDtypeStruct((size, size), jnp.float32),
    )(a)
    return -swept[:n, :n]


def window_count(first, local, total):
    index = first + jnp.arange(local)
    upper = jnp.minimum(index + HALF, total - 1)
    lower = jnp.maximum(index - HALF, 0)
    return (upper - lower + 1).astype(jnp.float32)


def sum_pixels(values, width, dtype):
    weights = band_matrix(width + 2 * HALF, width, dtype)
    return jnp.einsum(
        "lqb,qp->lpb", values, weights, precision=None, preferred_element_type=jnp.float32
    )


def sum_lines(values, height, dtype, precision):
    weights = band_matrix(height + 2 * HALF, height, dtype)
    return jnp.einsum(
        "kpb,kl->lpb", values, weights, precision=precision, preferred_element_type=jnp.float32
    )


def neighbour_pairs(n_track, n_cross, dt, dc):
    pairs = []
    for t in range(n_track):
        for c in range(n_cross):
            if 0 <= t + dt < n_track and 0 <= c + dc < n_cross:
                pairs.append(((t + dt) * n_cross + c + dc, t * n_cross + c))
    return pairs


def halos(planes):
    n_track = lax.axis_size("track")
    n_cross = lax.axis_size("cross")
    both = ("track", "cross")

    def fetch(piece, dt, dc):
        if dt == 0:
            pairs = [(c + dc, c) for c in range(n_cross) if 0 <= c + dc < n_cross]
            return lax.ppermute(piece, "cross", pairs)
        if dc == 0:
            pairs = [(t + dt, t) for t in range(n_track) if 0 <= t + dt < n_track]
            return lax.ppermute(piece, "track", pairs)
        return lax.ppermute(piece, both, neighbour_pairs(n_track, n_cross, dt, dc))

    first, last = slice(0, HALF), slice(-HALF, None)
    to_right, to_left, planes = lax.optimization_barrier((planes[last], planes[first], planes))
    sides = {
        "left": fetch(to_right, 0, -1),
        "right": fetch(to_left, 0, 1),
    }
    top = fetch(planes[:, :, last], -1, 0)
    bottom = fetch(planes[:, :, first], 1, 0)
    tops = {
        "left": fetch(top[last], 0, -1),
        "middle": top,
        "right": fetch(top[first], 0, 1),
    }
    bottoms = {
        "left": fetch(bottom[last], 0, -1),
        "middle": bottom,
        "right": fetch(bottom[first], 0, 1),
    }
    return sides, tops, bottoms


def line_weights(lines):
    target = jnp.arange(lines)[None, :]
    middle = jnp.abs(jnp.arange(lines)[:, None] - target) <= HALF
    side = jnp.arange(HALF)[:, None]
    top = target <= side
    bottom = target >= lines - HALF + side
    return [w.astype(jnp.bfloat16) for w in (top, middle, bottom)]


def sum_lines(top, middle, bottom, weights):
    total = None
    for values, w in zip((top, middle, bottom), weights):
        term = jnp.einsum("qbk,kl->qbl", values, w, preferred_element_type=jnp.float32)
        total = term if total is None else total + term
    return total


def residual_kernel(left_ref, middle_ref, right_ref, x_ref, count_ref, out_ref, out_bf_ref):
    refs = [(left_ref, q) for q in range(left_ref.shape[0])]
    refs += [(middle_ref, q) for q in range(middle_ref.shape[0])]
    refs += [(right_ref, q) for q in range(right_ref.shape[0])]

    def plane(q):
        ref, i = refs[q]
        return ref[i]

    def emit(p, running):
        value = x_ref[p].astype(jnp.float32) - running / count_ref[p]
        out_ref[p] = value
        out_bf_ref[p] = value.astype(jnp.bfloat16)

    span = 2 * HALF + 1
    running = plane(0)
    for q in range(1, span):
        running = running + plane(q)
    emit(0, running)
    for p in range(1, out_ref.shape[0]):
        running = running + plane(p + span - 1) - plane(p - 1)
        emit(p, running)


def residuals(left, middle, right, planes, count):
    width, bands, lines = middle.shape
    block = next((b for b in (56, 32, 16, 8) if bands % b == 0), bands)
    spec = lambda n: pl.BlockSpec((n, block, lines), lambda i: (0, i, 0))
    count_spec = pl.BlockSpec((width, 1, lines), lambda i: (0, 0, 0))
    return pl.pallas_call(
        residual_kernel,
        grid=(bands // block,),
        in_specs=[spec(left.shape[0]), spec(width), spec(right.shape[0]), spec(width), count_spec],
        out_specs=[spec(width), spec(width)],
        out_shape=[
            jax.ShapeDtypeStruct((width, bands, lines), jnp.float32),
            jax.ShapeDtypeStruct((width, bands, lines), jnp.bfloat16),
        ],
    )(left, middle, right, planes, count)


def shards(cube):
    lines_dev, pix_dev, bands = cube.shape
    n_track = lax.axis_size("track")
    n_cross = lax.axis_size("cross")
    total_lines = lines_dev * n_track
    total_pix = pix_dev * n_cross
    highest = lax.Precision.HIGHEST
    planes = jnp.transpose(cube, (1, 2, 0))
    sides, tops, bottoms = halos(planes)
    weights = line_weights(lines_dev)
    middle = sum_lines(tops["middle"], planes, bottoms["middle"], weights)
    left = sum_lines(tops["left"], sides["left"], bottoms["left"], weights)
    right = sum_lines(tops["right"], sides["right"], bottoms["right"], weights)
    line_count = window_count(lax.axis_index("track") * lines_dev, lines_dev, total_lines)
    pixel_count = window_count(lax.axis_index("cross") * pix_dev, pix_dev, total_pix)
    count = pixel_count[:, None, None] * line_count[None, None, :]
    residual, residual_bf = residuals(left, middle, right, planes, count)
    partial_cov = jnp.einsum(
        "pjl,pkl->jk", residual_bf, residual_bf, preferred_element_type=jnp.float32
    )
    packed = butterfly_sum(butterfly_sum(pack_symmetric(partial_cov), "cross"), "track")
    covariance = unpack_symmetric(packed) / (total_lines * total_pix)
    inverse = spd_inverse(covariance, LOAD)
    solved = jnp.einsum(
        "pbl,bj->pjl", residual, inverse, precision=highest, preferred_element_type=jnp.float32
    )
    scores = jnp.sum(residual * solved, axis=1) / bands
    return scores.T


def solution(mesh):
    return jax.shard_map(
        shards,
        mesh=mesh,
        in_specs=(P("track", "cross", None),),
        out_specs=P("track", "cross"),
        check_vma=False,
    )
```

```python
import functools

import jax
import jax.numpy as jnp
from jax import lax
from jax.experimental import pallas as pl
from jax.experimental.layout import Layout, with_layout_constraint
from jax.sharding import PartitionSpec as P

HALF = 15


LOAD = 0.02


def with_halo(block, sides, width):
    for axis, dim in sides:
        count = lax.axis_size(axis)
        forward = [(i, i + 1) for i in range(count - 1)]
        backward = [(target, source) for source, target in forward]
        low = lax.ppermute(
            lax.slice_in_dim(block, block.shape[dim] - width, None, axis=dim), axis, forward
        )
        high = lax.ppermute(lax.slice_in_dim(block, 0, width, axis=dim), axis, backward)
        block = jnp.concatenate([low, block, high], axis=dim)
    return block


def band_matrix(rows_in, rows_out, dtype):
    source = jnp.arange(rows_in)[:, None]
    target = jnp.arange(rows_out)[None, :]
    inside = (source >= target) & (source <= target + 2 * HALF)
    return inside.astype(dtype)


def butterfly_sum(x, axis):
    count = lax.axis_size(axis)
    step = 1
    while step < count:
        pairs = [(i, i ^ step) for i in range(count)]
        x = x + lax.ppermute(x, axis, pairs)
        step *= 2
    return x


def ring_sum(x, axis, stride):
    count = lax.axis_size(axis)
    groups = count // stride
    total = x
    for shift in range(1, groups):
        pairs = [
            (i, (i + shift * stride) % count) for i in range(count)
        ]
        total = total + lax.ppermute(x, axis, pairs)
    return total


def pack_symmetric(c):
    h = c.shape[0] // 2
    row = jnp.arange(h)[:, None]
    col = jnp.arange(h)[None, :]
    c11, c12, c22 = c[:h, :h], c[:h, h:], c[h:, h:]
    mixed = jnp.where(col >= row, c11, c22)
    diagonal = jnp.sum(jnp.where(col == row, c22, 0.0), axis=0, keepdims=True)
    return jnp.concatenate([c12, mixed, diagonal], axis=0)


def unpack_symmetric(p):
    h = p.shape[1]
    row = jnp.arange(h)[:, None]
    col = jnp.arange(h)[None, :]
    c12, mixed, d22 = p[:h], p[h:2 * h], p[2 * h]
    c11 = jnp.where(col >= row, mixed, mixed.T)
    c22 = jnp.where(col < row, mixed, mixed.T)
    c22 = jnp.where(col == row, d22[None, :], c22)
    top = jnp.concatenate([c11, c12], axis=1)
    bottom = jnp.concatenate([c12.T, c22], axis=1)
    return jnp.concatenate([top, bottom], axis=0)


def sweep_kernel(n, load, a_ref, o_ref):
    size = o_ref.shape[0]
    rows = lax.broadcasted_iota(jnp.int32, (size, 1), 0)
    lanes = lax.broadcasted_iota(jnp.int32, (1, size), 1)
    o_ref[...] = jnp.where(rows == lanes, 1.0, 0.0).astype(jnp.float32)
    o_ref[:n, :n] = a_ref[...]
    if load:
        on_diagonal = (rows == lanes) & (rows < n)
        full = o_ref[...]
        trace = jnp.sum(jnp.where(on_diagonal, full, 0.0), axis=(0, 1), keepdims=True)
        o_ref[...] = jnp.where(on_diagonal, full + load * (trace / n), full)
    sub8 = lax.broadcasted_iota(jnp.int32, (8, 1), 0)

    def pick(v, j):
        return jnp.sum(jnp.where(lanes == j, v, 0.0), axis=1, keepdims=True)

    def body(m, carry):
        k = 2 * m
        base = pl.multiple_of((k // 8) * 8, 8)
        slab = o_ref[pl.ds(base, 8), :]
        r0 = jnp.sum(jnp.where(sub8 == k - base, slab, 0.0), axis=0, keepdims=True)
        r1 = jnp.sum(jnp.where(sub8 == k + 1 - base, slab, 0.0), axis=0, keepdims=True)
        a00, a01, a11 = pick(r0, k), pick(r0, k + 1), pick(r1, k + 1)
        det = a00 * a11 - a01 * a01
        p00, p01, p11 = a11 / det, -a01 / det, a00 / det
        a = o_ref[...]
        c0 = jnp.sum(jnp.where(lanes == k, a, 0.0), axis=1, keepdims=True)
        c1 = jnp.sum(jnp.where(lanes == k + 1, a, 0.0), axis=1, keepdims=True)
        u0 = c0 * p00 + c1 * p01
        u1 = c0 * p01 + c1 * p11
        s0 = r0 * p00 + r1 * p01
        s1 = r0 * p01 + r1 * p11
        main = a - u0 * r0 - u1 * r1
        row0, row1 = rows == k, rows == k + 1
        col0, col1 = lanes == k, lanes == k + 1
        in_rows = row0 | row1
        in_cols = col0 | col1
        corner = jnp.where(row0, jnp.where(col0, -p00, -p01), jnp.where(col0, -p01, -p11))
        side_cols = jnp.where(col0, u0, u1)
        side_rows = jnp.where(row0, s0, s1)
        edge = jnp.where(in_rows, jnp.where(in_cols, corner, side_rows), side_cols)
        o_ref[...] = jnp.where(in_rows | in_cols, edge, main)
        return carry

    lax.fori_loop(0, n // 2, body, 0)


def spd_inverse(a, load=0.0):
    n = a.shape[0]
    assert n % 2 == 0
    size = -(-n // 128) * 128
    swept = pl.pallas_call(
        functools.partial(sweep_kernel, n, load),
        out_shape=jax.ShapeDtypeStruct((size, size), jnp.float32),
    )(a)
    return -swept[:n, :n]


def window_count(first, local, total):
    index = first + jnp.arange(local)
    upper = jnp.minimum(index + HALF, total - 1)
    lower = jnp.maximum(index - HALF, 0)
    return (upper - lower + 1).astype(jnp.float32)


def sum_pixels(values, width, dtype):
    weights = band_matrix(width + 2 * HALF, width, dtype)
    return jnp.einsum(
        "lqb,qp->lpb", values, weights, precision=None, preferred_element_type=jnp.float32
    )


def sum_lines(values, height, dtype, precision):
    weights = band_matrix(height + 2 * HALF, height, dtype)
    return jnp.einsum(
        "kpb,kl->lpb", values, weights, precision=precision, preferred_element_type=jnp.float32
    )


def neighbour_pairs(n_track, n_cross, dt, dc):
    pairs = []
    for t in range(n_track):
        for c in range(n_cross):
            if 0 <= t + dt < n_track and 0 <= c + dc < n_cross:
                pairs.append(((t + dt) * n_cross + c + dc, t * n_cross + c))
    return pairs


def halos(planes):
    n_track = lax.axis_size("track")
    n_cross = lax.axis_size("cross")
    both = ("track", "cross")

    def fetch(piece, dt, dc):
        if dt == 0:
            pairs = [(c + dc, c) for c in range(n_cross) if 0 <= c + dc < n_cross]
            return lax.ppermute(piece, "cross", pairs)
        if dc == 0:
            pairs = [(t + dt, t) for t in range(n_track) if 0 <= t + dt < n_track]
            return lax.ppermute(piece, "track", pairs)
        return lax.ppermute(piece, both, neighbour_pairs(n_track, n_cross, dt, dc))

    first, last = slice(0, HALF), slice(-HALF, None)
    to_right, to_left, planes = lax.optimization_barrier((planes[last], planes[first], planes))
    sides = {
        "left": fetch(to_right, 0, -1),
        "right": fetch(to_left, 0, 1),
    }
    top = fetch(planes[:, :, last], -1, 0)
    bottom = fetch(planes[:, :, first], 1, 0)
    tops = {
        "left": fetch(top[last], 0, -1),
        "middle": top,
        "right": fetch(top[first], 0, 1),
    }
    bottoms = {
        "left": fetch(bottom[last], 0, -1),
        "middle": bottom,
        "right": fetch(bottom[first], 0, 1),
    }
    return sides, tops, bottoms


def line_weights(lines):
    target = jnp.arange(lines)[None, :]
    middle = jnp.abs(jnp.arange(lines)[:, None] - target) <= HALF
    side = jnp.arange(HALF)[:, None]
    top = target <= side
    bottom = target >= lines - HALF + side
    return [w.astype(jnp.bfloat16) for w in (top, middle, bottom)]


def sum_lines(top, middle, bottom, weights):
    total = None
    for values, w in zip((top, middle, bottom), weights):
        term = jnp.einsum("qbk,kl->qbl", values, w, preferred_element_type=jnp.float32)
        total = term if total is None else total + term
    return total


def residual_kernel(left_ref, middle_ref, right_ref, x_ref, count_ref, out_ref, out_bf_ref):
    refs = [(left_ref, q) for q in range(left_ref.shape[0])]
    refs += [(middle_ref, q) for q in range(middle_ref.shape[0])]
    refs += [(right_ref, q) for q in range(right_ref.shape[0])]

    def plane(q):
        ref, i = refs[q]
        return ref[i]

    def emit(p, running):
        value = x_ref[p].astype(jnp.float32) - running / count_ref[p]
        out_ref[p] = value
        out_bf_ref[p] = value.astype(jnp.bfloat16)

    span = 2 * HALF + 1
    running = plane(0)
    for q in range(1, span):
        running = running + plane(q)
    emit(0, running)
    for p in range(1, out_ref.shape[0]):
        running = running + plane(p + span - 1) - plane(p - 1)
        emit(p, running)


def residuals(left, middle, right, planes, count):
    width, bands, lines = middle.shape
    block = next((b for b in (56, 32, 16, 8) if bands % b == 0), bands)
    spec = lambda n: pl.BlockSpec((n, block, lines), lambda i: (0, i, 0))
    count_spec = pl.BlockSpec((width, 1, lines), lambda i: (0, 0, 0))
    return pl.pallas_call(
        residual_kernel,
        grid=(bands // block,),
        in_specs=[spec(left.shape[0]), spec(width), spec(right.shape[0]), spec(width), count_spec],
        out_specs=[spec(width), spec(width)],
        out_shape=[
            jax.ShapeDtypeStruct((width, bands, lines), jnp.float32),
            jax.ShapeDtypeStruct((width, bands, lines), jnp.bfloat16),
        ],
    )(left, middle, right, planes, count)


def shards(cube):
    lines_dev, pix_dev, bands = cube.shape
    n_track = lax.axis_size("track")
    n_cross = lax.axis_size("cross")
    total_lines = lines_dev * n_track
    total_pix = pix_dev * n_cross
    highest = lax.Precision.HIGHEST
    planes = jnp.transpose(cube, (1, 2, 0))
    sides, tops, bottoms = halos(planes)
    weights = line_weights(lines_dev)
    middle = sum_lines(tops["middle"], planes, bottoms["middle"], weights)
    left = sum_lines(tops["left"], sides["left"], bottoms["left"], weights)
    right = sum_lines(tops["right"], sides["right"], bottoms["right"], weights)
    line_count = window_count(lax.axis_index("track") * lines_dev, lines_dev, total_lines)
    pixel_count = window_count(lax.axis_index("cross") * pix_dev, pix_dev, total_pix)
    count = pixel_count[:, None, None] * line_count[None, None, :]
    residual, residual_bf = residuals(left, middle, right, planes, count)
    partial_cov = jnp.einsum(
        "pjl,pkl->jk", residual_bf, residual_bf, preferred_element_type=jnp.float32
    )
    packed = pack_symmetric(partial_cov)
    packed = packed + lax.ppermute(packed, "cross", [(i, i ^ 1) for i in range(n_cross)])
    packed = butterfly_sum(ring_sum(packed, "cross", 2), "track")
    covariance = unpack_symmetric(packed) / (total_lines * total_pix)
    inverse = spd_inverse(covariance, LOAD)
    solved = jnp.einsum(
        "jb,pbl->pjl", inverse.T, residual, precision=highest, preferred_element_type=jnp.float32
    )
    scores = jnp.sum(residual * solved, axis=1) / bands
    return scores.T


def solution(mesh):
    return jax.shard_map(
        shards,
        mesh=mesh,
        in_specs=(P("track", "cross", None),),
        out_specs=P("track", "cross"),
        check_vma=False,
    )
```

```python
import functools

import jax
import jax.numpy as jnp
from jax import lax
from jax.experimental import pallas as pl
from jax.experimental.layout import Layout, with_layout_constraint
from jax.sharding import PartitionSpec as P

HALF = 15


LOAD = 0.02


def with_halo(block, sides, width):
    for axis, dim in sides:
        count = lax.axis_size(axis)
        forward = [(i, i + 1) for i in range(count - 1)]
        backward = [(target, source) for source, target in forward]
        low = lax.ppermute(
            lax.slice_in_dim(block, block.shape[dim] - width, None, axis=dim), axis, forward
        )
        high = lax.ppermute(lax.slice_in_dim(block, 0, width, axis=dim), axis, backward)
        block = jnp.concatenate([low, block, high], axis=dim)
    return block


def band_matrix(rows_in, rows_out, dtype):
    source = jnp.arange(rows_in)[:, None]
    target = jnp.arange(rows_out)[None, :]
    inside = (source >= target) & (source <= target + 2 * HALF)
    return inside.astype(dtype)


def butterfly_sum(x, axis):
    count = lax.axis_size(axis)
    step = 1
    while step < count:
        pairs = [(i, i ^ step) for i in range(count)]
        x = x + lax.ppermute(x, axis, pairs)
        step *= 2
    return x


def ring_sum(x, axis, stride):
    count = lax.axis_size(axis)
    groups = count // stride
    total = x
    for shift in range(1, groups):
        pairs = [
            (i, (i + shift * stride) % count) for i in range(count)
        ]
        total = total + lax.ppermute(x, axis, pairs)
    return total


def pack_symmetric(c):
    h = c.shape[0] // 2
    row = jnp.arange(h)[:, None]
    col = jnp.arange(h)[None, :]
    c11, c12, c22 = c[:h, :h], c[:h, h:], c[h:, h:]
    mixed = jnp.where(col >= row, c11, c22)
    diagonal = jnp.sum(jnp.where(col == row, c22, 0.0), axis=0, keepdims=True)
    return jnp.concatenate([c12, mixed, diagonal], axis=0)


def unpack_symmetric(p):
    h = p.shape[1]
    row = jnp.arange(h)[:, None]
    col = jnp.arange(h)[None, :]
    c12, mixed, d22 = p[:h], p[h:2 * h], p[2 * h]
    c11 = jnp.where(col >= row, mixed, mixed.T)
    c22 = jnp.where(col < row, mixed, mixed.T)
    c22 = jnp.where(col == row, d22[None, :], c22)
    top = jnp.concatenate([c11, c12], axis=1)
    bottom = jnp.concatenate([c12.T, c22], axis=1)
    return jnp.concatenate([top, bottom], axis=0)


def sweep_kernel(n, load, a_ref, o_ref):
    size = o_ref.shape[0]
    rows = lax.broadcasted_iota(jnp.int32, (size, 1), 0)
    lanes = lax.broadcasted_iota(jnp.int32, (1, size), 1)
    o_ref[...] = jnp.where(rows == lanes, 1.0, 0.0).astype(jnp.float32)
    o_ref[:n, :n] = a_ref[...]
    if load:
        on_diagonal = (rows == lanes) & (rows < n)
        full = o_ref[...]
        trace = jnp.sum(jnp.where(on_diagonal, full, 0.0), axis=(0, 1), keepdims=True)
        o_ref[...] = jnp.where(on_diagonal, full + load * (trace / n), full)
    sub8 = lax.broadcasted_iota(jnp.int32, (8, 1), 0)

    def pick(v, j):
        return jnp.sum(jnp.where(lanes == j, v, 0.0), axis=1, keepdims=True)

    def body(m, carry):
        k = 2 * m
        base = pl.multiple_of((k // 8) * 8, 8)
        slab = o_ref[pl.ds(base, 8), :]
        r0 = jnp.sum(jnp.where(sub8 == k - base, slab, 0.0), axis=0, keepdims=True)
        r1 = jnp.sum(jnp.where(sub8 == k + 1 - base, slab, 0.0), axis=0, keepdims=True)
        a00, a01, a11 = pick(r0, k), pick(r0, k + 1), pick(r1, k + 1)
        det = a00 * a11 - a01 * a01
        p00, p01, p11 = a11 / det, -a01 / det, a00 / det
        a = o_ref[...]
        c0 = jnp.sum(jnp.where(lanes == k, a, 0.0), axis=1, keepdims=True)
        c1 = jnp.sum(jnp.where(lanes == k + 1, a, 0.0), axis=1, keepdims=True)
        u0 = c0 * p00 + c1 * p01
        u1 = c0 * p01 + c1 * p11
        s0 = r0 * p00 + r1 * p01
        s1 = r0 * p01 + r1 * p11
        main = a - u0 * r0 - u1 * r1
        row0, row1 = rows == k, rows == k + 1
        col0, col1 = lanes == k, lanes == k + 1
        in_rows = row0 | row1
        in_cols = col0 | col1
        corner = jnp.where(row0, jnp.where(col0, -p00, -p01), jnp.where(col0, -p01, -p11))
        side_cols = jnp.where(col0, u0, u1)
        side_rows = jnp.where(row0, s0, s1)
        edge = jnp.where(in_rows, jnp.where(in_cols, corner, side_rows), side_cols)
        o_ref[...] = jnp.where(in_rows | in_cols, edge, main)
        return carry

    lax.fori_loop(0, n // 2, body, 0)


def spd_inverse(a, load=0.0):
    n = a.shape[0]
    assert n % 2 == 0
    size = -(-n // 128) * 128
    swept = pl.pallas_call(
        functools.partial(sweep_kernel, n, load),
        out_shape=jax.ShapeDtypeStruct((size, size), jnp.float32),
    )(a)
    return -swept[:n, :n]


def window_count(first, local, total):
    index = first + jnp.arange(local)
    upper = jnp.minimum(index + HALF, total - 1)
    lower = jnp.maximum(index - HALF, 0)
    return (upper - lower + 1).astype(jnp.float32)


def sum_pixels(values, width, dtype):
    weights = band_matrix(width + 2 * HALF, width, dtype)
    return jnp.einsum(
        "lqb,qp->lpb", values, weights, precision=None, preferred_element_type=jnp.float32
    )


def sum_lines(values, height, dtype, precision):
    weights = band_matrix(height + 2 * HALF, height, dtype)
    return jnp.einsum(
        "kpb,kl->lpb", values, weights, precision=precision, preferred_element_type=jnp.float32
    )


def neighbour_pairs(n_track, n_cross, dt, dc):
    pairs = []
    for t in range(n_track):
        for c in range(n_cross):
            if 0 <= t + dt < n_track and 0 <= c + dc < n_cross:
                pairs.append(((t + dt) * n_cross + c + dc, t * n_cross + c))
    return pairs


def halos(planes):
    n_track = lax.axis_size("track")
    n_cross = lax.axis_size("cross")
    both = ("track", "cross")

    def fetch(piece, dt, dc):
        if dt == 0:
            pairs = [(c + dc, c) for c in range(n_cross) if 0 <= c + dc < n_cross]
            return lax.ppermute(piece, "cross", pairs)
        if dc == 0:
            pairs = [(t + dt, t) for t in range(n_track) if 0 <= t + dt < n_track]
            return lax.ppermute(piece, "track", pairs)
        return lax.ppermute(piece, both, neighbour_pairs(n_track, n_cross, dt, dc))

    first, last = slice(0, HALF), slice(-HALF, None)
    to_right, to_left, planes = lax.optimization_barrier((planes[last], planes[first], planes))
    sides = {
        "left": fetch(to_right, 0, -1),
        "right": fetch(to_left, 0, 1),
    }
    top = fetch(planes[:, :, last], -1, 0)
    bottom = fetch(planes[:, :, first], 1, 0)
    tops = {
        "left": fetch(top[last], 0, -1),
        "middle": top,
        "right": fetch(top[first], 0, 1),
    }
    bottoms = {
        "left": fetch(bottom[last], 0, -1),
        "middle": bottom,
        "right": fetch(bottom[first], 0, 1),
    }
    return sides, tops, bottoms


def line_weights(lines):
    target = jnp.arange(lines)[None, :]
    middle = jnp.abs(jnp.arange(lines)[:, None] - target) <= HALF
    side = jnp.arange(HALF)[:, None]
    top = target <= side
    bottom = target >= lines - HALF + side
    return [w.astype(jnp.bfloat16) for w in (top, middle, bottom)]


def sum_lines(top, middle, bottom, weights):
    total = None
    for values, w in zip((top, middle, bottom), weights):
        term = jnp.einsum("qbk,kl->qbl", values, w, preferred_element_type=jnp.float32)
        total = term if total is None else total + term
    return total


def residual_kernel(left_ref, middle_ref, right_ref, x_ref, count_ref, out_ref):
    refs = [(left_ref, q) for q in range(left_ref.shape[0])]
    refs += [(middle_ref, q) for q in range(middle_ref.shape[0])]
    refs += [(right_ref, q) for q in range(right_ref.shape[0])]

    def plane(q):
        ref, i = refs[q]
        return ref[i]

    def emit(p, running):
        value = x_ref[p].astype(jnp.float32) - running / count_ref[p]
        out_ref[p] = value

    span = 2 * HALF + 1
    running = plane(0)
    for q in range(1, span):
        running = running + plane(q)
    emit(0, running)
    for p in range(1, out_ref.shape[0]):
        running = running + plane(p + span - 1) - plane(p - 1)
        emit(p, running)


def residuals(left, middle, right, planes, count):
    width, bands, lines = middle.shape
    block = next((b for b in (56, 32, 16, 8) if bands % b == 0), bands)
    spec = lambda n: pl.BlockSpec((n, block, lines), lambda i: (0, i, 0))
    count_spec = pl.BlockSpec((width, 1, lines), lambda i: (0, 0, 0))
    return pl.pallas_call(
        residual_kernel,
        grid=(bands // block,),
        in_specs=[spec(left.shape[0]), spec(width), spec(right.shape[0]), spec(width), count_spec],
        out_specs=spec(width),
        out_shape=jax.ShapeDtypeStruct((width, bands, lines), jnp.float32),
    )(left, middle, right, planes, count)


def shards(cube):
    lines_dev, pix_dev, bands = cube.shape
    n_track = lax.axis_size("track")
    n_cross = lax.axis_size("cross")
    total_lines = lines_dev * n_track
    total_pix = pix_dev * n_cross
    highest = lax.Precision.HIGHEST
    planes = jnp.transpose(cube, (1, 2, 0))
    sides, tops, bottoms = halos(planes)
    weights = line_weights(lines_dev)
    middle = sum_lines(tops["middle"], planes, bottoms["middle"], weights)
    left = sum_lines(tops["left"], sides["left"], bottoms["left"], weights)
    right = sum_lines(tops["right"], sides["right"], bottoms["right"], weights)
    line_count = window_count(lax.axis_index("track") * lines_dev, lines_dev, total_lines)
    pixel_count = window_count(lax.axis_index("cross") * pix_dev, pix_dev, total_pix)
    count = pixel_count[:, None, None] * line_count[None, None, :]
    residual = residuals(left, middle, right, planes, count)
    residual_bf = residual.astype(jnp.bfloat16)
    partial_cov = jnp.einsum(
        "pjl,pkl->jk", residual_bf, residual_bf, preferred_element_type=jnp.float32
    )
    packed = pack_symmetric(partial_cov)
    packed = packed + lax.ppermute(packed, "cross", [(i, i ^ 1) for i in range(n_cross)])
    packed = butterfly_sum(ring_sum(packed, "cross", 2), "track")
    covariance = unpack_symmetric(packed) / (total_lines * total_pix)
    inverse = spd_inverse(covariance, LOAD)
    solved = jnp.einsum(
        "jb,pbl->pjl", inverse.T, residual, precision=highest, preferred_element_type=jnp.float32
    )
    scores = jnp.sum(residual * solved, axis=1) / bands
    return scores.T


def solution(mesh):
    return jax.shard_map(
        shards,
        mesh=mesh,
        in_specs=(P("track", "cross", None),),
        out_specs=P("track", "cross"),
        check_vma=False,
    )
```

```python
import functools

import jax
import jax.numpy as jnp
from jax import lax
from jax.experimental import pallas as pl
from jax.experimental.layout import Layout, with_layout_constraint
from jax.sharding import PartitionSpec as P

HALF = 15


LOAD = 0.02


def with_halo(block, sides, width):
    for axis, dim in sides:
        count = lax.axis_size(axis)
        forward = [(i, i + 1) for i in range(count - 1)]
        backward = [(target, source) for source, target in forward]
        low = lax.ppermute(
            lax.slice_in_dim(block, block.shape[dim] - width, None, axis=dim), axis, forward
        )
        high = lax.ppermute(lax.slice_in_dim(block, 0, width, axis=dim), axis, backward)
        block = jnp.concatenate([low, block, high], axis=dim)
    return block


def band_matrix(rows_in, rows_out, dtype):
    source = jnp.arange(rows_in)[:, None]
    target = jnp.arange(rows_out)[None, :]
    inside = (source >= target) & (source <= target + 2 * HALF)
    return inside.astype(dtype)


def butterfly_sum(x, axis):
    count = lax.axis_size(axis)
    step = 1
    while step < count:
        pairs = [(i, i ^ step) for i in range(count)]
        x = x + lax.ppermute(x, axis, pairs)
        step *= 2
    return x


def ring_sum(x, axis, stride):
    count = lax.axis_size(axis)
    groups = count // stride
    total = x
    for shift in range(1, groups):
        pairs = [
            (i, (i + shift * stride) % count) for i in range(count)
        ]
        total = total + lax.ppermute(x, axis, pairs)
    return total


def pack_symmetric(c):
    h = c.shape[0] // 2
    row = jnp.arange(h)[:, None]
    col = jnp.arange(h)[None, :]
    c11, c12, c22 = c[:h, :h], c[:h, h:], c[h:, h:]
    mixed = jnp.where(col >= row, c11, c22)
    diagonal = jnp.sum(jnp.where(col == row, c22, 0.0), axis=0, keepdims=True)
    return jnp.concatenate([c12, mixed, diagonal], axis=0)


def unpack_symmetric(p):
    h = p.shape[1]
    row = jnp.arange(h)[:, None]
    col = jnp.arange(h)[None, :]
    c12, mixed, d22 = p[:h], p[h:2 * h], p[2 * h]
    c11 = jnp.where(col >= row, mixed, mixed.T)
    c22 = jnp.where(col < row, mixed, mixed.T)
    c22 = jnp.where(col == row, d22[None, :], c22)
    top = jnp.concatenate([c11, c12], axis=1)
    bottom = jnp.concatenate([c12.T, c22], axis=1)
    return jnp.concatenate([top, bottom], axis=0)


def sweep_kernel(n, load, a_ref, o_ref):
    size = o_ref.shape[0]
    rows = lax.broadcasted_iota(jnp.int32, (size, 1), 0)
    lanes = lax.broadcasted_iota(jnp.int32, (1, size), 1)
    o_ref[...] = jnp.where(rows == lanes, 1.0, 0.0).astype(jnp.float32)
    o_ref[:n, :n] = a_ref[...]
    if load:
        on_diagonal = (rows == lanes) & (rows < n)
        full = o_ref[...]
        trace = jnp.sum(jnp.where(on_diagonal, full, 0.0), axis=(0, 1), keepdims=True)
        o_ref[...] = jnp.where(on_diagonal, full + load * (trace / n), full)
    sub8 = lax.broadcasted_iota(jnp.int32, (8, 1), 0)

    def pick(v, j):
        return jnp.sum(jnp.where(lanes == j, v, 0.0), axis=1, keepdims=True)

    def body(m, carry):
        k = 2 * m
        base = pl.multiple_of((k // 8) * 8, 8)
        slab = o_ref[pl.ds(base, 8), :]
        r0 = jnp.sum(jnp.where(sub8 == k - base, slab, 0.0), axis=0, keepdims=True)
        r1 = jnp.sum(jnp.where(sub8 == k + 1 - base, slab, 0.0), axis=0, keepdims=True)
        a00, a01, a11 = pick(r0, k), pick(r0, k + 1), pick(r1, k + 1)
        det = a00 * a11 - a01 * a01
        p00, p01, p11 = a11 / det, -a01 / det, a00 / det
        a = o_ref[...]
        start = pl.multiple_of((k // 128) * 128, 128)
        tile = o_ref[:, pl.ds(start, 128)]
        tile_lanes = lax.broadcasted_iota(jnp.int32, (1, 128), 1) + start
        c0 = jnp.sum(jnp.where(tile_lanes == k, tile, 0.0), axis=1, keepdims=True)
        c1 = jnp.sum(jnp.where(tile_lanes == k + 1, tile, 0.0), axis=1, keepdims=True)
        u0 = c0 * p00 + c1 * p01
        u1 = c0 * p01 + c1 * p11
        s0 = r0 * p00 + r1 * p01
        s1 = r0 * p01 + r1 * p11
        main = a - u0 * r0 - u1 * r1
        row0, row1 = rows == k, rows == k + 1
        col0, col1 = lanes == k, lanes == k + 1
        in_rows = row0 | row1
        in_cols = col0 | col1
        corner = jnp.where(row0, jnp.where(col0, -p00, -p01), jnp.where(col0, -p01, -p11))
        side_cols = jnp.where(col0, u0, u1)
        side_rows = jnp.where(row0, s0, s1)
        edge = jnp.where(in_rows, jnp.where(in_cols, corner, side_rows), side_cols)
        o_ref[...] = jnp.where(in_rows | in_cols, edge, main)
        return carry

    lax.fori_loop(0, n // 2, body, 0)


def spd_inverse(a, load=0.0):
    n = a.shape[0]
    assert n % 2 == 0
    size = -(-n // 128) * 128
    swept = pl.pallas_call(
        functools.partial(sweep_kernel, n, load),
        out_shape=jax.ShapeDtypeStruct((size, size), jnp.float32),
    )(a)
    return -swept[:n, :n]


def window_count(first, local, total):
    index = first + jnp.arange(local)
    upper = jnp.minimum(index + HALF, total - 1)
    lower = jnp.maximum(index - HALF, 0)
    return (upper - lower + 1).astype(jnp.float32)


def sum_pixels(values, width, dtype):
    weights = band_matrix(width + 2 * HALF, width, dtype)
    return jnp.einsum(
        "lqb,qp->lpb", values, weights, precision=None, preferred_element_type=jnp.float32
    )


def sum_lines(values, height, dtype, precision):
    weights = band_matrix(height + 2 * HALF, height, dtype)
    return jnp.einsum(
        "kpb,kl->lpb", values, weights, precision=precision, preferred_element_type=jnp.float32
    )


def neighbour_pairs(n_track, n_cross, dt, dc):
    pairs = []
    for t in range(n_track):
        for c in range(n_cross):
            if 0 <= t + dt < n_track and 0 <= c + dc < n_cross:
                pairs.append(((t + dt) * n_cross + c + dc, t * n_cross + c))
    return pairs


def halos(planes):
    n_track = lax.axis_size("track")
    n_cross = lax.axis_size("cross")
    both = ("track", "cross")

    def fetch(piece, dt, dc):
        if dt == 0:
            pairs = [(c + dc, c) for c in range(n_cross) if 0 <= c + dc < n_cross]
            return lax.ppermute(piece, "cross", pairs)
        if dc == 0:
            pairs = [(t + dt, t) for t in range(n_track) if 0 <= t + dt < n_track]
            return lax.ppermute(piece, "track", pairs)
        return lax.ppermute(piece, both, neighbour_pairs(n_track, n_cross, dt, dc))

    first, last = slice(0, HALF), slice(-HALF, None)
    to_right, to_left, planes = lax.optimization_barrier((planes[last], planes[first], planes))
    sides = {
        "left": fetch(to_right, 0, -1),
        "right": fetch(to_left, 0, 1),
    }
    top = fetch(planes[:, :, last], -1, 0)
    bottom = fetch(planes[:, :, first], 1, 0)
    tops = {
        "left": fetch(top[last], 0, -1),
        "middle": top,
        "right": fetch(top[first], 0, 1),
    }
    bottoms = {
        "left": fetch(bottom[last], 0, -1),
        "middle": bottom,
        "right": fetch(bottom[first], 0, 1),
    }
    return sides, tops, bottoms


def line_weights(lines):
    target = jnp.arange(lines)[None, :]
    middle = jnp.abs(jnp.arange(lines)[:, None] - target) <= HALF
    side = jnp.arange(HALF)[:, None]
    top = target <= side
    bottom = target >= lines - HALF + side
    return [w.astype(jnp.bfloat16) for w in (top, middle, bottom)]


def sum_lines(top, middle, bottom, weights):
    total = None
    for values, w in zip((top, middle, bottom), weights):
        term = jnp.einsum("qbk,kl->qbl", values, w, preferred_element_type=jnp.float32)
        total = term if total is None else total + term
    return total


def residual_kernel(left_ref, middle_ref, right_ref, x_ref, count_ref, out_ref, out_bf_ref):
    refs = [(left_ref, q) for q in range(left_ref.shape[0])]
    refs += [(middle_ref, q) for q in range(middle_ref.shape[0])]
    refs += [(right_ref, q) for q in range(right_ref.shape[0])]

    def plane(q):
        ref, i = refs[q]
        return ref[i]

    def emit(p, running):
        value = x_ref[p].astype(jnp.float32) - running / count_ref[p]
        out_ref[p] = value
        out_bf_ref[p] = value.astype(jnp.bfloat16)

    span = 2 * HALF + 1
    running = plane(0)
    for q in range(1, span):
        running = running + plane(q)
    emit(0, running)
    for p in range(1, out_ref.shape[0]):
        running = running + plane(p + span - 1) - plane(p - 1)
        emit(p, running)


def residuals(left, middle, right, planes, count):
    width, bands, lines = middle.shape
    block = next((b for b in (56, 32, 16, 8) if bands % b == 0), bands)
    spec = lambda n: pl.BlockSpec((n, block, lines), lambda i: (0, i, 0))
    count_spec = pl.BlockSpec((width, 1, lines), lambda i: (0, 0, 0))
    return pl.pallas_call(
        residual_kernel,
        grid=(bands // block,),
        in_specs=[spec(left.shape[0]), spec(width), spec(right.shape[0]), spec(width), count_spec],
        out_specs=[spec(width), spec(width)],
        out_shape=[
            jax.ShapeDtypeStruct((width, bands, lines), jnp.float32),
            jax.ShapeDtypeStruct((width, bands, lines), jnp.bfloat16),
        ],
    )(left, middle, right, planes, count)


def shards(cube):
    lines_dev, pix_dev, bands = cube.shape
    n_track = lax.axis_size("track")
    n_cross = lax.axis_size("cross")
    total_lines = lines_dev * n_track
    total_pix = pix_dev * n_cross
    highest = lax.Precision.HIGHEST
    planes = jnp.transpose(cube, (1, 2, 0))
    sides, tops, bottoms = halos(planes)
    weights = line_weights(lines_dev)
    middle = sum_lines(tops["middle"], planes, bottoms["middle"], weights)
    left = sum_lines(tops["left"], sides["left"], bottoms["left"], weights)
    right = sum_lines(tops["right"], sides["right"], bottoms["right"], weights)
    line_count = window_count(lax.axis_index("track") * lines_dev, lines_dev, total_lines)
    pixel_count = window_count(lax.axis_index("cross") * pix_dev, pix_dev, total_pix)
    count = pixel_count[:, None, None] * line_count[None, None, :]
    residual, residual_bf = residuals(left, middle, right, planes, count)
    partial_cov = jnp.einsum(
        "pjl,pkl->jk", residual_bf, residual_bf, preferred_element_type=jnp.float32
    )
    packed = pack_symmetric(partial_cov)
    packed = packed + lax.ppermute(packed, "cross", [(i, i ^ 1) for i in range(n_cross)])
    packed = butterfly_sum(ring_sum(packed, "cross", 2), "track")
    covariance = unpack_symmetric(packed) / (total_lines * total_pix)
    inverse = spd_inverse(covariance, LOAD)
    solved = jnp.einsum(
        "jb,pbl->pjl", inverse.T, residual, precision=highest, preferred_element_type=jnp.float32
    )
    scores = jnp.sum(residual * solved, axis=1) / bands
    return scores.T


def solution(mesh):
    return jax.shard_map(
        shards,
        mesh=mesh,
        in_specs=(P("track", "cross", None),),
        out_specs=P("track", "cross"),
        check_vma=False,
    )
```

```python
import functools

import jax
import jax.numpy as jnp
from jax import lax
from jax.experimental import pallas as pl
from jax.experimental.layout import Layout, with_layout_constraint
from jax.sharding import PartitionSpec as P

HALF = 15


LOAD = 0.02


def with_halo(block, sides, width):
    for axis, dim in sides:
        count = lax.axis_size(axis)
        forward = [(i, i + 1) for i in range(count - 1)]
        backward = [(target, source) for source, target in forward]
        low = lax.ppermute(
            lax.slice_in_dim(block, block.shape[dim] - width, None, axis=dim), axis, forward
        )
        high = lax.ppermute(lax.slice_in_dim(block, 0, width, axis=dim), axis, backward)
        block = jnp.concatenate([low, block, high], axis=dim)
    return block


def band_matrix(rows_in, rows_out, dtype):
    source = jnp.arange(rows_in)[:, None]
    target = jnp.arange(rows_out)[None, :]
    inside = (source >= target) & (source <= target + 2 * HALF)
    return inside.astype(dtype)


def butterfly_sum(x, axis):
    count = lax.axis_size(axis)
    step = 1
    while step < count:
        pairs = [(i, i ^ step) for i in range(count)]
        x = x + lax.ppermute(x, axis, pairs)
        step *= 2
    return x


def ring_sum(x, axis, stride):
    count = lax.axis_size(axis)
    groups = count // stride
    total = x
    for shift in range(1, groups):
        pairs = [
            (i, (i + shift * stride) % count) for i in range(count)
        ]
        total = total + lax.ppermute(x, axis, pairs)
    return total


def pack_symmetric(c):
    h = c.shape[0] // 2
    row = jnp.arange(h)[:, None]
    col = jnp.arange(h)[None, :]
    c11, c12, c22 = c[:h, :h], c[:h, h:], c[h:, h:]
    mixed = jnp.where(col >= row, c11, c22)
    diagonal = jnp.sum(jnp.where(col == row, c22, 0.0), axis=0, keepdims=True)
    return jnp.concatenate([c12, mixed, diagonal], axis=0)


def unpack_symmetric(p):
    h = p.shape[1]
    row = jnp.arange(h)[:, None]
    col = jnp.arange(h)[None, :]
    c12, mixed, d22 = p[:h], p[h:2 * h], p[2 * h]
    c11 = jnp.where(col >= row, mixed, mixed.T)
    c22 = jnp.where(col < row, mixed, mixed.T)
    c22 = jnp.where(col == row, d22[None, :], c22)
    top = jnp.concatenate([c11, c12], axis=1)
    bottom = jnp.concatenate([c12.T, c22], axis=1)
    return jnp.concatenate([top, bottom], axis=0)


def sweep_kernel(n, load, a_ref, o_ref):
    size = o_ref.shape[0]
    rows = lax.broadcasted_iota(jnp.int32, (size, 1), 0)
    lanes = lax.broadcasted_iota(jnp.int32, (1, size), 1)
    o_ref[...] = jnp.where(rows == lanes, 1.0, 0.0).astype(jnp.float32)
    o_ref[:n, :n] = a_ref[...]
    if load:
        on_diagonal = (rows == lanes) & (rows < n)
        full = o_ref[...]
        trace = jnp.sum(jnp.where(on_diagonal, full, 0.0), axis=(0, 1), keepdims=True)
        o_ref[...] = jnp.where(on_diagonal, full + load * (trace / n), full)
    sub8 = lax.broadcasted_iota(jnp.int32, (8, 1), 0)

    def pick(v, j):
        return jnp.sum(jnp.where(lanes == j, v, 0.0), axis=1, keepdims=True)

    def body(m, carry):
        k = 2 * m
        base = pl.multiple_of((k // 8) * 8, 8)
        slab = o_ref[pl.ds(base, 8), :]
        r0 = jnp.sum(jnp.where(sub8 == k - base, slab, 0.0), axis=0, keepdims=True)
        r1 = jnp.sum(jnp.where(sub8 == k + 1 - base, slab, 0.0), axis=0, keepdims=True)
        a00, a01, a11 = pick(r0, k), pick(r0, k + 1), pick(r1, k + 1)
        det = a00 * a11 - a01 * a01
        p00, p01, p11 = a11 / det, -a01 / det, a00 / det
        a = o_ref[...]
        c0 = jnp.sum(jnp.where(lanes == k, a, 0.0), axis=1, keepdims=True)
        c1 = jnp.sum(jnp.where(lanes == k + 1, a, 0.0), axis=1, keepdims=True)
        u0 = c0 * p00 + c1 * p01
        u1 = c0 * p01 + c1 * p11
        s0 = r0 * p00 + r1 * p01
        s1 = r0 * p01 + r1 * p11
        main = a - u0 * r0 - u1 * r1
        row0, row1 = rows == k, rows == k + 1
        col0, col1 = lanes == k, lanes == k + 1
        in_rows = row0 | row1
        in_cols = col0 | col1
        corner = jnp.where(row0, jnp.where(col0, -p00, -p01), jnp.where(col0, -p01, -p11))
        side_cols = jnp.where(col0, u0, u1)
        side_rows = jnp.where(row0, s0, s1)
        edge = jnp.where(in_rows, jnp.where(in_cols, corner, side_rows), side_cols)
        o_ref[...] = jnp.where(in_rows | in_cols, edge, main)
        return carry

    lax.fori_loop(0, n // 2, body, 0)


def spd_inverse(a, load=0.0):
    n = a.shape[0]
    assert n % 2 == 0
    size = -(-n // 128) * 128
    swept = pl.pallas_call(
        functools.partial(sweep_kernel, n, load),
        out_shape=jax.ShapeDtypeStruct((size, size), jnp.float32),
    )(a)
    return -swept[:n, :n]


def window_count(first, local, total):
    index = first + jnp.arange(local)
    upper = jnp.minimum(index + HALF, total - 1)
    lower = jnp.maximum(index - HALF, 0)
    return (upper - lower + 1).astype(jnp.float32)


def sum_pixels(values, width, dtype):
    weights = band_matrix(width + 2 * HALF, width, dtype)
    return jnp.einsum(
        "lqb,qp->lpb", values, weights, precision=None, preferred_element_type=jnp.float32
    )


def sum_lines(values, height, dtype, precision):
    weights = band_matrix(height + 2 * HALF, height, dtype)
    return jnp.einsum(
        "kpb,kl->lpb", values, weights, precision=precision, preferred_element_type=jnp.float32
    )


def neighbour_pairs(n_track, n_cross, dt, dc):
    pairs = []
    for t in range(n_track):
        for c in range(n_cross):
            if 0 <= t + dt < n_track and 0 <= c + dc < n_cross:
                pairs.append(((t + dt) * n_cross + c + dc, t * n_cross + c))
    return pairs


def halos(planes):
    n_track = lax.axis_size("track")
    n_cross = lax.axis_size("cross")
    both = ("track", "cross")

    def fetch(piece, dt, dc):
        if dt == 0:
            pairs = [(c + dc, c) for c in range(n_cross) if 0 <= c + dc < n_cross]
            return lax.ppermute(piece, "cross", pairs)
        if dc == 0:
            pairs = [(t + dt, t) for t in range(n_track) if 0 <= t + dt < n_track]
            return lax.ppermute(piece, "track", pairs)
        return lax.ppermute(piece, both, neighbour_pairs(n_track, n_cross, dt, dc))

    first, last = slice(0, HALF), slice(-HALF, None)
    to_right, to_left, planes = lax.optimization_barrier((planes[last], planes[first], planes))
    sides = {
        "left": fetch(to_right, 0, -1),
        "right": fetch(to_left, 0, 1),
    }
    top = fetch(planes[:, :, last], -1, 0)
    bottom = fetch(planes[:, :, first], 1, 0)
    tops = {
        "left": fetch(top[last], 0, -1),
        "middle": top,
        "right": fetch(top[first], 0, 1),
    }
    bottoms = {
        "left": fetch(bottom[last], 0, -1),
        "middle": bottom,
        "right": fetch(bottom[first], 0, 1),
    }
    return sides, tops, bottoms


def line_weights(lines):
    target = jnp.arange(lines)[None, :]
    middle = jnp.abs(jnp.arange(lines)[:, None] - target) <= HALF
    side = jnp.arange(HALF)[:, None]
    top = target <= side
    bottom = target >= lines - HALF + side
    return [w.astype(jnp.bfloat16) for w in (top, middle, bottom)]


def sum_lines(top, middle, bottom, weights):
    total = None
    for values, w in zip((top, middle, bottom), weights):
        term = jnp.einsum("qbk,kl->qbl", values, w, preferred_element_type=jnp.float32)
        total = term if total is None else total + term
    return total


def residual_kernel(left_ref, middle_ref, right_ref, x_ref, count_ref, out_ref, out_bf_ref):
    refs = [(left_ref, q) for q in range(left_ref.shape[0])]
    refs += [(middle_ref, q) for q in range(middle_ref.shape[0])]
    refs += [(right_ref, q) for q in range(right_ref.shape[0])]

    def plane(q):
        ref, i = refs[q]
        return ref[i]

    def emit(p, running):
        value = x_ref[p].astype(jnp.float32) - running / count_ref[p]
        out_ref[p] = value
        out_bf_ref[p] = value.astype(jnp.bfloat16)

    span = 2 * HALF + 1
    running = plane(0)
    for q in range(1, span):
        running = running + plane(q)
    emit(0, running)
    for p in range(1, out_ref.shape[0]):
        running = running + plane(p + span - 1) - plane(p - 1)
        emit(p, running)


def residuals(left, middle, right, planes, count):
    width, bands, lines = middle.shape
    block = next((b for b in (56, 32, 16, 8) if bands % b == 0), bands)
    spec = lambda n: pl.BlockSpec((n, block, lines), lambda i: (0, i, 0))
    count_spec = pl.BlockSpec((width, 1, lines), lambda i: (0, 0, 0))
    return pl.pallas_call(
        residual_kernel,
        grid=(bands // block,),
        in_specs=[spec(left.shape[0]), spec(width), spec(right.shape[0]), spec(width), count_spec],
        out_specs=[spec(width), spec(width)],
        out_shape=[
            jax.ShapeDtypeStruct((width, bands, lines), jnp.float32),
            jax.ShapeDtypeStruct((width, bands, lines), jnp.bfloat16),
        ],
    )(left, middle, right, planes, count)


def shards(cube):
    lines_dev, pix_dev, bands = cube.shape
    n_track = lax.axis_size("track")
    n_cross = lax.axis_size("cross")
    total_lines = lines_dev * n_track
    total_pix = pix_dev * n_cross
    highest = lax.Precision.HIGHEST
    planes = jnp.transpose(cube, (1, 2, 0))
    sides, tops, bottoms = halos(planes)
    weights = line_weights(lines_dev)
    middle = sum_lines(tops["middle"], planes, bottoms["middle"], weights)
    left = sum_lines(tops["left"], sides["left"], bottoms["left"], weights)
    right = sum_lines(tops["right"], sides["right"], bottoms["right"], weights)
    line_count = window_count(lax.axis_index("track") * lines_dev, lines_dev, total_lines)
    pixel_count = window_count(lax.axis_index("cross") * pix_dev, pix_dev, total_pix)
    count = pixel_count[:, None, None] * line_count[None, None, :]
    residual, residual_bf = residuals(left, middle, right, planes, count)
    partial_cov = jnp.einsum(
        "pjl,pkl->jk", residual_bf, residual_bf, preferred_element_type=jnp.float32
    )
    packed = butterfly_sum(pack_symmetric(partial_cov), "track")
    packed = packed + lax.ppermute(packed, "cross", [(i, i ^ 1) for i in range(n_cross)])
    packed = ring_sum(packed, "cross", 2)
    covariance = unpack_symmetric(packed) / (total_lines * total_pix)
    inverse = spd_inverse(covariance, LOAD)
    solved = jnp.einsum(
        "jb,pbl->pjl", inverse.T, residual, precision=highest, preferred_element_type=jnp.float32
    )
    scores = jnp.sum(residual * solved, axis=1) / bands
    return scores.T


def solution(mesh):
    return jax.shard_map(
        shards,
        mesh=mesh,
        in_specs=(P("track", "cross", None),),
        out_specs=P("track", "cross"),
        check_vma=False,
    )
```

```python
import functools

import jax
import jax.numpy as jnp
from jax import lax
from jax.experimental import pallas as pl
from jax.experimental.layout import Layout, with_layout_constraint
from jax.sharding import PartitionSpec as P

HALF = 15


LOAD = 0.02


def with_halo(block, sides, width):
    for axis, dim in sides:
        count = lax.axis_size(axis)
        forward = [(i, i + 1) for i in range(count - 1)]
        backward = [(target, source) for source, target in forward]
        low = lax.ppermute(
            lax.slice_in_dim(block, block.shape[dim] - width, None, axis=dim), axis, forward
        )
        high = lax.ppermute(lax.slice_in_dim(block, 0, width, axis=dim), axis, backward)
        block = jnp.concatenate([low, block, high], axis=dim)
    return block


def band_matrix(rows_in, rows_out, dtype):
    source = jnp.arange(rows_in)[:, None]
    target = jnp.arange(rows_out)[None, :]
    inside = (source >= target) & (source <= target + 2 * HALF)
    return inside.astype(dtype)


def butterfly_sum(x, axis):
    count = lax.axis_size(axis)
    step = 1
    while step < count:
        pairs = [(i, i ^ step) for i in range(count)]
        x = x + lax.ppermute(x, axis, pairs)
        step *= 2
    return x


def ring_sum(x, axis, stride):
    count = lax.axis_size(axis)
    groups = count // stride
    total = x
    for shift in range(1, groups):
        pairs = [
            (i, (i + shift * stride) % count) for i in range(count)
        ]
        total = total + lax.ppermute(x, axis, pairs)
    return total


def pack_symmetric(c):
    h = c.shape[0] // 2
    row = jnp.arange(h)[:, None]
    col = jnp.arange(h)[None, :]
    c11, c12, c22 = c[:h, :h], c[:h, h:], c[h:, h:]
    mixed = jnp.where(col >= row, c11, c22)
    diagonal = jnp.sum(jnp.where(col == row, c22, 0.0), axis=0, keepdims=True)
    return jnp.concatenate([c12, mixed, diagonal], axis=0)


def unpack_symmetric(p):
    h = p.shape[1]
    row = jnp.arange(h)[:, None]
    col = jnp.arange(h)[None, :]
    c12, mixed, d22 = p[:h], p[h:2 * h], p[2 * h]
    c11 = jnp.where(col >= row, mixed, mixed.T)
    c22 = jnp.where(col < row, mixed, mixed.T)
    c22 = jnp.where(col == row, d22[None, :], c22)
    top = jnp.concatenate([c11, c12], axis=1)
    bottom = jnp.concatenate([c12.T, c22], axis=1)
    return jnp.concatenate([top, bottom], axis=0)


def sweep_kernel(n, load, a_ref, o_ref):
    size = o_ref.shape[0]
    rows = lax.broadcasted_iota(jnp.int32, (size, 1), 0)
    lanes = lax.broadcasted_iota(jnp.int32, (1, size), 1)
    o_ref[...] = jnp.where(rows == lanes, 1.0, 0.0).astype(jnp.float32)
    o_ref[:n, :n] = a_ref[...]
    if load:
        on_diagonal = (rows == lanes) & (rows < n)
        full = o_ref[...]
        trace = jnp.sum(jnp.where(on_diagonal, full, 0.0), axis=(0, 1), keepdims=True)
        o_ref[...] = jnp.where(on_diagonal, full + load * (trace / n), full)
    sub8 = lax.broadcasted_iota(jnp.int32, (8, 1), 0)

    def pick(v, j):
        return jnp.sum(jnp.where(lanes == j, v, 0.0), axis=1, keepdims=True)

    def body(m, carry):
        k = 2 * m
        base = pl.multiple_of((k // 8) * 8, 8)
        slab = o_ref[pl.ds(base, 8), :]
        r0 = jnp.sum(jnp.where(sub8 == k - base, slab, 0.0), axis=0, keepdims=True)
        r1 = jnp.sum(jnp.where(sub8 == k + 1 - base, slab, 0.0), axis=0, keepdims=True)
        a00, a01, a11 = pick(r0, k), pick(r0, k + 1), pick(r1, k + 1)
        det = a00 * a11 - a01 * a01
        p00, p01, p11 = a11 / det, -a01 / det, a00 / det
        a = o_ref[...]
        c0 = jnp.sum(jnp.where(lanes == k, a, 0.0), axis=1, keepdims=True)
        c1 = jnp.sum(jnp.where(lanes == k + 1, a, 0.0), axis=1, keepdims=True)
        u0 = c0 * p00 + c1 * p01
        u1 = c0 * p01 + c1 * p11
        s0 = r0 * p00 + r1 * p01
        s1 = r0 * p01 + r1 * p11
        main = a - u0 * r0 - u1 * r1
        row0, row1 = rows == k, rows == k + 1
        col0, col1 = lanes == k, lanes == k + 1
        in_rows = row0 | row1
        in_cols = col0 | col1
        corner = jnp.where(row0, jnp.where(col0, -p00, -p01), jnp.where(col0, -p01, -p11))
        side_cols = jnp.where(col0, u0, u1)
        side_rows = jnp.where(row0, s0, s1)
        edge = jnp.where(in_rows, jnp.where(in_cols, corner, side_rows), side_cols)
        o_ref[...] = jnp.where(in_rows | in_cols, edge, main)
        return carry

    lax.fori_loop(0, n // 2, body, 0)


def spd_inverse(a, load=0.0):
    n = a.shape[0]
    assert n % 2 == 0
    size = -(-n // 128) * 128
    swept = pl.pallas_call(
        functools.partial(sweep_kernel, n, load),
        out_shape=jax.ShapeDtypeStruct((size, size), jnp.float32),
    )(a)
    return -swept[:n, :n]


def window_count(first, local, total):
    index = first + jnp.arange(local)
    upper = jnp.minimum(index + HALF, total - 1)
    lower = jnp.maximum(index - HALF, 0)
    return (upper - lower + 1).astype(jnp.float32)


def sum_pixels(values, width, dtype):
    weights = band_matrix(width + 2 * HALF, width, dtype)
    return jnp.einsum(
        "lqb,qp->lpb", values, weights, precision=None, preferred_element_type=jnp.float32
    )


def sum_lines(values, height, dtype, precision):
    weights = band_matrix(height + 2 * HALF, height, dtype)
    return jnp.einsum(
        "kpb,kl->lpb", values, weights, precision=precision, preferred_element_type=jnp.float32
    )


def neighbour_pairs(n_track, n_cross, dt, dc):
    pairs = []
    for t in range(n_track):
        for c in range(n_cross):
            if 0 <= t + dt < n_track and 0 <= c + dc < n_cross:
                pairs.append(((t + dt) * n_cross + c + dc, t * n_cross + c))
    return pairs


def halos(planes):
    n_track = lax.axis_size("track")
    n_cross = lax.axis_size("cross")
    both = ("track", "cross")

    def fetch(piece, dt, dc):
        if dt == 0:
            pairs = [(c + dc, c) for c in range(n_cross) if 0 <= c + dc < n_cross]
            return lax.ppermute(piece, "cross", pairs)
        if dc == 0:
            pairs = [(t + dt, t) for t in range(n_track) if 0 <= t + dt < n_track]
            return lax.ppermute(piece, "track", pairs)
        return lax.ppermute(piece, both, neighbour_pairs(n_track, n_cross, dt, dc))

    first, last = slice(0, HALF), slice(-HALF, None)
    to_right, to_left, planes = lax.optimization_barrier((planes[last], planes[first], planes))
    sides = {
        "left": fetch(to_right, 0, -1),
        "right": fetch(to_left, 0, 1),
    }
    top = fetch(planes[:, :, last], -1, 0)
    bottom = fetch(planes[:, :, first], 1, 0)
    tops = {
        "left": fetch(top[last], 0, -1),
        "middle": top,
        "right": fetch(top[first], 0, 1),
    }
    bottoms = {
        "left": fetch(bottom[last], 0, -1),
        "middle": bottom,
        "right": fetch(bottom[first], 0, 1),
    }
    return sides, tops, bottoms


def line_weights(lines):
    target = jnp.arange(lines)[None, :]
    middle = jnp.abs(jnp.arange(lines)[:, None] - target) <= HALF
    side = jnp.arange(HALF)[:, None]
    top = target <= side
    bottom = target >= lines - HALF + side
    return [w.astype(jnp.bfloat16) for w in (top, middle, bottom)]


def sum_lines(top, middle, bottom, weights):
    total = None
    for values, w in zip((top, middle, bottom), weights):
        term = jnp.einsum("qbk,kl->qbl", values, w, preferred_element_type=jnp.float32)
        total = term if total is None else total + term
    return total


def residual_kernel(left_ref, middle_ref, right_ref, x_ref, count_ref, out_ref, out_bf_ref):
    refs = [(left_ref, q) for q in range(left_ref.shape[0])]
    refs += [(middle_ref, q) for q in range(middle_ref.shape[0])]
    refs += [(right_ref, q) for q in range(right_ref.shape[0])]

    def plane(q):
        ref, i = refs[q]
        return ref[i]

    def emit(p, running):
        value = x_ref[p].astype(jnp.float32) - running / count_ref[p]
        out_ref[p] = value
        out_bf_ref[p] = value.astype(jnp.bfloat16)

    span = 2 * HALF + 1
    running = plane(0)
    for q in range(1, span):
        running = running + plane(q)
    emit(0, running)
    for p in range(1, out_ref.shape[0]):
        running = running + plane(p + span - 1) - plane(p - 1)
        emit(p, running)


def residuals(left, middle, right, planes, count):
    width, bands, lines = middle.shape
    block = next((b for b in (56, 32, 16, 8) if bands % b == 0), bands)
    spec = lambda n: pl.BlockSpec((n, block, lines), lambda i: (0, i, 0))
    count_spec = pl.BlockSpec((width, 1, lines), lambda i: (0, 0, 0))
    return pl.pallas_call(
        residual_kernel,
        grid=(bands // block,),
        in_specs=[spec(left.shape[0]), spec(width), spec(right.shape[0]), spec(width), count_spec],
        out_specs=[spec(width), spec(width)],
        out_shape=[
            jax.ShapeDtypeStruct((width, bands, lines), jnp.float32),
            jax.ShapeDtypeStruct((width, bands, lines), jnp.bfloat16),
        ],
    )(left, middle, right, planes, count)


def shards(cube):
    lines_dev, pix_dev, bands = cube.shape
    n_track = lax.axis_size("track")
    n_cross = lax.axis_size("cross")
    total_lines = lines_dev * n_track
    total_pix = pix_dev * n_cross
    highest = lax.Precision.HIGHEST
    planes = jnp.transpose(cube, (1, 2, 0))
    sides, tops, bottoms = halos(planes)
    weights = line_weights(lines_dev)
    middle = sum_lines(tops["middle"], planes, bottoms["middle"], weights)
    left = sum_lines(tops["left"], sides["left"], bottoms["left"], weights)
    right = sum_lines(tops["right"], sides["right"], bottoms["right"], weights)
    line_count = window_count(lax.axis_index("track") * lines_dev, lines_dev, total_lines)
    pixel_count = window_count(lax.axis_index("cross") * pix_dev, pix_dev, total_pix)
    count = pixel_count[:, None, None] * line_count[None, None, :]
    residual, residual_bf = residuals(left, middle, right, planes, count)
    partial_cov = jnp.einsum(
        "pjl,pkl->jk", residual_bf, residual_bf, preferred_element_type=jnp.float32
    )
    packed = pack_symmetric(partial_cov)
    packed = packed + lax.ppermute(packed, "cross", [(i, i ^ 1) for i in range(n_cross)])
    packed = butterfly_sum(ring_sum(packed, "cross", 2), "track")
    covariance = unpack_symmetric(packed) / (total_lines * total_pix)
    inverse = spd_inverse(covariance, LOAD)
    solved = jnp.einsum(
        "jb,pbl->pjl", inverse.T, residual, precision=highest, preferred_element_type=jnp.float32
    )
    scores = jnp.einsum("pjl,pjl->lp", residual, solved, precision=lax.Precision.HIGHEST)
    return scores / bands


def solution(mesh):
    return jax.shard_map(
        shards,
        mesh=mesh,
        in_specs=(P("track", "cross", None),),
        out_specs=P("track", "cross"),
        check_vma=False,
    )
```
